32 devices in a mesh: blk: 8 (over z, core), mesh: 4 (over y, x).
Axes of the slice: x: 2, y: 2, z: 4, core: 2. Of those that a mesh axis runs over, the one named last changes fastest.
Arguments:
- flow_field: float32 [8, 5, 96, 1024], P('blk', None, None, 'mesh'), may hold values from -6 to 6
- lower_row_history: float32 [8, 64, 5, 1024], P('blk', None, None, 'mesh'), may hold values from -6 to 6
- upper_row_history: float32 [8, 64, 5, 1024], P('blk', None, None, 'mesh'), may hold values from -6 to 6
- lower_lag_slot: int32 [8], replicated, may hold values from 0 to 63
- upper_lag_slot: int32 [8], replicated, may hold values from 0 to 63
- axial_jacobian: float32 [5, 5], replicated, may hold values from -2.5 to 2.5
- pitch_jacobian: float32 [5, 5], replicated, may hold values from -2.5 to 2.5
- mode_shape: float32 [4, 96, 1024], P(None, None, 'mesh'), may hold values from -16 to 16
- stiffness: float32 [8, 4], P('blk'), may hold values from 0.5 to 4
- displacement: float32 [8, 4], P('blk'), may hold values from -4 to 4
- velocity: float32 [8, 4], P('blk'), may hold values from -4 to 4
Outputs:
- new_flow: float32 [8, 5, 96, 1024], P('blk', None, None, 'mesh')
- new_displacement: float32 [8, 4], P('blk')
- new_velocity: float32 [8, 4], P('blk')
The draws below stay inside these ranges and needn't reach their ends.
All inputs are finite; a program needn't handle non-finite values.
Results may differ from the reference program's by a relative error of at most 0.0003.
Values sent between devices are 32-bit elements; how exact they have to be, the bound alone decides.
No kernel may reach another device: no remote copies, remote signals or barrier semaphores. Data moves between devices by JAX's collectives and lax.ppermute only.
A program may use at most 64 MiB of HBM per device.

```python
import math
import jax
import jax.numpy as jnp
from jax import lax

CP = 96
HISTORY_SLOTS = 64
STEP_COUNT = 2
MODES = 4
BLADE_PASSAGES = 8
AXIAL_COUNT = 1024


def draw_mode_shape(key, part):
    position = jnp.arange(AXIAL_COUNT, dtype=jnp.float32) / max(AXIAL_COUNT - 1, 1)
    base = jnp.clip(jax.random.normal(key, (MODES, CP, AXIAL_COUNT), jnp.float32), -4.0, 4.0)
    growth = 1.0 + 2.0 * position
    return base * growth[None, None, :]


def place_ends(result, key, least, top_value):
    longest = result.shape.index(max(result.shape))
    spots = []
    for shift in (0, 1):
        where = [jax.random.randint(jax.random.fold_in(key, axis), (), 0, length) for axis, length in enumerate(result.shape)]
        where[longest] = (where[longest] + shift) % result.shape[longest]
        spots.append(tuple(where))
    return result.at[spots[0]].set(least).at[spots[1]].set(top_value)


def level_of(own_key, shape, shards, low, largest):
    def one(dim, shards_of):
        heights = jax.random.uniform(jax.random.fold_in(jax.random.fold_in(own_key, 6), dim), (shards_of,), jnp.float32, low / len(shards), largest / len(shards))
        return jnp.repeat(jnp.exp(heights), shape[dim] // shards_of).reshape((-1,) + (1,) * (len(shape) - dim - 1))

    factor_of = one(*shards[0])
    for cut in shards[1:]:
        factor_of = factor_of * one(*cut)
    return factor_of


def normal_values(key, shape, width, limit, shards=(), kind=jnp.bfloat16):
    values = width * jax.random.normal(key, shape, jnp.float32)
    if shards:
        values = values * level_of(key, shape, shards, -0.22, 0.18)
    return jnp.clip(values, -limit, limit).astype(kind)


def setup_inputs(seed: int = 0) -> dict:
    key_list = jax.random.split(jax.random.key(seed), 12)
    flow_field = normal_values(key_list[0], (BLADE_PASSAGES, 5, CP, AXIAL_COUNT), 1.0, 6.0, ((0, 8), (3, 4)), jnp.float32)
    lower_row_history = normal_values(key_list[1], (BLADE_PASSAGES, HISTORY_SLOTS, 5, AXIAL_COUNT), 1.0, 6.0, ((0, 8), (3, 4)), jnp.float32)
    upper_row_history = normal_values(key_list[2], (BLADE_PASSAGES, HISTORY_SLOTS, 5, AXIAL_COUNT), 1.0, 6.0, ((0, 8), (3, 4)), jnp.float32)
    lower_lag_slot = place_ends(jax.random.randint(key_list[3], (BLADE_PASSAGES,), 0, HISTORY_SLOTS), jax.random.fold_in(key_list[3], 1), 0, HISTORY_SLOTS - 1).astype(jnp.int32)
    upper_lag_slot = place_ends(jax.random.randint(key_list[4], (BLADE_PASSAGES,), 0, HISTORY_SLOTS), jax.random.fold_in(key_list[4], 1), 0, HISTORY_SLOTS - 1).astype(jnp.int32)
    axial_jacobian = normal_values(key_list[5], (5, 5), 5 ** -0.5, 2.5, (), jnp.float32)
    pitch_jacobian = normal_values(key_list[6], (5, 5), 5 ** -0.5, 2.5, (), jnp.float32)
    mode_shape = draw_mode_shape(jax.random.fold_in(key_list[11], 71), 0)
    stiffness = jnp.clip(jnp.exp(math.log(4.0) - 2.0794415 * jax.random.uniform(key_list[8], (BLADE_PASSAGES, MODES), jnp.float32) ** level_of(key_list[8], (BLADE_PASSAGES, MODES), ((0, 8),), -0.2, 0.2)), 0.5, 4.0)
    displacement = normal_values(key_list[9], (BLADE_PASSAGES, MODES), 1.0, 4.0, ((0, 8),), jnp.float32)
    velocity = normal_values(key_list[10], (BLADE_PASSAGES, MODES), 1.0, 4.0, ((0, 8),), jnp.float32)
    return {"flow_field": flow_field, "lower_row_history": lower_row_history, "upper_row_history": upper_row_history, "lower_lag_slot": lower_lag_slot, "upper_lag_slot": upper_lag_slot, "axial_jacobian": axial_jacobian, "pitch_jacobian": pitch_jacobian, "mode_shape": mode_shape, "stiffness": stiffness, "displacement": displacement, "velocity": velocity}


PRECISE = lax.Precision.HIGHEST
TIME_STEP = 0.4
DIFFUSION = 0.1
COUPLING = 0.3
DAMPING = 0.1

def rates_from(flow_state, padded_axial, modal_velocity, lower_ghost, upper_ghost, axial_jacobian, pitch_jacobian, mode_shape):
    padded_pitch = jnp.concatenate([lower_ghost[:, None, :], flow_state, upper_ghost[:, None, :]], axis=1)
    grad_axial = 0.5 * (padded_axial[:, :, 2:] - padded_axial[:, :, :-2])
    grad_pitch = 0.5 * (padded_pitch[:, 2:, :] - padded_pitch[:, :-2, :])
    laplacian = padded_axial[:, :, 2:] + padded_axial[:, :, :-2] + padded_pitch[:, 2:, :] + padded_pitch[:, :-2, :] - 4.0 * flow_state
    flux = jnp.einsum('ij,jpx->ipx', axial_jacobian, grad_axial, precision=PRECISE)
    flux = flux + jnp.einsum('ij,jpx->ipx', pitch_jacobian, grad_pitch, precision=PRECISE)
    push = COUPLING * jnp.einsum('m,mpx->px', modal_velocity, mode_shape, precision=PRECISE)
    rate = DIFFUSION * laplacian - flux
    rate = rate.at[1].add(push)
    partial_value = jnp.einsum('mpx,px->m', mode_shape, flow_state[4], precision=PRECISE)
    return (rate, partial_value)

def reference(flow_field, lower_row_history, upper_row_history, lower_lag_slot, upper_lag_slot, axial_jacobian, pitch_jacobian, mode_shape, stiffness, displacement, velocity):
    force_scale = 1.0 / math.sqrt(AXIAL_COUNT * CP)
    shifted_upper = jnp.roll(upper_row_history, 1, axis=0)
    shifted_lower = jnp.roll(lower_row_history, -1, axis=0)
    passage_blocks = jnp.arange(BLADE_PASSAGES, dtype=jnp.int32)
    lower_rows_gathered = jnp.stack([shifted_upper[passage_blocks, (lower_lag_slot + advance_once) % HISTORY_SLOTS] for advance_once in range(STEP_COUNT)], axis=1)
    upper_rows_gathered = jnp.stack([shifted_lower[passage_blocks, (upper_lag_slot + advance_once) % HISTORY_SLOTS] for advance_once in range(STEP_COUNT)], axis=1)

    def one_passage(inputs):
        flow_state, modal_disp, modal_velocity, blade_stiffness, lower_ghosts, upper_ghosts = inputs
        for advance_once in range(STEP_COUNT):
            lower_ghost = lower_ghosts[advance_once]
            upper_ghost = upper_ghosts[advance_once]

            def evaluate(state_now, disp_now, velocity_now):
                padded_axial = jnp.pad(state_now, ((0, 0), (0, 0), (1, 1)))
                rate, partial_value = rates_from(state_now, padded_axial, velocity_now, lower_ghost, upper_ghost, axial_jacobian, pitch_jacobian, mode_shape)
                accel = partial_value * force_scale - blade_stiffness * disp_now - DAMPING * velocity_now
                return (rate, velocity_now, accel)
            first_rate, first_disp, first_accel = evaluate(flow_state, modal_disp, modal_velocity)
            mid_state = flow_state + TIME_STEP * first_rate
            mid_disp = modal_disp + TIME_STEP * first_disp
            mid_velocity = modal_velocity + TIME_STEP * first_accel
            second_rate, second_disp, second_accel = evaluate(mid_state, mid_disp, mid_velocity)
            flow_state = flow_state + 0.5 * TIME_STEP * (first_rate + second_rate)
            modal_disp = modal_disp + 0.5 * TIME_STEP * (first_disp + second_disp)
            modal_velocity = modal_velocity + 0.5 * TIME_STEP * (first_accel + second_accel)
        return (flow_state, modal_disp, modal_velocity)
    new_flow, new_displacement, new_velocity = lax.map(one_passage, (flow_field, displacement, velocity, stiffness, lower_rows_gathered, upper_rows_gathered))
    return (new_flow, new_displacement, new_velocity)
```

```python
import math

import jax
import jax.numpy as jnp
from jax import lax
from jax.sharding import PartitionSpec as P

STEP_COUNT = 2


PRECISE = lax.Precision.HIGHEST
TIME_STEP = 0.4
DIFFUSION = 0.1
COUPLING = 0.3
DAMPING = 0.1


def shifted(value, axis, by):
    peers = lax.axis_size(axis)
    return lax.ppermute(value, axis, [(i, (i + by) % peers) for i in range(peers)])


def halo(value):
    peers = lax.axis_size("mesh")
    up = [(i, i + 1) for i in range(peers - 1)]
    down = [(i + 1, i) for i in range(peers - 1)]
    before = lax.ppermute(value[..., -1:], "mesh", up)
    after = lax.ppermute(value[..., :1], "mesh", down)
    return before, after


def axial_pad(value, before, after):
    return jnp.concatenate([before, value, after], axis=-1)


def pitch_pad(value, lower, upper):
    return jnp.concatenate([lower[:, None, :], value, upper[:, None, :]], axis=1)


def flow_rate(state, before, after, lower_ghost, upper_ghost, axial_jacobian, pitch_jacobian):
    padded_axial = axial_pad(state, before, after)
    padded_pitch = pitch_pad(state, lower_ghost, upper_ghost)
    grad_axial = 0.5 * (padded_axial[:, :, 2:] - padded_axial[:, :, :-2])
    grad_pitch = 0.5 * (padded_pitch[:, 2:, :] - padded_pitch[:, :-2, :])
    laplacian = (
        padded_axial[:, :, 2:]
        + padded_axial[:, :, :-2]
        + padded_pitch[:, 2:, :]
        + padded_pitch[:, :-2, :]
        - 4.0 * state
    )
    flux = jnp.einsum("ij,jpx->ipx", axial_jacobian, grad_axial, precision=PRECISE)
    flux = flux + jnp.einsum("ij,jpx->ipx", pitch_jacobian, grad_pitch, precision=PRECISE)
    return DIFFUSION * laplacian - flux


def single_field_grads(field, before, after):
    padded_axial = jnp.concatenate([before, field, after], axis=-1)
    zero_row = jnp.zeros_like(field[..., :1, :])
    padded_pitch = jnp.concatenate([zero_row, field, zero_row], axis=-2)
    grad_axial = 0.5 * (padded_axial[..., 2:] - padded_axial[..., :-2])
    grad_pitch = 0.5 * (padded_pitch[..., 2:, :] - padded_pitch[..., :-2, :])
    laplacian = (
        padded_axial[..., 2:]
        + padded_axial[..., :-2]
        + padded_pitch[..., 2:, :]
        + padded_pitch[..., :-2, :]
        - 4.0 * field
    )
    return grad_axial, grad_pitch, laplacian


def modal_field(weights, mode_shape):
    return jnp.einsum("m,mpx->px", weights, mode_shape, precision=PRECISE)


def projection(mode_shape, field):
    return jnp.einsum("mpx,px->m", mode_shape, field, precision=PRECISE)


def add_field_one(rate, extra):
    return rate.at[1].add(extra)


def on_device(
    flow_field,
    lower_row_history,
    upper_row_history,
    lower_lag_slot,
    upper_lag_slot,
    axial_jacobian,
    pitch_jacobian,
    mode_shape,
    stiffness,
    displacement,
    velocity,
):
    h = TIME_STEP
    state0 = flow_field[0]
    fields = state0.shape[0]
    pitch_cells = state0.shape[1]
    axial_cells = state0.shape[2]
    modes = mode_shape.shape[0]
    force_scale = 1.0 / math.sqrt(pitch_cells * axial_cells * lax.axis_size("mesh"))
    passages = lax.axis_size("blk")
    position = lax.axis_index("blk")
    slot_count = lower_row_history.shape[1]
    blade_stiffness = stiffness[0]
    disp0 = displacement[0]
    vel0 = velocity[0]

    after_me = (position + 1) % passages
    before_me = (position + passages - 1) % passages
    slot_next = lax.dynamic_index_in_dim(lower_lag_slot, after_me, 0, keepdims=False)
    slot_prev = lax.dynamic_index_in_dim(upper_lag_slot, before_me, 0, keepdims=False)
    rows_up = jnp.stack(
        [
            lax.dynamic_index_in_dim(
                upper_row_history[0], (slot_next + s) % slot_count, 0, keepdims=False
            )
            for s in range(STEP_COUNT)
        ]
    )
    rows_down = jnp.stack(
        [
            lax.dynamic_index_in_dim(
                lower_row_history[0], (slot_prev + s) % slot_count, 0, keepdims=False
            )
            for s in range(STEP_COUNT)
        ]
    )
    lower_ghosts = shifted(rows_up, "blk", 1)
    upper_ghosts = shifted(rows_down, "blk", -1)

    both_before, both_after = halo(jnp.concatenate([state0, mode_shape], axis=0))
    state0_before, mode_before = both_before[:fields], both_before[fields:]
    state0_after, mode_after = both_after[:fields], both_after[fields:]

    ax_col = axial_jacobian[:, 1]
    pt_col = pitch_jacobian[:, 1]

    def zero_ghost_rate_one(weights):
        field = modal_field(weights, mode_shape)
        f_before = modal_field(weights, mode_before)
        f_after = modal_field(weights, mode_after)
        ga, gp, lap = single_field_grads(field, f_before, f_after)
        rate = -(ax_col[:, None, None] * ga[None] + pt_col[:, None, None] * gp[None])
        return add_field_one(rate, DIFFUSION * lap)

    ms_ga, ms_gp, _ = single_field_grads(mode_shape, mode_before, mode_after)
    grad_a_sum = jnp.einsum("mpx,npx->mn", mode_shape, ms_ga, precision=PRECISE)
    grad_p_sum = jnp.einsum("mpx,npx->mn", mode_shape, ms_gp, precision=PRECISE)
    coupling_sum = -(axial_jacobian[4, 1] * grad_a_sum + pitch_jacobian[4, 1] * grad_p_sum)

    gl1, gu1 = lower_ghosts[0], upper_ghosts[0]
    gl2, gu2 = lower_ghosts[1], upper_ghosts[1]
    push0 = COUPLING * modal_field(vel0, mode_shape)
    rate1 = add_field_one(
        flow_rate(state0, state0_before, state0_after, gl1, gu1, axial_jacobian, pitch_jacobian),
        push0,
    )
    mid1 = state0 + h * rate1
    m_before, m_after = halo(mid1)
    rate1b = add_field_one(
        flow_rate(mid1, m_before, m_after, gl1, gu1, axial_jacobian, pitch_jacobian), push0
    )
    base1 = state0 + 0.5 * h * (rate1 + rate1b)
    b_before, b_after = halo(base1)
    rate2_base = flow_rate(base1, b_before, b_after, gl2, gu2, axial_jacobian, pitch_jacobian)

    partials = jnp.concatenate(
        [
            projection(mode_shape, state0[4]),
            projection(mode_shape, mid1[4]),
            projection(mode_shape, base1[4]),
            projection(mode_shape, rate2_base[4]),
            coupling_sum.reshape(-1),
        ]
    )
    totals = lax.psum(partials, "mesh")
    force0 = force_scale * totals[0:modes]
    force1 = force_scale * totals[modes : 2 * modes]
    force2 = force_scale * totals[2 * modes : 3 * modes]
    force3 = force_scale * totals[3 * modes : 4 * modes]
    couple = force_scale * totals[4 * modes :].reshape(modes, modes)

    acc1 = force0 - blade_stiffness * disp0 - DAMPING * vel0
    disp1m = disp0 + h * vel0
    vel1m = vel0 + h * acc1
    acc1m = force1 - blade_stiffness * disp1m - DAMPING * vel1m
    disp1 = disp0 + 0.5 * h * (vel0 + vel1m)
    vel1 = vel0 + 0.5 * h * (acc1 + acc1m)

    acc2 = force2 - blade_stiffness * disp1 - DAMPING * vel1
    disp2m = disp1 + h * vel1
    vel2m = vel1 + h * acc2
    force2m = force2 + h * force3 + h * (0.5 * h * h * COUPLING) * (couple @ acc1)
    acc2m = force2m - blade_stiffness * disp2m - DAMPING * vel2m
    disp2 = disp1 + 0.5 * h * (vel1 + vel2m)
    vel2 = vel1 + 0.5 * h * (acc2 + acc2m)

    corr = 0.5 * h * h * COUPLING
    state1 = add_field_one(base1, corr * modal_field(acc1, mode_shape))
    rate2 = rate2_base + corr * zero_ghost_rate_one(acc1)
    rate2 = add_field_one(rate2, COUPLING * modal_field(vel1, mode_shape))
    mid2 = state1 + h * rate2
    m2_before, m2_after = halo(mid2)
    rate2b = add_field_one(
        flow_rate(mid2, m2_before, m2_after, gl2, gu2, axial_jacobian, pitch_jacobian),
        COUPLING * modal_field(vel2m, mode_shape),
    )
    state2 = state1 + 0.5 * h * (rate2 + rate2b)
    return (state2[None], disp2[None], vel2[None])


def solution(mesh):
    return jax.shard_map(
        on_device,
        mesh=mesh,
        in_specs=(
            P("blk", None, None, "mesh"),
            P("blk", None, None, "mesh"),
            P("blk", None, None, "mesh"),
            P(),
            P(),
            P(),
            P(),
            P(None, None, "mesh"),
            P("blk", None),
            P("blk", None),
            P("blk", None),
        ),
        out_specs=(P("blk", None, None, "mesh"), P("blk", None), P("blk", None)),
        check_vma=False,
    )
```

```python
import math

import jax
import jax.numpy as jnp
from jax import lax
from jax.sharding import PartitionSpec as P

STEP_COUNT = 2


PRECISE = lax.Precision.HIGHEST
TIME_STEP = 0.4
DIFFUSION = 0.1
COUPLING = 0.3
DAMPING = 0.1


def shifted(value, axis, by):
    peers = lax.axis_size(axis)
    return lax.ppermute(value, axis, [(i, (i + by) % peers) for i in range(peers)])


def halo(value):
    peers = lax.axis_size("mesh")
    me = lax.axis_index("mesh")
    before = shifted(value[..., -1:], "mesh", 1)
    after = shifted(value[..., :1], "mesh", -1)
    before = jnp.where(me > 0, before, jnp.zeros_like(before))
    after = jnp.where(me < peers - 1, after, jnp.zeros_like(after))
    return before, after


def mesh_sum(value):
    peers = lax.axis_size("mesh")
    if peers & (peers - 1):
        return lax.psum(value, "mesh")
    step = 1
    while step < peers:
        value = value + lax.ppermute(value, "mesh", [(i, i ^ step) for i in range(peers)])
        step *= 2
    return value


def pick_rows(table, index, count):
    slots = table.shape[0]
    wanted = (index + jnp.arange(count, dtype=jnp.int32)) % slots
    hit = wanted[:, None] == jnp.arange(slots, dtype=jnp.int32)[None, :]
    hit = hit.reshape(hit.shape + (1,) * (table.ndim - 1))
    return jnp.sum(jnp.where(hit, table[None], jnp.zeros_like(table[None])), axis=1)


def pick_entry(values, index):
    hit = jnp.arange(values.shape[0], dtype=jnp.int32) == index
    return jnp.sum(jnp.where(hit, values, jnp.zeros_like(values)))


def axial_pad(value, before, after):
    return jnp.concatenate([before, value, after], axis=-1)


def pitch_pad(value, lower, upper):
    return jnp.concatenate([lower[:, None, :], value, upper[:, None, :]], axis=1)


def flow_rate(state, before, after, lower_ghost, upper_ghost, axial_jacobian, pitch_jacobian):
    padded_axial = axial_pad(state, before, after)
    padded_pitch = pitch_pad(state, lower_ghost, upper_ghost)
    grad_axial = 0.5 * (padded_axial[:, :, 2:] - padded_axial[:, :, :-2])
    grad_pitch = 0.5 * (padded_pitch[:, 2:, :] - padded_pitch[:, :-2, :])
    laplacian = (
        padded_axial[:, :, 2:]
        + padded_axial[:, :, :-2]
        + padded_pitch[:, 2:, :]
        + padded_pitch[:, :-2, :]
        - 4.0 * state
    )
    flux = jnp.einsum("ij,jpx->ipx", axial_jacobian, grad_axial, precision=PRECISE)
    flux = flux + jnp.einsum("ij,jpx->ipx", pitch_jacobian, grad_pitch, precision=PRECISE)
    return DIFFUSION * laplacian - flux


def single_field_grads(field, before, after):
    padded_axial = jnp.concatenate([before, field, after], axis=-1)
    zero_row = jnp.zeros_like(field[..., :1, :])
    padded_pitch = jnp.concatenate([zero_row, field, zero_row], axis=-2)
    grad_axial = 0.5 * (padded_axial[..., 2:] - padded_axial[..., :-2])
    grad_pitch = 0.5 * (padded_pitch[..., 2:, :] - padded_pitch[..., :-2, :])
    laplacian = (
        padded_axial[..., 2:]
        + padded_axial[..., :-2]
        + padded_pitch[..., 2:, :]
        + padded_pitch[..., :-2, :]
        - 4.0 * field
    )
    return grad_axial, grad_pitch, laplacian


def modal_field(weights, mode_shape):
    return jnp.einsum("m,mpx->px", weights, mode_shape, precision=PRECISE)


def projection(mode_shape, field):
    return jnp.einsum("mpx,px->m", mode_shape, field, precision=PRECISE)


def add_field_one(rate, extra):
    return rate.at[1].add(extra)


def on_device(
    flow_field,
    lower_row_history,
    upper_row_history,
    lower_lag_slot,
    upper_lag_slot,
    axial_jacobian,
    pitch_jacobian,
    mode_shape,
    stiffness,
    displacement,
    velocity,
):
    h = TIME_STEP
    state0 = flow_field[0]
    fields = state0.shape[0]
    pitch_cells = state0.shape[1]
    axial_cells = state0.shape[2]
    modes = mode_shape.shape[0]
    force_scale = 1.0 / math.sqrt(pitch_cells * axial_cells * lax.axis_size("mesh"))
    passages = lax.axis_size("blk")
    position = lax.axis_index("blk")
    blade_stiffness = stiffness[0]
    disp0 = displacement[0]
    vel0 = velocity[0]

    after_me = (position + 1) % passages
    before_me = (position + passages - 1) % passages
    slot_next = pick_entry(lower_lag_slot, after_me)
    slot_prev = pick_entry(upper_lag_slot, before_me)
    rows_up = pick_rows(upper_row_history[0], slot_next, STEP_COUNT)
    rows_down = pick_rows(lower_row_history[0], slot_prev, STEP_COUNT)
    lower_ghosts = shifted(rows_up, "blk", 1)
    upper_ghosts = shifted(rows_down, "blk", -1)

    both_before, both_after = halo(jnp.concatenate([state0, mode_shape], axis=0))
    state0_before, mode_before = both_before[:fields], both_before[fields:]
    state0_after, mode_after = both_after[:fields], both_after[fields:]

    ax_col = axial_jacobian[:, 1]
    pt_col = pitch_jacobian[:, 1]

    def zero_ghost_rate_one(weights):
        field = modal_field(weights, mode_shape)
        f_before = modal_field(weights, mode_before)
        f_after = modal_field(weights, mode_after)
        ga, gp, lap = single_field_grads(field, f_before, f_after)
        rate = -(ax_col[:, None, None] * ga[None] + pt_col[:, None, None] * gp[None])
        return add_field_one(rate, DIFFUSION * lap)

    ms_ga, ms_gp, _ = single_field_grads(mode_shape, mode_before, mode_after)
    ms_rate4 = -(axial_jacobian[4, 1] * ms_ga + pitch_jacobian[4, 1] * ms_gp)
    coupling_sum = jnp.einsum("mpx,npx->mn", mode_shape, ms_rate4, precision=PRECISE)

    gl1, gu1 = lower_ghosts[0], upper_ghosts[0]
    gl2, gu2 = lower_ghosts[1], upper_ghosts[1]
    push0 = COUPLING * modal_field(vel0, mode_shape)
    rate1 = add_field_one(
        flow_rate(state0, state0_before, state0_after, gl1, gu1, axial_jacobian, pitch_jacobian),
        push0,
    )
    mid1 = state0 + h * rate1
    m_before, m_after = halo(mid1)
    rate1b = add_field_one(
        flow_rate(mid1, m_before, m_after, gl1, gu1, axial_jacobian, pitch_jacobian), push0
    )
    base1 = state0 + 0.5 * h * (rate1 + rate1b)
    b_before, b_after = halo(base1)
    rate2_base = flow_rate(base1, b_before, b_after, gl2, gu2, axial_jacobian, pitch_jacobian)

    partials = jnp.concatenate(
        [
            projection(mode_shape, state0[4]),
            projection(mode_shape, mid1[4]),
            projection(mode_shape, base1[4]),
            projection(mode_shape, rate2_base[4]),
            coupling_sum.reshape(-1),
        ]
    )
    totals = mesh_sum(partials)
    force0 = force_scale * totals[0:modes]
    force1 = force_scale * totals[modes : 2 * modes]
    force2 = force_scale * totals[2 * modes : 3 * modes]
    force3 = force_scale * totals[3 * modes : 4 * modes]
    couple = force_scale * totals[4 * modes :].reshape(modes, modes)

    acc1 = force0 - blade_stiffness * disp0 - DAMPING * vel0
    disp1m = disp0 + h * vel0
    vel1m = vel0 + h * acc1
    acc1m = force1 - blade_stiffness * disp1m - DAMPING * vel1m
    disp1 = disp0 + 0.5 * h * (vel0 + vel1m)
    vel1 = vel0 + 0.5 * h * (acc1 + acc1m)

    acc2 = force2 - blade_stiffness * disp1 - DAMPING * vel1
    disp2m = disp1 + h * vel1
    vel2m = vel1 + h * acc2
    force2m = force2 + h * force3 + h * (0.5 * h * h * COUPLING) * jnp.dot(couple, acc1, precision=PRECISE)
    acc2m = force2m - blade_stiffness * disp2m - DAMPING * vel2m
    disp2 = disp1 + 0.5 * h * (vel1 + vel2m)
    vel2 = vel1 + 0.5 * h * (acc2 + acc2m)

    corr = 0.5 * h * h * COUPLING
    state1 = add_field_one(base1, corr * modal_field(acc1, mode_shape))
    rate2 = rate2_base + corr * zero_ghost_rate_one(acc1)
    rate2 = add_field_one(rate2, COUPLING * modal_field(vel1, mode_shape))
    mid2 = state1 + h * rate2
    m2_before, m2_after = halo(mid2)
    rate2b = add_field_one(
        flow_rate(mid2, m2_before, m2_after, gl2, gu2, axial_jacobian, pitch_jacobian),
        COUPLING * modal_field(vel2m, mode_shape),
    )
    state2 = state1 + 0.5 * h * (rate2 + rate2b)
    return (state2[None], disp2[None], vel2[None])


def solution(mesh):
    return jax.shard_map(
        on_device,
        mesh=mesh,
        in_specs=(
            P("blk", None, None, "mesh"),
            P("blk", None, None, "mesh"),
            P("blk", None, None, "mesh"),
            P(),
            P(),
            P(),
            P(),
            P(None, None, "mesh"),
            P("blk", None),
            P("blk", None),
            P("blk", None),
        ),
        out_specs=(P("blk", None, None, "mesh"), P("blk", None), P("blk", None)),
        check_vma=False,
    )
```

```python
import math

import jax
import jax.numpy as jnp
from jax import lax
from jax.sharding import PartitionSpec as P

STEP_COUNT = 2


PRECISE = lax.Precision.HIGHEST
TIME_STEP = 0.4
DIFFUSION = 0.1
COUPLING = 0.3
DAMPING = 0.1


def shifted(value, axis, by):
    peers = lax.axis_size(axis)
    return lax.ppermute(value, axis, [(i, (i + by) % peers) for i in range(peers)])


def halo(value):
    peers = lax.axis_size("mesh")
    me = lax.axis_index("mesh")
    before = shifted(value[..., -1:], "mesh", 1)
    after = shifted(value[..., :1], "mesh", -1)
    before = jnp.where(me > 0, before, jnp.zeros_like(before))
    after = jnp.where(me < peers - 1, after, jnp.zeros_like(after))
    return before, after


def mesh_sum(value):
    peers = lax.axis_size("mesh")
    if peers & (peers - 1):
        return lax.psum(value, "mesh")
    step = 1
    while step < peers:
        value = value + lax.ppermute(value, "mesh", [(i, i ^ step) for i in range(peers)])
        step *= 2
    return value


def pick_rows(table, index, count):
    slots = table.shape[0]
    slot = jnp.arange(slots, dtype=jnp.int32).reshape((slots,) + (1,) * (table.ndim - 1))
    rows = []
    for s in range(count):
        hit = slot == (index + s) % slots
        rows.append(jnp.sum(jnp.where(hit, table, jnp.zeros_like(table)), axis=0))
    return jnp.stack(rows)


def pick_entry(values, index):
    hit = jnp.arange(values.shape[0], dtype=jnp.int32) == index
    return jnp.sum(jnp.where(hit, values, jnp.zeros_like(values)))


def axial_pad(value, before, after):
    return jnp.concatenate([before, value, after], axis=-1)


def pitch_pad(value, lower, upper):
    return jnp.concatenate([lower[:, None, :], value, upper[:, None, :]], axis=1)


def flow_rate(state, before, after, lower_ghost, upper_ghost, axial_jacobian, pitch_jacobian):
    padded_axial = axial_pad(state, before, after)
    padded_pitch = pitch_pad(state, lower_ghost, upper_ghost)
    grad_axial = 0.5 * (padded_axial[:, :, 2:] - padded_axial[:, :, :-2])
    grad_pitch = 0.5 * (padded_pitch[:, 2:, :] - padded_pitch[:, :-2, :])
    laplacian = (
        padded_axial[:, :, 2:]
        + padded_axial[:, :, :-2]
        + padded_pitch[:, 2:, :]
        + padded_pitch[:, :-2, :]
        - 4.0 * state
    )
    flux = jnp.einsum("ij,jpx->ipx", axial_jacobian, grad_axial, precision=PRECISE)
    flux = flux + jnp.einsum("ij,jpx->ipx", pitch_jacobian, grad_pitch, precision=PRECISE)
    return DIFFUSION * laplacian - flux


def single_field_grads(field, before, after):
    padded_axial = jnp.concatenate([before, field, after], axis=-1)
    zero_row = jnp.zeros_like(field[..., :1, :])
    padded_pitch = jnp.concatenate([zero_row, field, zero_row], axis=-2)
    grad_axial = 0.5 * (padded_axial[..., 2:] - padded_axial[..., :-2])
    grad_pitch = 0.5 * (padded_pitch[..., 2:, :] - padded_pitch[..., :-2, :])
    laplacian = (
        padded_axial[..., 2:]
        + padded_axial[..., :-2]
        + padded_pitch[..., 2:, :]
        + padded_pitch[..., :-2, :]
        - 4.0 * field
    )
    return grad_axial, grad_pitch, laplacian


def modal_field(weights, mode_shape):
    return jnp.einsum("m,mpx->px", weights, mode_shape, precision=PRECISE)


def projection(mode_shape, field):
    return jnp.einsum("mpx,px->m", mode_shape, field, precision=PRECISE)


def add_field_one(rate, extra):
    return rate.at[1].add(extra)


def rate_field4(state, lower_ghost, upper_ghost, axial_jacobian, pitch_jacobian):
    zero_col = jnp.zeros_like(state[..., :1])
    padded_axial = jnp.concatenate([zero_col, state, zero_col], axis=-1)
    padded_pitch = pitch_pad(state, lower_ghost, upper_ghost)
    grad_axial = 0.5 * (padded_axial[:, :, 2:] - padded_axial[:, :, :-2])
    grad_pitch = 0.5 * (padded_pitch[:, 2:, :] - padded_pitch[:, :-2, :])
    laplacian = (
        padded_axial[4, :, 2:]
        + padded_axial[4, :, :-2]
        + padded_pitch[4, 2:, :]
        + padded_pitch[4, :-2, :]
        - 4.0 * state[4]
    )
    flux = jnp.einsum("j,jpx->px", axial_jacobian[4], grad_axial, precision=PRECISE)
    flux = flux + jnp.einsum("j,jpx->px", pitch_jacobian[4], grad_pitch, precision=PRECISE)
    return DIFFUSION * laplacian - flux


def pack(parts, width):
    flat = [part.reshape(-1, width) for part in parts]
    return jnp.concatenate(flat, axis=0)


def unpack(buffer, shapes):
    out, offset = [], 0
    for shape in shapes:
        count = math.prod(shape[:-1])
        out.append(buffer[offset : offset + count].reshape(shape))
        offset += count
    return out


def on_device(
    flow_field,
    lower_row_history,
    upper_row_history,
    lower_lag_slot,
    upper_lag_slot,
    axial_jacobian,
    pitch_jacobian,
    mode_shape,
    stiffness,
    displacement,
    velocity,
):
    h = TIME_STEP
    state0 = flow_field[0]
    fields, pitch_cells, axial_cells = state0.shape
    modes = mode_shape.shape[0]
    mesh_peers = lax.axis_size("mesh")
    me = lax.axis_index("mesh")
    force_scale = 1.0 / math.sqrt(pitch_cells * axial_cells * mesh_peers)
    passages = lax.axis_size("blk")
    position = lax.axis_index("blk")
    blade_stiffness = stiffness[0]
    disp0 = displacement[0]
    vel0 = velocity[0]

    after_me = (position + 1) % passages
    before_me = (position + passages - 1) % passages
    slot_next = pick_entry(lower_lag_slot, after_me)
    slot_prev = pick_entry(upper_lag_slot, before_me)
    rows_up = pick_rows(upper_row_history[0], slot_next, STEP_COUNT)
    rows_down = pick_rows(lower_row_history[0], slot_prev, STEP_COUNT)
    lower_ghosts = shifted(rows_up, "blk", 1)
    upper_ghosts = shifted(rows_down, "blk", -1)

    reach = 2 * STEP_COUNT
    own = [state0, mode_shape, lower_ghosts, upper_ghosts]
    shapes = [part.shape[:-1] + (reach,) for part in own]
    from_left = shifted(pack([part[..., -reach:] for part in own], reach), "mesh", 1)
    from_right = shifted(pack([part[..., :reach] for part in own], reach), "mesh", -1)
    from_left = jnp.where(me > 0, from_left, jnp.zeros_like(from_left))
    from_right = jnp.where(me < mesh_peers - 1, from_right, jnp.zeros_like(from_right))
    wide = [
        jnp.concatenate([left, part, right], axis=-1)
        for left, part, right in zip(unpack(from_left, shapes), own, unpack(from_right, shapes))
    ]
    state0_w, mode_w, lower_w, upper_w = wide
    width = axial_cells + 2 * reach
    column = jnp.arange(width, dtype=jnp.int32)
    inside = ((column >= reach) | (me > 0)) & ((column < axial_cells + reach) | (me < mesh_peers - 1))
    inside = inside.astype(state0.dtype)
    owned = ((column >= reach) & (column < axial_cells + reach)).astype(state0.dtype)
    mode_owned = mode_w * owned

    def rate(state, lower_ghost, upper_ghost, weights):
        no_col = jnp.zeros_like(state[..., :1])
        flow = flow_rate(
            state, no_col, no_col, lower_ghost, upper_ghost, axial_jacobian, pitch_jacobian
        )
        return add_field_one(flow, COUPLING * modal_field(weights, mode_w)) * inside

    no_mode_col = jnp.zeros_like(mode_w[..., :1])
    ms_ga, ms_gp, _ = single_field_grads(mode_w, no_mode_col, no_mode_col)
    ms_rate4 = -(axial_jacobian[4, 1] * ms_ga + pitch_jacobian[4, 1] * ms_gp)
    coupling_sum = jnp.einsum("mpx,npx->mn", mode_owned, ms_rate4, precision=PRECISE)

    gl1, gu1 = lower_w[0], upper_w[0]
    gl2, gu2 = lower_w[1], upper_w[1]
    rate1 = rate(state0_w, gl1, gu1, vel0)
    mid1 = state0_w + h * rate1
    rate1b = rate(mid1, gl1, gu1, vel0)
    base1 = state0_w + 0.5 * h * (rate1 + rate1b)
    rate2_base4 = rate_field4(base1, gl2, gu2, axial_jacobian, pitch_jacobian)

    partials = jnp.concatenate(
        [
            projection(mode_owned, state0_w[4]),
            projection(mode_owned, mid1[4]),
            projection(mode_owned, base1[4]),
            projection(mode_owned, rate2_base4),
            coupling_sum.reshape(-1),
        ]
    )
    totals = mesh_sum(partials)
    force0 = force_scale * totals[0:modes]
    force1 = force_scale * totals[modes : 2 * modes]
    force2 = force_scale * totals[2 * modes : 3 * modes]
    force3 = force_scale * totals[3 * modes : 4 * modes]
    couple = force_scale * totals[4 * modes :].reshape(modes, modes)

    acc1 = force0 - blade_stiffness * disp0 - DAMPING * vel0
    disp1m = disp0 + h * vel0
    vel1m = vel0 + h * acc1
    acc1m = force1 - blade_stiffness * disp1m - DAMPING * vel1m
    disp1 = disp0 + 0.5 * h * (vel0 + vel1m)
    vel1 = vel0 + 0.5 * h * (acc1 + acc1m)

    acc2 = force2 - blade_stiffness * disp1 - DAMPING * vel1
    disp2m = disp1 + h * vel1
    vel2m = vel1 + h * acc2
    corr = 0.5 * h * h * COUPLING
    force2m = force2 + h * force3 + h * corr * jnp.dot(couple, acc1, precision=PRECISE)
    acc2m = force2m - blade_stiffness * disp2m - DAMPING * vel2m
    disp2 = disp1 + 0.5 * h * (vel1 + vel2m)
    vel2 = vel1 + 0.5 * h * (acc2 + acc2m)

    state1 = add_field_one(base1, corr * modal_field(acc1, mode_w))
    rate2 = rate(state1, gl2, gu2, vel1)
    mid2 = state1 + h * rate2
    rate2b = rate(mid2, gl2, gu2, vel2m)
    state2 = state1 + 0.5 * h * (rate2 + rate2b)
    state2 = state2[..., reach : reach + axial_cells]
    return (state2[None], disp2[None], vel2[None])


def solution(mesh):
    return jax.shard_map(
        on_device,
        mesh=mesh,
        in_specs=(
            P("blk", None, None, "mesh"),
            P("blk", None, None, "mesh"),
            P("blk", None, None, "mesh"),
            P(),
            P(),
            P(),
            P(),
            P(None, None, "mesh"),
            P("blk", None),
            P("blk", None),
            P("blk", None),
        ),
        out_specs=(P("blk", None, None, "mesh"), P("blk", None), P("blk", None)),
        check_vma=False,
    )
```

```python
import math

import jax
import jax.numpy as jnp
from jax import lax
from jax.experimental import pallas as pl
from jax.experimental.pallas import tpu as pltpu
from jax.sharding import PartitionSpec as P

STEP_COUNT = 2


PRECISE = lax.Precision.HIGHEST
TIME_STEP = 0.4
DIFFUSION = 0.1
COUPLING = 0.3
DAMPING = 0.1


def shifted(value, axis, by):
    peers = lax.axis_size(axis)
    return lax.ppermute(value, axis, [(i, (i + by) % peers) for i in range(peers)])


def halo(value):
    peers = lax.axis_size("mesh")
    me = lax.axis_index("mesh")
    before = shifted(value[..., -1:], "mesh", 1)
    after = shifted(value[..., :1], "mesh", -1)
    before = jnp.where(me > 0, before, jnp.zeros_like(before))
    after = jnp.where(me < peers - 1, after, jnp.zeros_like(after))
    return before, after


def mesh_sum(value):
    peers = lax.axis_size("mesh")
    if peers & (peers - 1):
        return lax.psum(value, "mesh")
    step = 1
    while step < peers:
        value = value + lax.ppermute(value, "mesh", [(i, i ^ step) for i in range(peers)])
        step *= 2
    return value


def pick_rows(table, index, count):
    slots = table.shape[0]
    slot = jnp.arange(slots, dtype=jnp.int32).reshape((slots,) + (1,) * (table.ndim - 1))
    rows = []
    for s in range(count):
        hit = slot == (index + s) % slots
        rows.append(jnp.sum(jnp.where(hit, table, jnp.zeros_like(table)), axis=0))
    return jnp.stack(rows)


def pick_entry(values, index):
    hit = jnp.arange(values.shape[0], dtype=jnp.int32) == index
    return jnp.sum(jnp.where(hit, values, jnp.zeros_like(values)))


def axial_pad(value, before, after):
    return jnp.concatenate([before, value, after], axis=-1)


def pitch_pad(value, lower, upper):
    return jnp.concatenate([lower[:, None, :], value, upper[:, None, :]], axis=1)


def flow_rate(state, before, after, lower_ghost, upper_ghost, axial_jacobian, pitch_jacobian):
    padded_axial = axial_pad(state, before, after)
    padded_pitch = pitch_pad(state, lower_ghost, upper_ghost)
    grad_axial = 0.5 * (padded_axial[:, :, 2:] - padded_axial[:, :, :-2])
    grad_pitch = 0.5 * (padded_pitch[:, 2:, :] - padded_pitch[:, :-2, :])
    laplacian = (
        padded_axial[:, :, 2:]
        + padded_axial[:, :, :-2]
        + padded_pitch[:, 2:, :]
        + padded_pitch[:, :-2, :]
        - 4.0 * state
    )
    flux = jnp.einsum("ij,jpx->ipx", axial_jacobian, grad_axial, precision=PRECISE)
    flux = flux + jnp.einsum("ij,jpx->ipx", pitch_jacobian, grad_pitch, precision=PRECISE)
    return DIFFUSION * laplacian - flux


def single_field_grads(field, before, after):
    padded_axial = jnp.concatenate([before, field, after], axis=-1)
    zero_row = jnp.zeros_like(field[..., :1, :])
    padded_pitch = jnp.concatenate([zero_row, field, zero_row], axis=-2)
    grad_axial = 0.5 * (padded_axial[..., 2:] - padded_axial[..., :-2])
    grad_pitch = 0.5 * (padded_pitch[..., 2:, :] - padded_pitch[..., :-2, :])
    laplacian = (
        padded_axial[..., 2:]
        + padded_axial[..., :-2]
        + padded_pitch[..., 2:, :]
        + padded_pitch[..., :-2, :]
        - 4.0 * field
    )
    return grad_axial, grad_pitch, laplacian


def modal_field(weights, mode_shape):
    return jnp.einsum("m,mpx->px", weights, mode_shape, precision=PRECISE)


def projection(mode_shape, field):
    return jnp.einsum("mpx,px->m", mode_shape, field, precision=PRECISE)


def add_field_one(rate, extra):
    return rate.at[1].add(extra)


def rate_field4(state, lower_ghost, upper_ghost, axial_jacobian, pitch_jacobian):
    zero_col = jnp.zeros_like(state[..., :1])
    padded_axial = jnp.concatenate([zero_col, state, zero_col], axis=-1)
    padded_pitch = pitch_pad(state, lower_ghost, upper_ghost)
    grad_axial = 0.5 * (padded_axial[:, :, 2:] - padded_axial[:, :, :-2])
    grad_pitch = 0.5 * (padded_pitch[:, 2:, :] - padded_pitch[:, :-2, :])
    laplacian = (
        padded_axial[4, :, 2:]
        + padded_axial[4, :, :-2]
        + padded_pitch[4, 2:, :]
        + padded_pitch[4, :-2, :]
        - 4.0 * state[4]
    )
    flux = jnp.einsum("j,jpx->px", axial_jacobian[4], grad_axial, precision=PRECISE)
    flux = flux + jnp.einsum("j,jpx->px", pitch_jacobian[4], grad_pitch, precision=PRECISE)
    return DIFFUSION * laplacian - flux


def pack(parts, width):
    flat = [part.reshape(-1, width) for part in parts]
    return jnp.concatenate(flat, axis=0)


def unpack(buffer, shapes):
    out, offset = [], 0
    for shape in shapes:
        count = math.prod(shape[:-1])
        out.append(buffer[offset : offset + count].reshape(shape))
        offset += count
    return out


LANES = 128


def lane_roll(x, shift):
    return pltpu.roll(x, shift % x.shape[-1], x.ndim - 1)


def row_roll(x, shift):
    return pltpu.roll(x, shift % x.shape[0], 0)


def kernel_rate(state, lower, upper, jac, push, inside, fields_out):
    ax, pt = jac
    rows = state[0].shape[0]
    row = lax.broadcasted_iota(jnp.int32, state[0].shape, 0)
    grads_a, grads_p, laps = [], [], []
    for j, s in enumerate(state):
        east = lane_roll(s, -1)
        west = lane_roll(s, 1)
        north = jnp.where(row == rows - 1, upper[j], row_roll(s, -1))
        south = jnp.where(row == 0, lower[j], row_roll(s, 1))
        grads_a.append(0.5 * (east - west))
        grads_p.append(0.5 * (north - south))
        laps.append(east + west + north + south - 4.0 * s)
    out = []
    for i in fields_out:
        r = DIFFUSION * laps[i]
        for j in range(len(state)):
            r = r - ax[i][j] * grads_a[j] - pt[i][j] * grads_p[j]
        if i == 1 and push is not None:
            r = r + push
        out.append(r * inside)
    return out


def read_jacobians(sc_ref, fields):
    ax = [[sc_ref[i * fields + j] for j in range(fields)] for i in range(fields)]
    pt = [[sc_ref[fields * fields + i * fields + j] for j in range(fields)] for i in range(fields)]
    return ax, pt


def lane_fold(x):
    x = jnp.sum(x, axis=0, keepdims=True)
    total = x[:, :LANES]
    for t in range(1, x.shape[1] // LANES):
        total = total + x[:, t * LANES : (t + 1) * LANES]
    return total


def first_kernel(sc_ref, u_ref, ms_ref, gl_ref, gu_ref, inside_ref, owned_ref, a_ref, part_ref):
    h = TIME_STEP
    fields = u_ref.shape[0]
    modes = ms_ref.shape[0]
    jac = read_jacobians(sc_ref, fields)
    base = 2 * fields * fields
    vel = [sc_ref[base + m] for m in range(modes)]
    inside = inside_ref[...]
    owned = owned_ref[...]
    ms = [ms_ref[m] for m in range(modes)]
    push = vel[0] * ms[0]
    for m in range(1, modes):
        push = push + vel[m] * ms[m]
    push = COUPLING * push
    gl1 = [gl_ref[0, j : j + 1, :] for j in range(fields)]
    gu1 = [gu_ref[0, j : j + 1, :] for j in range(fields)]
    gl2 = [gl_ref[1, j : j + 1, :] for j in range(fields)]
    gu2 = [gu_ref[1, j : j + 1, :] for j in range(fields)]
    every = list(range(fields))
    u0 = [u_ref[j] for j in range(fields)]
    k1 = kernel_rate(u0, gl1, gu1, jac, push, inside, every)
    mid = [u0[j] + h * k1[j] for j in every]
    k2 = kernel_rate(mid, gl1, gu1, jac, push, inside, every)
    a = [u0[j] + 0.5 * h * (k1[j] + k2[j]) for j in every]
    for j in every:
        a_ref[j] = a[j]
    (ra4,) = kernel_rate(a, gl2, gu2, jac, None, inside, [4])
    weighted = [ms[m] * owned for m in range(modes)]
    k = 0
    for field in (u0[4], mid[4], a[4], ra4):
        for m in range(modes):
            part_ref[k : k + 1, :] = lane_fold(weighted[m] * field)
            k += 1
    ax41, pt41 = jac[0][4][1], jac[1][4][1]
    rows = ms[0].shape[0]
    row = lax.broadcasted_iota(jnp.int32, ms[0].shape, 0)
    for n in range(modes):
        s = ms[n]
        ga = 0.5 * (lane_roll(s, -1) - lane_roll(s, 1))
        north = jnp.where(row == rows - 1, 0.0, row_roll(s, -1))
        south = jnp.where(row == 0, 0.0, row_roll(s, 1))
        gp = 0.5 * (north - south)
        t = -(ax41 * ga + pt41 * gp)
        for m in range(modes):
            part_ref[k + m * modes + n : k + m * modes + n + 1, :] = lane_fold(weighted[m] * t)


def second_kernel(sc_ref, a_ref, ms_ref, gl_ref, gu_ref, inside_ref, out_ref):
    h = TIME_STEP
    fields = a_ref.shape[0]
    modes = ms_ref.shape[0]
    reach = 2 * STEP_COUNT
    jac = read_jacobians(sc_ref, fields)
    base = 2 * fields * fields
    coef = [[sc_ref[base + w * modes + m] for m in range(modes)] for w in range(3)]
    inside = inside_ref[...]
    ms = [ms_ref[m] for m in range(modes)]

    def combine(weights):
        total = weights[0] * ms[0]
        for m in range(1, modes):
            total = total + weights[m] * ms[m]
        return total

    gl2 = [gl_ref[1, j : j + 1, :] for j in range(fields)]
    gu2 = [gu_ref[1, j : j + 1, :] for j in range(fields)]
    every = list(range(fields))
    s1 = [a_ref[j] for j in every]
    s1[1] = s1[1] + combine(coef[0])
    k1 = kernel_rate(s1, gl2, gu2, jac, COUPLING * combine(coef[1]), inside, every)
    mid = [s1[j] + h * k1[j] for j in every]
    k2 = kernel_rate(mid, gl2, gu2, jac, COUPLING * combine(coef[2]), inside, every)
    width = out_ref.shape[-1]
    for j in every:
        s2 = s1[j] + 0.5 * h * (k1[j] + k2[j])
        out_ref[j] = lane_roll(s2, -reach)[:, :width]


def vmem_spec():
    return pl.BlockSpec(memory_space=pltpu.VMEM)


def smem_spec():
    return pl.BlockSpec(memory_space=pltpu.SMEM)


def on_device(
    flow_field,
    lower_row_history,
    upper_row_history,
    lower_lag_slot,
    upper_lag_slot,
    axial_jacobian,
    pitch_jacobian,
    mode_shape,
    stiffness,
    displacement,
    velocity,
):
    h = TIME_STEP
    state0 = flow_field[0]
    fields, pitch_cells, axial_cells = state0.shape
    modes = mode_shape.shape[0]
    mesh_peers = lax.axis_size("mesh")
    me = lax.axis_index("mesh")
    force_scale = 1.0 / math.sqrt(pitch_cells * axial_cells * mesh_peers)
    passages = lax.axis_size("blk")
    position = lax.axis_index("blk")
    blade_stiffness = stiffness[0]
    disp0 = displacement[0]
    vel0 = velocity[0]

    after_me = (position + 1) % passages
    before_me = (position + passages - 1) % passages
    slot_next = pick_entry(lower_lag_slot, after_me)
    slot_prev = pick_entry(upper_lag_slot, before_me)
    rows_up = pick_rows(upper_row_history[0], slot_next, STEP_COUNT)
    rows_down = pick_rows(lower_row_history[0], slot_prev, STEP_COUNT)
    lower_ghosts = shifted(rows_up, "blk", 1)
    upper_ghosts = shifted(rows_down, "blk", -1)

    reach = 2 * STEP_COUNT
    own = [state0, mode_shape, lower_ghosts, upper_ghosts]
    shapes = [part.shape[:-1] + (reach,) for part in own]
    from_left = shifted(pack([part[..., -reach:] for part in own], reach), "mesh", 1)
    from_right = shifted(pack([part[..., :reach] for part in own], reach), "mesh", -1)
    from_left = jnp.where(me > 0, from_left, jnp.zeros_like(from_left))
    from_right = jnp.where(me < mesh_peers - 1, from_right, jnp.zeros_like(from_right))
    def widen(left, part, right):
        spare = lanes_wide - axial_cells - 2 * reach
        tail = jnp.zeros(part.shape[:-1] + (spare,), part.dtype)
        return jnp.concatenate([left, part, right, tail], axis=-1)

    lanes_wide = -(-(axial_cells + 2 * reach) // LANES) * LANES
    wide = [
        widen(left, part, right)
        for left, part, right in zip(unpack(from_left, shapes), own, unpack(from_right, shapes))
    ]
    state0_w, mode_w, lower_w, upper_w = wide
    column = jnp.arange(lanes_wide, dtype=jnp.int32)[None, :]
    inside = (
        ((column >= reach) | (me > 0))
        & ((column < axial_cells + reach) | (me < mesh_peers - 1))
        & (column < axial_cells + 2 * reach)
    ).astype(state0.dtype)
    owned = ((column >= reach) & (column < axial_cells + reach)).astype(state0.dtype)

    jac_flat = jnp.concatenate([axial_jacobian.reshape(-1), pitch_jacobian.reshape(-1)])
    base1, part_lanes = pl.pallas_call(
        first_kernel,
        out_shape=(
            jax.ShapeDtypeStruct(state0_w.shape, state0.dtype),
            jax.ShapeDtypeStruct((4 * modes + modes * modes, LANES), state0.dtype),
        ),
        in_specs=[smem_spec()] + [vmem_spec()] * 6,
        out_specs=(vmem_spec(), vmem_spec()),
    )(jnp.concatenate([jac_flat, vel0]), state0_w, mode_w, lower_w, upper_w, inside, owned)

    totals = mesh_sum(jnp.sum(part_lanes, axis=1))
    force0 = force_scale * totals[0:modes]
    force1 = force_scale * totals[modes : 2 * modes]
    force2 = force_scale * totals[2 * modes : 3 * modes]
    force3 = force_scale * totals[3 * modes : 4 * modes]
    couple = force_scale * totals[4 * modes :].reshape(modes, modes)

    acc1 = force0 - blade_stiffness * disp0 - DAMPING * vel0
    disp1m = disp0 + h * vel0
    vel1m = vel0 + h * acc1
    acc1m = force1 - blade_stiffness * disp1m - DAMPING * vel1m
    disp1 = disp0 + 0.5 * h * (vel0 + vel1m)
    vel1 = vel0 + 0.5 * h * (acc1 + acc1m)

    acc2 = force2 - blade_stiffness * disp1 - DAMPING * vel1
    disp2m = disp1 + h * vel1
    vel2m = vel1 + h * acc2
    corr = 0.5 * h * h * COUPLING
    force2m = force2 + h * force3 + h * corr * jnp.dot(couple, acc1, precision=PRECISE)
    acc2m = force2m - blade_stiffness * disp2m - DAMPING * vel2m
    disp2 = disp1 + 0.5 * h * (vel1 + vel2m)
    vel2 = vel1 + 0.5 * h * (acc2 + acc2m)

    state2 = pl.pallas_call(
        second_kernel,
        out_shape=jax.ShapeDtypeStruct(state0.shape, state0.dtype),
        in_specs=[smem_spec()] + [vmem_spec()] * 5,
        out_specs=vmem_spec(),
    )(jnp.concatenate([jac_flat, corr * acc1, vel1, vel2m]), base1, mode_w, lower_w, upper_w, inside)
    return (state2[None], disp2[None], vel2[None])


def solution(mesh):
    return jax.shard_map(
        on_device,
        mesh=mesh,
        in_specs=(
            P("blk", None, None, "mesh"),
            P("blk", None, None, "mesh"),
            P("blk", None, None, "mesh"),
            P(),
            P(),
            P(),
            P(),
            P(None, None, "mesh"),
            P("blk", None),
            P("blk", None),
            P("blk", None),
        ),
        out_specs=(P("blk", None, None, "mesh"), P("blk", None), P("blk", None)),
        check_vma=False,
    )
```

```python
import functools
import math

import jax
import jax.numpy as jnp
from jax import lax
from jax.experimental import pallas as pl
from jax.experimental.pallas import tpu as pltpu
from jax.sharding import PartitionSpec as P

STEP_COUNT = 2


PRECISE = lax.Precision.HIGHEST
TIME_STEP = 0.4
DIFFUSION = 0.1
COUPLING = 0.3
DAMPING = 0.1


def shifted(value, axis, by):
    peers = lax.axis_size(axis)
    return lax.ppermute(value, axis, [(i, (i + by) % peers) for i in range(peers)])


def halo(value):
    peers = lax.axis_size("mesh")
    me = lax.axis_index("mesh")
    before = shifted(value[..., -1:], "mesh", 1)
    after = shifted(value[..., :1], "mesh", -1)
    before = jnp.where(me > 0, before, jnp.zeros_like(before))
    after = jnp.where(me < peers - 1, after, jnp.zeros_like(after))
    return before, after


def mesh_sum(value):
    peers = lax.axis_size("mesh")
    if peers & (peers - 1):
        return lax.psum(value, "mesh")
    step = 1
    while step < peers:
        value = value + lax.ppermute(value, "mesh", [(i, i ^ step) for i in range(peers)])
        step *= 2
    return value


def pick_rows(table, index, count):
    slots = table.shape[0]
    slot = jnp.arange(slots, dtype=jnp.int32).reshape((slots,) + (1,) * (table.ndim - 1))
    rows = []
    for s in range(count):
        hit = slot == (index + s) % slots
        rows.append(jnp.sum(jnp.where(hit, table, jnp.zeros_like(table)), axis=0))
    return jnp.stack(rows)


def pick_entry(values, index):
    hit = jnp.arange(values.shape[0], dtype=jnp.int32) == index
    return jnp.sum(jnp.where(hit, values, jnp.zeros_like(values)))


def axial_pad(value, before, after):
    return jnp.concatenate([before, value, after], axis=-1)


def pitch_pad(value, lower, upper):
    return jnp.concatenate([lower[:, None, :], value, upper[:, None, :]], axis=1)


def flow_rate(state, before, after, lower_ghost, upper_ghost, axial_jacobian, pitch_jacobian):
    padded_axial = axial_pad(state, before, after)
    padded_pitch = pitch_pad(state, lower_ghost, upper_ghost)
    grad_axial = 0.5 * (padded_axial[:, :, 2:] - padded_axial[:, :, :-2])
    grad_pitch = 0.5 * (padded_pitch[:, 2:, :] - padded_pitch[:, :-2, :])
    laplacian = (
        padded_axial[:, :, 2:]
        + padded_axial[:, :, :-2]
        + padded_pitch[:, 2:, :]
        + padded_pitch[:, :-2, :]
        - 4.0 * state
    )
    flux = jnp.einsum("ij,jpx->ipx", axial_jacobian, grad_axial, precision=PRECISE)
    flux = flux + jnp.einsum("ij,jpx->ipx", pitch_jacobian, grad_pitch, precision=PRECISE)
    return DIFFUSION * laplacian - flux


def single_field_grads(field, before, after):
    padded_axial = jnp.concatenate([before, field, after], axis=-1)
    zero_row = jnp.zeros_like(field[..., :1, :])
    padded_pitch = jnp.concatenate([zero_row, field, zero_row], axis=-2)
    grad_axial = 0.5 * (padded_axial[..., 2:] - padded_axial[..., :-2])
    grad_pitch = 0.5 * (padded_pitch[..., 2:, :] - padded_pitch[..., :-2, :])
    laplacian = (
        padded_axial[..., 2:]
        + padded_axial[..., :-2]
        + padded_pitch[..., 2:, :]
        + padded_pitch[..., :-2, :]
        - 4.0 * field
    )
    return grad_axial, grad_pitch, laplacian


def modal_field(weights, mode_shape):
    return jnp.einsum("m,mpx->px", weights, mode_shape, precision=PRECISE)


def projection(mode_shape, field):
    return jnp.einsum("mpx,px->m", mode_shape, field, precision=PRECISE)


def add_field_one(rate, extra):
    return rate.at[1].add(extra)


def rate_field4(state, lower_ghost, upper_ghost, axial_jacobian, pitch_jacobian):
    zero_col = jnp.zeros_like(state[..., :1])
    padded_axial = jnp.concatenate([zero_col, state, zero_col], axis=-1)
    padded_pitch = pitch_pad(state, lower_ghost, upper_ghost)
    grad_axial = 0.5 * (padded_axial[:, :, 2:] - padded_axial[:, :, :-2])
    grad_pitch = 0.5 * (padded_pitch[:, 2:, :] - padded_pitch[:, :-2, :])
    laplacian = (
        padded_axial[4, :, 2:]
        + padded_axial[4, :, :-2]
        + padded_pitch[4, 2:, :]
        + padded_pitch[4, :-2, :]
        - 4.0 * state[4]
    )
    flux = jnp.einsum("j,jpx->px", axial_jacobian[4], grad_axial, precision=PRECISE)
    flux = flux + jnp.einsum("j,jpx->px", pitch_jacobian[4], grad_pitch, precision=PRECISE)
    return DIFFUSION * laplacian - flux


def pack(parts, width):
    flat = [part.reshape(-1, width) for part in parts]
    return jnp.concatenate(flat, axis=0)


def unpack(buffer, shapes):
    out, offset = [], 0
    for shape in shapes:
        count = math.prod(shape[:-1])
        out.append(buffer[offset : offset + count].reshape(shape))
        offset += count
    return out


LANES = 128


def lane_roll(x, shift):
    return pltpu.roll(x, shift % x.shape[-1], x.ndim - 1)


def row_roll(x, shift):
    return pltpu.roll(x, shift % x.shape[0], 0)


def kernel_rate(state, lower, upper, jac, push, inside, fields_out):
    ax, pt = jac
    rows = state[0].shape[0]
    row = lax.broadcasted_iota(jnp.int32, state[0].shape, 0)
    grads_a, grads_p, laps = [], [], []
    for j, s in enumerate(state):
        east = lane_roll(s, -1)
        west = lane_roll(s, 1)
        north = jnp.where(row == rows - 1, upper[j], row_roll(s, -1))
        south = jnp.where(row == 0, lower[j], row_roll(s, 1))
        grads_a.append(0.5 * (east - west))
        grads_p.append(0.5 * (north - south))
        laps.append(east + west + north + south - 4.0 * s)
    out = []
    for i in fields_out:
        r = DIFFUSION * laps[i]
        for j in range(len(state)):
            r = r - ax[i][j] * grads_a[j] - pt[i][j] * grads_p[j]
        if i == 1 and push is not None:
            r = r + push
        out.append(r * inside)
    return out


def read_jacobians(sc_ref, fields):
    ax = [[sc_ref[i * fields + j] for j in range(fields)] for i in range(fields)]
    pt = [[sc_ref[fields * fields + i * fields + j] for j in range(fields)] for i in range(fields)]
    return ax, pt


def lane_fold(x):
    x = jnp.sum(x, axis=0, keepdims=True)
    total = x[:, :LANES]
    for t in range(1, x.shape[1] // LANES):
        total = total + x[:, t * LANES : (t + 1) * LANES]
    return total


def pick_kernel(peers, lower_slot_ref, upper_slot_ref, upper_hist_ref, lower_hist_ref, up_ref, down_ref):
    slots = upper_hist_ref.shape[0]
    position = lax.axis_index("blk")
    slot_next = lower_slot_ref[(position + 1) % peers]
    slot_prev = upper_slot_ref[(position + peers - 1) % peers]
    for s in range(up_ref.shape[0]):
        up_ref[s] = upper_hist_ref[(slot_next + s) % slots]
        down_ref[s] = lower_hist_ref[(slot_prev + s) % slots]


def widened(own, left, right):
    tile = right + lane_roll(left, -2 * STEP_COUNT)
    return jnp.concatenate([own, tile], axis=-1)


def lane_masks(peers, shape, own_width):
    reach = 2 * STEP_COUNT
    me = lax.axis_index("mesh")
    lane = lax.broadcasted_iota(jnp.int32, shape, len(shape) - 1)
    width = shape[-1]
    right_ok = (lane >= own_width) & (lane < own_width + reach) & (me < peers - 1)
    left_ok = (lane >= width - reach) & (me > 0)
    owned = lane < own_width
    inside = owned | right_ok | left_ok
    return inside.astype(jnp.float32), owned.astype(jnp.float32)


def assemble(u_ref, ms_ref, glo_ref, gup_ref, left_ref, right_ref, fields, modes, pitch):
    u = []
    for j in range(fields):
        rows = slice(j * pitch, (j + 1) * pitch)
        u.append(widened(u_ref[j], left_ref[rows, :], right_ref[rows, :]))
    ms = []
    for m in range(modes):
        rows = slice((fields + m) * pitch, (fields + m + 1) * pitch)
        ms.append(widened(ms_ref[m], left_ref[rows, :], right_ref[rows, :]))
    base = (fields + modes) * pitch
    steps = glo_ref.shape[0]
    ghosts = []
    for side, ref in enumerate((glo_ref, gup_ref)):
        per_step = []
        for s in range(steps):
            start = base + (side * steps + s) * fields
            rows = slice(start, start + fields)
            block = widened(ref[s], left_ref[rows, :], right_ref[rows, :])
            per_step.append([block[j : j + 1, :] for j in range(fields)])
        ghosts.append(per_step)
    return u, ms, ghosts[0], ghosts[1]


def first_kernel(peers, sc_ref, u_ref, ms_ref, glo_ref, gup_ref, left_ref, right_ref, a_ref, part_ref):
    h = TIME_STEP
    fields = u_ref.shape[0]
    modes = ms_ref.shape[0]
    pitch = u_ref.shape[1]
    jac = read_jacobians(sc_ref, fields)
    base = 2 * fields * fields
    vel = [sc_ref[base + m] for m in range(modes)]
    u0, ms, gl, gu = assemble(u_ref, ms_ref, glo_ref, gup_ref, left_ref, right_ref, fields, modes, pitch)
    inside, owned = lane_masks(peers, u0[0].shape, u_ref.shape[-1])
    push = vel[0] * ms[0]
    for m in range(1, modes):
        push = push + vel[m] * ms[m]
    push = COUPLING * push
    gl1, gu1, gl2, gu2 = gl[0], gu[0], gl[1], gu[1]
    every = list(range(fields))
    k1 = kernel_rate(u0, gl1, gu1, jac, push, inside, every)
    mid = [u0[j] + h * k1[j] for j in every]
    k2 = kernel_rate(mid, gl1, gu1, jac, push, inside, every)
    a = [u0[j] + 0.5 * h * (k1[j] + k2[j]) for j in every]
    for j in every:
        a_ref[j] = a[j]
    (ra4,) = kernel_rate(a, gl2, gu2, jac, None, inside, [4])
    weighted = [ms[m] * owned for m in range(modes)]
    k = 0
    for field in (u0[4], mid[4], a[4], ra4):
        for m in range(modes):
            part_ref[k : k + 1, :] = lane_fold(weighted[m] * field)
            k += 1
    ax41, pt41 = jac[0][4][1], jac[1][4][1]
    rows = ms[0].shape[0]
    row = lax.broadcasted_iota(jnp.int32, ms[0].shape, 0)
    for n in range(modes):
        s = ms[n]
        ga = 0.5 * (lane_roll(s, -1) - lane_roll(s, 1))
        north = jnp.where(row == rows - 1, 0.0, row_roll(s, -1))
        south = jnp.where(row == 0, 0.0, row_roll(s, 1))
        gp = 0.5 * (north - south)
        t = -(ax41 * ga + pt41 * gp)
        for m in range(modes):
            part_ref[k + m * modes + n : k + m * modes + n + 1, :] = lane_fold(weighted[m] * t)


def second_kernel(peers, sc_ref, a_ref, u_ref, ms_ref, glo_ref, gup_ref, left_ref, right_ref, out_ref):
    h = TIME_STEP
    fields = a_ref.shape[0]
    modes = ms_ref.shape[0]
    pitch = u_ref.shape[1]
    jac = read_jacobians(sc_ref, fields)
    base = 2 * fields * fields
    coef = [[sc_ref[base + w * modes + m] for m in range(modes)] for w in range(3)]
    _, ms, gl, gu = assemble(u_ref, ms_ref, glo_ref, gup_ref, left_ref, right_ref, fields, modes, pitch)
    inside, _ = lane_masks(peers, ms[0].shape, u_ref.shape[-1])

    def combine(weights):
        total = weights[0] * ms[0]
        for m in range(1, modes):
            total = total + weights[m] * ms[m]
        return total

    gl2, gu2 = gl[1], gu[1]
    every = list(range(fields))
    s1 = [a_ref[j] for j in every]
    s1[1] = s1[1] + combine(coef[0])
    k1 = kernel_rate(s1, gl2, gu2, jac, COUPLING * combine(coef[1]), inside, every)
    mid = [s1[j] + h * k1[j] for j in every]
    k2 = kernel_rate(mid, gl2, gu2, jac, COUPLING * combine(coef[2]), inside, every)
    width = out_ref.shape[-1]
    for j in every:
        s2 = s1[j] + 0.5 * h * (k1[j] + k2[j])
        out_ref[j] = s2[:, :width]


def vmem_spec():
    return pl.BlockSpec(memory_space=pltpu.VMEM)


def smem_spec():
    return pl.BlockSpec(memory_space=pltpu.SMEM)


def on_device(
    flow_field,
    lower_row_history,
    upper_row_history,
    lower_lag_slot,
    upper_lag_slot,
    axial_jacobian,
    pitch_jacobian,
    mode_shape,
    stiffness,
    displacement,
    velocity,
):
    h = TIME_STEP
    state0 = flow_field[0]
    fields, pitch_cells, axial_cells = state0.shape
    modes = mode_shape.shape[0]
    mesh_peers = lax.axis_size("mesh")
    me = lax.axis_index("mesh")
    force_scale = 1.0 / math.sqrt(pitch_cells * axial_cells * mesh_peers)
    passages = lax.axis_size("blk")
    position = lax.axis_index("blk")
    blade_stiffness = stiffness[0]
    disp0 = displacement[0]
    vel0 = velocity[0]

    row_shape = jax.ShapeDtypeStruct((STEP_COUNT,) + upper_row_history.shape[2:], state0.dtype)
    rows_up, rows_down = pl.pallas_call(
        functools.partial(pick_kernel, passages),
        out_shape=(row_shape, row_shape),
        in_specs=[smem_spec(), smem_spec(), vmem_spec(), vmem_spec()],
        out_specs=(vmem_spec(), vmem_spec()),
    )(lower_lag_slot, upper_lag_slot, upper_row_history[0], lower_row_history[0])
    lower_ghosts = shifted(rows_up, "blk", 1)
    upper_ghosts = shifted(rows_down, "blk", -1)

    reach = 2 * STEP_COUNT
    own = [state0, mode_shape, lower_ghosts, upper_ghosts]
    shapes = [part.shape[:-1] + (reach,) for part in own]
    from_left = shifted(pack([part[..., -reach:] for part in own], reach), "mesh", 1)
    from_right = shifted(pack([part[..., :reach] for part in own], reach), "mesh", -1)
    from_left = jnp.where(me > 0, from_left, jnp.zeros_like(from_left))
    from_right = jnp.where(me < mesh_peers - 1, from_right, jnp.zeros_like(from_right))
    pad = [(0, 0), (0, LANES - reach)]
    from_left = jnp.pad(from_left, pad)
    from_right = jnp.pad(from_right, pad)
    lanes_wide = axial_cells + LANES
    ins = (state0, mode_shape, lower_ghosts, upper_ghosts, from_left, from_right)

    jac_flat = jnp.concatenate([axial_jacobian.reshape(-1), pitch_jacobian.reshape(-1)])
    base1, part_lanes = pl.pallas_call(
        functools.partial(first_kernel, mesh_peers),
        out_shape=(
            jax.ShapeDtypeStruct((fields, pitch_cells, lanes_wide), state0.dtype),
            jax.ShapeDtypeStruct((4 * modes + modes * modes, LANES), state0.dtype),
        ),
        in_specs=[smem_spec()] + [vmem_spec()] * 6,
        out_specs=(vmem_spec(), vmem_spec()),
    )(jnp.concatenate([jac_flat, vel0]), *ins)

    totals = mesh_sum(jnp.sum(part_lanes, axis=1))
    force0 = force_scale * totals[0:modes]
    force1 = force_scale * totals[modes : 2 * modes]
    force2 = force_scale * totals[2 * modes : 3 * modes]
    force3 = force_scale * totals[3 * modes : 4 * modes]
    couple = force_scale * totals[4 * modes :].reshape(modes, modes)

    acc1 = force0 - blade_stiffness * disp0 - DAMPING * vel0
    disp1m = disp0 + h * vel0
    vel1m = vel0 + h * acc1
    acc1m = force1 - blade_stiffness * disp1m - DAMPING * vel1m
    disp1 = disp0 + 0.5 * h * (vel0 + vel1m)
    vel1 = vel0 + 0.5 * h * (acc1 + acc1m)

    acc2 = force2 - blade_stiffness * disp1 - DAMPING * vel1
    disp2m = disp1 + h * vel1
    vel2m = vel1 + h * acc2
    corr = 0.5 * h * h * COUPLING
    force2m = force2 + h * force3 + h * corr * jnp.dot(couple, acc1, precision=PRECISE)
    acc2m = force2m - blade_stiffness * disp2m - DAMPING * vel2m
    disp2 = disp1 + 0.5 * h * (vel1 + vel2m)
    vel2 = vel1 + 0.5 * h * (acc2 + acc2m)

    state2 = pl.pallas_call(
        functools.partial(second_kernel, mesh_peers),
        out_shape=jax.ShapeDtypeStruct(state0.shape, state0.dtype),
        in_specs=[smem_spec()] + [vmem_spec()] * 7,
        out_specs=vmem_spec(),
    )(jnp.concatenate([jac_flat, corr * acc1, vel1, vel2m]), base1, *ins)
    return (state2[None], disp2[None], vel2[None])


def solution(mesh):
    return jax.shard_map(
        on_device,
        mesh=mesh,
        in_specs=(
            P("blk", None, None, "mesh"),
            P("blk", None, None, "mesh"),
            P("blk", None, None, "mesh"),
            P(),
            P(),
            P(),
            P(),
            P(None, None, "mesh"),
            P("blk", None),
            P("blk", None),
            P("blk", None),
        ),
        out_specs=(P("blk", None, None, "mesh"), P("blk", None), P("blk", None)),
        check_vma=False,
    )
```

```python
import functools
import math

import jax
import jax.numpy as jnp
from jax import lax
from jax.experimental import pallas as pl
from jax.experimental.pallas import tpu as pltpu
from jax.sharding import PartitionSpec as P

STEP_COUNT = 2


PRECISE = lax.Precision.HIGHEST
TIME_STEP = 0.4
DIFFUSION = 0.1
COUPLING = 0.3
DAMPING = 0.1


def shifted(value, axis, by):
    peers = lax.axis_size(axis)
    return lax.ppermute(value, axis, [(i, (i + by) % peers) for i in range(peers)])


def halo(value):
    peers = lax.axis_size("mesh")
    me = lax.axis_index("mesh")
    before = shifted(value[..., -1:], "mesh", 1)
    after = shifted(value[..., :1], "mesh", -1)
    before = jnp.where(me > 0, before, jnp.zeros_like(before))
    after = jnp.where(me < peers - 1, after, jnp.zeros_like(after))
    return before, after


def mesh_sum(value):
    peers = lax.axis_size("mesh")
    if peers & (peers - 1):
        return lax.psum(value, "mesh")
    step = 1
    while step < peers:
        value = value + lax.ppermute(value, "mesh", [(i, i ^ step) for i in range(peers)])
        step *= 2
    return value


def pick_rows(table, index, count):
    slots = table.shape[0]
    slot = jnp.arange(slots, dtype=jnp.int32).reshape((slots,) + (1,) * (table.ndim - 1))
    rows = []
    for s in range(count):
        hit = slot == (index + s) % slots
        rows.append(jnp.sum(jnp.where(hit, table, jnp.zeros_like(table)), axis=0))
    return jnp.stack(rows)


def pick_entry(values, index):
    hit = jnp.arange(values.shape[0], dtype=jnp.int32) == index
    return jnp.sum(jnp.where(hit, values, jnp.zeros_like(values)))


def axial_pad(value, before, after):
    return jnp.concatenate([before, value, after], axis=-1)


def pitch_pad(value, lower, upper):
    return jnp.concatenate([lower[:, None, :], value, upper[:, None, :]], axis=1)


def flow_rate(state, before, after, lower_ghost, upper_ghost, axial_jacobian, pitch_jacobian):
    padded_axial = axial_pad(state, before, after)
    padded_pitch = pitch_pad(state, lower_ghost, upper_ghost)
    grad_axial = 0.5 * (padded_axial[:, :, 2:] - padded_axial[:, :, :-2])
    grad_pitch = 0.5 * (padded_pitch[:, 2:, :] - padded_pitch[:, :-2, :])
    laplacian = (
        padded_axial[:, :, 2:]
        + padded_axial[:, :, :-2]
        + padded_pitch[:, 2:, :]
        + padded_pitch[:, :-2, :]
        - 4.0 * state
    )
    flux = jnp.einsum("ij,jpx->ipx", axial_jacobian, grad_axial, precision=PRECISE)
    flux = flux + jnp.einsum("ij,jpx->ipx", pitch_jacobian, grad_pitch, precision=PRECISE)
    return DIFFUSION * laplacian - flux


def single_field_grads(field, before, after):
    padded_axial = jnp.concatenate([before, field, after], axis=-1)
    zero_row = jnp.zeros_like(field[..., :1, :])
    padded_pitch = jnp.concatenate([zero_row, field, zero_row], axis=-2)
    grad_axial = 0.5 * (padded_axial[..., 2:] - padded_axial[..., :-2])
    grad_pitch = 0.5 * (padded_pitch[..., 2:, :] - padded_pitch[..., :-2, :])
    laplacian = (
        padded_axial[..., 2:]
        + padded_axial[..., :-2]
        + padded_pitch[..., 2:, :]
        + padded_pitch[..., :-2, :]
        - 4.0 * field
    )
    return grad_axial, grad_pitch, laplacian


def modal_field(weights, mode_shape):
    return jnp.einsum("m,mpx->px", weights, mode_shape, precision=PRECISE)


def projection(mode_shape, field):
    return jnp.einsum("mpx,px->m", mode_shape, field, precision=PRECISE)


def add_field_one(rate, extra):
    return rate.at[1].add(extra)


def rate_field4(state, lower_ghost, upper_ghost, axial_jacobian, pitch_jacobian):
    zero_col = jnp.zeros_like(state[..., :1])
    padded_axial = jnp.concatenate([zero_col, state, zero_col], axis=-1)
    padded_pitch = pitch_pad(state, lower_ghost, upper_ghost)
    grad_axial = 0.5 * (padded_axial[:, :, 2:] - padded_axial[:, :, :-2])
    grad_pitch = 0.5 * (padded_pitch[:, 2:, :] - padded_pitch[:, :-2, :])
    laplacian = (
        padded_axial[4, :, 2:]
        + padded_axial[4, :, :-2]
        + padded_pitch[4, 2:, :]
        + padded_pitch[4, :-2, :]
        - 4.0 * state[4]
    )
    flux = jnp.einsum("j,jpx->px", axial_jacobian[4], grad_axial, precision=PRECISE)
    flux = flux + jnp.einsum("j,jpx->px", pitch_jacobian[4], grad_pitch, precision=PRECISE)
    return DIFFUSION * laplacian - flux


def pack(parts, width):
    flat = [jnp.moveaxis(part, -1, 0).reshape(width, -1) for part in parts]
    return jnp.concatenate(flat, axis=1)


def unpack(buffer, shapes):
    out, offset = [], 0
    for shape in shapes:
        count = math.prod(shape[:-1])
        out.append(buffer[offset : offset + count].reshape(shape))
        offset += count
    return out


LANES = 128


def lane_roll(x, shift):
    return pltpu.roll(x, shift % x.shape[-1], x.ndim - 1)


def row_roll(x, shift):
    return pltpu.roll(x, shift % x.shape[0], 0)


def kernel_rate(state, lower, upper, jac, push, inside, fields_out):
    ax, pt = jac
    rows = state[0].shape[0]
    row = lax.broadcasted_iota(jnp.int32, state[0].shape, 0)
    grads_a, grads_p, laps = [], [], []
    for j, s in enumerate(state):
        east = lane_roll(s, -1)
        west = lane_roll(s, 1)
        north = jnp.where(row == rows - 1, upper[j], row_roll(s, -1))
        south = jnp.where(row == 0, lower[j], row_roll(s, 1))
        grads_a.append(0.5 * (east - west))
        grads_p.append(0.5 * (north - south))
        laps.append(east + west + north + south - 4.0 * s)
    out = []
    for i in fields_out:
        r = DIFFUSION * laps[i]
        for j in range(len(state)):
            r = r - ax[i][j] * grads_a[j] - pt[i][j] * grads_p[j]
        if i == 1 and push is not None:
            r = r + push
        out.append(r * inside)
    return out


def read_jacobians(sc_ref, fields):
    ax = [[sc_ref[i * fields + j] for j in range(fields)] for i in range(fields)]
    pt = [[sc_ref[fields * fields + i * fields + j] for j in range(fields)] for i in range(fields)]
    return ax, pt


def lane_fold(x):
    x = jnp.sum(x, axis=0, keepdims=True)
    total = x[:, :LANES]
    for t in range(1, x.shape[1] // LANES):
        total = total + x[:, t * LANES : (t + 1) * LANES]
    return total


def pick_kernel(peers, lower_slot_ref, upper_slot_ref, upper_hist_ref, lower_hist_ref, up_ref, down_ref):
    fields, slots = upper_hist_ref.shape[0], upper_hist_ref.shape[1]
    position = lax.axis_index("blk")
    slot_next = lower_slot_ref[(position + 1) % peers]
    slot_prev = upper_slot_ref[(position + peers - 1) % peers]
    for s in range(up_ref.shape[0]):
        up_at = (slot_next + s) % slots
        down_at = (slot_prev + s) % slots
        for f in range(fields):
            up_ref[s, f : f + 1, :] = upper_hist_ref[f, pl.ds(up_at, 1), :]
            down_ref[s, f : f + 1, :] = lower_hist_ref[f, pl.ds(down_at, 1), :]


def widened(own, left, right):
    tile = right + lane_roll(left, -2 * STEP_COUNT)
    return jnp.concatenate([own, tile], axis=-1)


def lane_masks(peers, shape, own_width):
    reach = 2 * STEP_COUNT
    me = lax.axis_index("mesh")
    lane = lax.broadcasted_iota(jnp.int32, shape, len(shape) - 1)
    width = shape[-1]
    right_ok = (lane >= own_width) & (lane < own_width + reach) & (me < peers - 1)
    left_ok = (lane >= width - reach) & (me > 0)
    owned = lane < own_width
    inside = owned | right_ok | left_ok
    return inside.astype(jnp.float32), owned.astype(jnp.float32)


def assemble(u_ref, ms_ref, glo_ref, gup_ref, left_ref, right_ref, fields, modes, pitch):
    u = []
    for j in range(fields):
        rows = slice(j * pitch, (j + 1) * pitch)
        u.append(widened(u_ref[j], left_ref[rows, :], right_ref[rows, :]))
    ms = []
    for m in range(modes):
        rows = slice((fields + m) * pitch, (fields + m + 1) * pitch)
        ms.append(widened(ms_ref[m], left_ref[rows, :], right_ref[rows, :]))
    base = (fields + modes) * pitch
    steps = glo_ref.shape[0]
    ghosts = []
    for side, ref in enumerate((glo_ref, gup_ref)):
        per_step = []
        for s in range(steps):
            start = base + (side * steps + s) * fields
            rows = slice(start, start + fields)
            block = widened(ref[s], left_ref[rows, :], right_ref[rows, :])
            per_step.append([block[j : j + 1, :] for j in range(fields)])
        ghosts.append(per_step)
    return u, ms, ghosts[0], ghosts[1]


def first_kernel(peers, sc_ref, u_ref, ms_ref, glo_ref, gup_ref, left_ref, right_ref, a_ref, part_ref):
    h = TIME_STEP
    fields = u_ref.shape[0]
    modes = ms_ref.shape[0]
    pitch = u_ref.shape[1]
    jac = read_jacobians(sc_ref, fields)
    base = 2 * fields * fields
    vel = [sc_ref[base + m] for m in range(modes)]
    u0, ms, gl, gu = assemble(u_ref, ms_ref, glo_ref, gup_ref, left_ref, right_ref, fields, modes, pitch)
    inside, owned = lane_masks(peers, u0[0].shape, u_ref.shape[-1])
    push = vel[0] * ms[0]
    for m in range(1, modes):
        push = push + vel[m] * ms[m]
    push = COUPLING * push
    gl1, gu1, gl2, gu2 = gl[0], gu[0], gl[1], gu[1]
    every = list(range(fields))
    k1 = kernel_rate(u0, gl1, gu1, jac, push, inside, every)
    mid = [u0[j] + h * k1[j] for j in every]
    k2 = kernel_rate(mid, gl1, gu1, jac, push, inside, every)
    a = [u0[j] + 0.5 * h * (k1[j] + k2[j]) for j in every]
    for j in every:
        a_ref[j] = a[j]
    (ra4,) = kernel_rate(a, gl2, gu2, jac, None, inside, [4])
    weighted = [ms[m] * owned for m in range(modes)]
    k = 0
    for field in (u0[4], mid[4], a[4], ra4):
        for m in range(modes):
            part_ref[k : k + 1, :] = lane_fold(weighted[m] * field)
            k += 1
    ax41, pt41 = jac[0][4][1], jac[1][4][1]
    rows = ms[0].shape[0]
    row = lax.broadcasted_iota(jnp.int32, ms[0].shape, 0)
    for n in range(modes):
        s = ms[n]
        ga = 0.5 * (lane_roll(s, -1) - lane_roll(s, 1))
        north = jnp.where(row == rows - 1, 0.0, row_roll(s, -1))
        south = jnp.where(row == 0, 0.0, row_roll(s, 1))
        gp = 0.5 * (north - south)
        t = -(ax41 * ga + pt41 * gp)
        for m in range(modes):
            part_ref[k + m * modes + n : k + m * modes + n + 1, :] = lane_fold(weighted[m] * t)


def second_kernel(peers, sc_ref, a_ref, u_ref, ms_ref, glo_ref, gup_ref, left_ref, right_ref, out_ref):
    h = TIME_STEP
    fields = a_ref.shape[0]
    modes = ms_ref.shape[0]
    pitch = u_ref.shape[1]
    jac = read_jacobians(sc_ref, fields)
    base = 2 * fields * fields
    coef = [[sc_ref[base + w * modes + m] for m in range(modes)] for w in range(3)]
    _, ms, gl, gu = assemble(u_ref, ms_ref, glo_ref, gup_ref, left_ref, right_ref, fields, modes, pitch)
    inside, _ = lane_masks(peers, ms[0].shape, u_ref.shape[-1])

    def combine(weights):
        total = weights[0] * ms[0]
        for m in range(1, modes):
            total = total + weights[m] * ms[m]
        return total

    gl2, gu2 = gl[1], gu[1]
    every = list(range(fields))
    s1 = [a_ref[j] for j in every]
    s1[1] = s1[1] + combine(coef[0])
    k1 = kernel_rate(s1, gl2, gu2, jac, COUPLING * combine(coef[1]), inside, every)
    mid = [s1[j] + h * k1[j] for j in every]
    k2 = kernel_rate(mid, gl2, gu2, jac, COUPLING * combine(coef[2]), inside, every)
    width = out_ref.shape[-1]
    for j in every:
        s2 = s1[j] + 0.5 * h * (k1[j] + k2[j])
        out_ref[j] = s2[:, :width]


def vmem_spec():
    return pl.BlockSpec(memory_space=pltpu.VMEM)


def smem_spec():
    return pl.BlockSpec(memory_space=pltpu.SMEM)


def on_device(
    flow_field,
    lower_row_history,
    upper_row_history,
    lower_lag_slot,
    upper_lag_slot,
    axial_jacobian,
    pitch_jacobian,
    mode_shape,
    stiffness,
    displacement,
    velocity,
):
    h = TIME_STEP
    state0 = flow_field[0]
    fields, pitch_cells, axial_cells = state0.shape
    modes = mode_shape.shape[0]
    mesh_peers = lax.axis_size("mesh")
    me = lax.axis_index("mesh")
    force_scale = 1.0 / math.sqrt(pitch_cells * axial_cells * mesh_peers)
    passages = lax.axis_size("blk")
    position = lax.axis_index("blk")
    blade_stiffness = stiffness[0]
    disp0 = displacement[0]
    vel0 = velocity[0]

    row_shape = jax.ShapeDtypeStruct((STEP_COUNT,) + upper_row_history.shape[2:], state0.dtype)
    rows_up, rows_down = pl.pallas_call(
        functools.partial(pick_kernel, passages),
        out_shape=(row_shape, row_shape),
        in_specs=[smem_spec(), smem_spec(), vmem_spec(), vmem_spec()],
        out_specs=(vmem_spec(), vmem_spec()),
    )(
        lower_lag_slot,
        upper_lag_slot,
        jnp.transpose(upper_row_history[0], (1, 0, 2)),
        jnp.transpose(lower_row_history[0], (1, 0, 2)),
    )
    lower_ghosts = shifted(rows_up, "blk", 1)
    upper_ghosts = shifted(rows_down, "blk", -1)

    reach = 2 * STEP_COUNT
    own = [state0, mode_shape, lower_ghosts, upper_ghosts]
    shapes = [part.shape[:-1] + (reach,) for part in own]
    from_left = shifted(pack([part[..., -reach:] for part in own], reach).reshape(-1), "mesh", 1)
    from_right = shifted(pack([part[..., :reach] for part in own], reach).reshape(-1), "mesh", -1)
    from_left = from_left.reshape(reach, -1)
    from_right = from_right.reshape(reach, -1)
    from_left = jnp.where(me > 0, from_left, jnp.zeros_like(from_left))
    from_right = jnp.where(me < mesh_peers - 1, from_right, jnp.zeros_like(from_right))
    pad = [(0, 0), (0, LANES - reach)]
    from_left = jnp.pad(from_left.T, pad)
    from_right = jnp.pad(from_right.T, pad)
    lanes_wide = axial_cells + LANES
    ins = (state0, mode_shape, lower_ghosts, upper_ghosts, from_left, from_right)

    jac_flat = jnp.concatenate([axial_jacobian.reshape(-1), pitch_jacobian.reshape(-1)])
    base1, part_lanes = pl.pallas_call(
        functools.partial(first_kernel, mesh_peers),
        out_shape=(
            jax.ShapeDtypeStruct((fields, pitch_cells, lanes_wide), state0.dtype),
            jax.ShapeDtypeStruct((4 * modes + modes * modes, LANES), state0.dtype),
        ),
        in_specs=[smem_spec()] + [vmem_spec()] * 6,
        out_specs=(vmem_spec(), vmem_spec()),
    )(jnp.concatenate([jac_flat, vel0]), *ins)

    totals = mesh_sum(jnp.sum(part_lanes, axis=1))
    force0 = force_scale * totals[0:modes]
    force1 = force_scale * totals[modes : 2 * modes]
    force2 = force_scale * totals[2 * modes : 3 * modes]
    force3 = force_scale * totals[3 * modes : 4 * modes]
    couple = force_scale * totals[4 * modes :].reshape(modes, modes)

    acc1 = force0 - blade_stiffness * disp0 - DAMPING * vel0
    disp1m = disp0 + h * vel0
    vel1m = vel0 + h * acc1
    acc1m = force1 - blade_stiffness * disp1m - DAMPING * vel1m
    disp1 = disp0 + 0.5 * h * (vel0 + vel1m)
    vel1 = vel0 + 0.5 * h * (acc1 + acc1m)

    acc2 = force2 - blade_stiffness * disp1 - DAMPING * vel1
    disp2m = disp1 + h * vel1
    vel2m = vel1 + h * acc2
    corr = 0.5 * h * h * COUPLING
    force2m = force2 + h * force3 + h * corr * jnp.dot(couple, acc1, precision=PRECISE)
    acc2m = force2m - blade_stiffness * disp2m - DAMPING * vel2m
    disp2 = disp1 + 0.5 * h * (vel1 + vel2m)
    vel2 = vel1 + 0.5 * h * (acc2 + acc2m)

    state2 = pl.pallas_call(
        functools.partial(second_kernel, mesh_peers),
        out_shape=jax.ShapeDtypeStruct(state0.shape, state0.dtype),
        in_specs=[smem_spec()] + [vmem_spec()] * 7,
        out_specs=vmem_spec(),
    )(jnp.concatenate([jac_flat, corr * acc1, vel1, vel2m]), base1, *ins)
    return (state2[None], disp2[None], vel2[None])


def solution(mesh):
    return jax.shard_map(
        on_device,
        mesh=mesh,
        in_specs=(
            P("blk", None, None, "mesh"),
            P("blk", None, None, "mesh"),
            P("blk", None, None, "mesh"),
            P(),
            P(),
            P(),
            P(),
            P(None, None, "mesh"),
            P("blk", None),
            P("blk", None),
            P("blk", None),
        ),
        out_specs=(P("blk", None, None, "mesh"), P("blk", None), P("blk", None)),
        check_vma=False,
    )
```

```python
import functools
import math

import jax
import jax.numpy as jnp
from jax import lax
from jax.experimental import pallas as pl
from jax.experimental.pallas import tpu as pltpu
from jax.sharding import PartitionSpec as P

STEP_COUNT = 2


PRECISE = lax.Precision.HIGHEST
TIME_STEP = 0.4
DIFFUSION = 0.1
COUPLING = 0.3
DAMPING = 0.1


def shifted(value, axis, by):
    peers = lax.axis_size(axis)
    return lax.ppermute(value, axis, [(i, (i + by) % peers) for i in range(peers)])


def halo(value):
    peers = lax.axis_size("mesh")
    me = lax.axis_index("mesh")
    before = shifted(value[..., -1:], "mesh", 1)
    after = shifted(value[..., :1], "mesh", -1)
    before = jnp.where(me > 0, before, jnp.zeros_like(before))
    after = jnp.where(me < peers - 1, after, jnp.zeros_like(after))
    return before, after


def mesh_sum(value):
    peers = lax.axis_size("mesh")
    if peers & (peers - 1):
        return lax.psum(value, "mesh")
    step = 1
    while step < peers:
        value = value + lax.ppermute(value, "mesh", [(i, i ^ step) for i in range(peers)])
        step *= 2
    return value


def pick_rows(table, index, count):
    slots = table.shape[0]
    slot = jnp.arange(slots, dtype=jnp.int32).reshape((slots,) + (1,) * (table.ndim - 1))
    rows = []
    for s in range(count):
        hit = slot == (index + s) % slots
        rows.append(jnp.sum(jnp.where(hit, table, jnp.zeros_like(table)), axis=0))
    return jnp.stack(rows)


def pick_entry(values, index):
    hit = jnp.arange(values.shape[0], dtype=jnp.int32) == index
    return jnp.sum(jnp.where(hit, values, jnp.zeros_like(values)))


def axial_pad(value, before, after):
    return jnp.concatenate([before, value, after], axis=-1)


def pitch_pad(value, lower, upper):
    return jnp.concatenate([lower[:, None, :], value, upper[:, None, :]], axis=1)


def flow_rate(state, before, after, lower_ghost, upper_ghost, axial_jacobian, pitch_jacobian):
    padded_axial = axial_pad(state, before, after)
    padded_pitch = pitch_pad(state, lower_ghost, upper_ghost)
    grad_axial = 0.5 * (padded_axial[:, :, 2:] - padded_axial[:, :, :-2])
    grad_pitch = 0.5 * (padded_pitch[:, 2:, :] - padded_pitch[:, :-2, :])
    laplacian = (
        padded_axial[:, :, 2:]
        + padded_axial[:, :, :-2]
        + padded_pitch[:, 2:, :]
        + padded_pitch[:, :-2, :]
        - 4.0 * state
    )
    flux = jnp.einsum("ij,jpx->ipx", axial_jacobian, grad_axial, precision=PRECISE)
    flux = flux + jnp.einsum("ij,jpx->ipx", pitch_jacobian, grad_pitch, precision=PRECISE)
    return DIFFUSION * laplacian - flux


def single_field_grads(field, before, after):
    padded_axial = jnp.concatenate([before, field, after], axis=-1)
    zero_row = jnp.zeros_like(field[..., :1, :])
    padded_pitch = jnp.concatenate([zero_row, field, zero_row], axis=-2)
    grad_axial = 0.5 * (padded_axial[..., 2:] - padded_axial[..., :-2])
    grad_pitch = 0.5 * (padded_pitch[..., 2:, :] - padded_pitch[..., :-2, :])
    laplacian = (
        padded_axial[..., 2:]
        + padded_axial[..., :-2]
        + padded_pitch[..., 2:, :]
        + padded_pitch[..., :-2, :]
        - 4.0 * field
    )
    return grad_axial, grad_pitch, laplacian


def modal_field(weights, mode_shape):
    return jnp.einsum("m,mpx->px", weights, mode_shape, precision=PRECISE)


def projection(mode_shape, field):
    return jnp.einsum("mpx,px->m", mode_shape, field, precision=PRECISE)


def add_field_one(rate, extra):
    return rate.at[1].add(extra)


def rate_field4(state, lower_ghost, upper_ghost, axial_jacobian, pitch_jacobian):
    zero_col = jnp.zeros_like(state[..., :1])
    padded_axial = jnp.concatenate([zero_col, state, zero_col], axis=-1)
    padded_pitch = pitch_pad(state, lower_ghost, upper_ghost)
    grad_axial = 0.5 * (padded_axial[:, :, 2:] - padded_axial[:, :, :-2])
    grad_pitch = 0.5 * (padded_pitch[:, 2:, :] - padded_pitch[:, :-2, :])
    laplacian = (
        padded_axial[4, :, 2:]
        + padded_axial[4, :, :-2]
        + padded_pitch[4, 2:, :]
        + padded_pitch[4, :-2, :]
        - 4.0 * state[4]
    )
    flux = jnp.einsum("j,jpx->px", axial_jacobian[4], grad_axial, precision=PRECISE)
    flux = flux + jnp.einsum("j,jpx->px", pitch_jacobian[4], grad_pitch, precision=PRECISE)
    return DIFFUSION * laplacian - flux


def pack(parts, width):
    flat = [jnp.moveaxis(part, -1, 0).reshape(width, -1) for part in parts]
    return jnp.concatenate(flat, axis=1)


def unpack(buffer, shapes):
    out, offset = [], 0
    for shape in shapes:
        count = math.prod(shape[:-1])
        out.append(buffer[offset : offset + count].reshape(shape))
        offset += count
    return out


LANES = 128


def lane_roll(x, shift):
    return pltpu.roll(x, shift % x.shape[-1], x.ndim - 1)


def row_roll(x, shift):
    return pltpu.roll(x, shift % x.shape[0], 0)


def kernel_rate(state, lower, upper, jac, push, inside, fields_out):
    ax, pt = jac
    rows = state[0].shape[0]
    row = lax.broadcasted_iota(jnp.int32, state[0].shape, 0)
    grads_a, grads_p, laps = [], [], []
    for j, s in enumerate(state):
        east = lane_roll(s, -1)
        west = lane_roll(s, 1)
        north = jnp.where(row == rows - 1, upper[j], row_roll(s, -1))
        south = jnp.where(row == 0, lower[j], row_roll(s, 1))
        grads_a.append(0.5 * (east - west))
        grads_p.append(0.5 * (north - south))
        laps.append(east + west + north + south - 4.0 * s)
    out = []
    for i in fields_out:
        r = DIFFUSION * laps[i]
        for j in range(len(state)):
            r = r - ax[i][j] * grads_a[j] - pt[i][j] * grads_p[j]
        if i == 1 and push is not None:
            r = r + push
        out.append(r * inside)
    return out


def read_jacobians(ax_ref, pt_ref, fields):
    ax = [[ax_ref[i, j] for j in range(fields)] for i in range(fields)]
    pt = [[pt_ref[i, j] for j in range(fields)] for i in range(fields)]
    return ax, pt


def lane_fold(x):
    x = jnp.sum(x, axis=0, keepdims=True)
    total = x[:, :LANES]
    for t in range(1, x.shape[1] // LANES):
        total = total + x[:, t * LANES : (t + 1) * LANES]
    return total


def pick_kernel(peers, lower_slot_ref, upper_slot_ref, upper_hist_ref, lower_hist_ref, up_ref, down_ref):
    fields, slots = upper_hist_ref.shape[0], upper_hist_ref.shape[1]
    position = lax.axis_index("blk")
    slot_next = lower_slot_ref[(position + 1) % peers]
    slot_prev = upper_slot_ref[(position + peers - 1) % peers]
    for s in range(up_ref.shape[0]):
        up_at = (slot_next + s) % slots
        down_at = (slot_prev + s) % slots
        for f in range(fields):
            up_ref[s, f : f + 1, :] = upper_hist_ref[f, pl.ds(up_at, 1), :]
            down_ref[s, f : f + 1, :] = lower_hist_ref[f, pl.ds(down_at, 1), :]


def widened(own, left, right):
    tile = right + lane_roll(left, -2 * STEP_COUNT)
    return jnp.concatenate([own, tile], axis=-1)


def lane_masks(peers, shape, own_width):
    reach = 2 * STEP_COUNT
    me = lax.axis_index("mesh")
    lane = lax.broadcasted_iota(jnp.int32, shape, len(shape) - 1)
    width = shape[-1]
    right_ok = (lane >= own_width) & (lane < own_width + reach) & (me < peers - 1)
    left_ok = (lane >= width - reach) & (me > 0)
    owned = lane < own_width
    inside = owned | right_ok | left_ok
    return inside.astype(jnp.float32), owned.astype(jnp.float32)


def assemble(u_ref, ms_ref, glo_ref, gup_ref, left_ref, right_ref, fields, modes, pitch):
    u = []
    for j in range(fields):
        rows = slice(j * pitch, (j + 1) * pitch)
        u.append(widened(u_ref[j], left_ref[rows, :], right_ref[rows, :]))
    ms = []
    for m in range(modes):
        rows = slice((fields + m) * pitch, (fields + m + 1) * pitch)
        ms.append(widened(ms_ref[m], left_ref[rows, :], right_ref[rows, :]))
    base = (fields + modes) * pitch
    steps = glo_ref.shape[0]
    ghosts = []
    for side, ref in enumerate((glo_ref, gup_ref)):
        per_step = []
        for s in range(steps):
            start = base + (side * steps + s) * fields
            rows = slice(start, start + fields)
            block = widened(ref[s], left_ref[rows, :], right_ref[rows, :])
            per_step.append([block[j : j + 1, :] for j in range(fields)])
        ghosts.append(per_step)
    return u, ms, ghosts[0], ghosts[1]


def first_kernel(peers, ax_ref, pt_ref, vel_ref, u_ref, ms_ref, glo_ref, gup_ref, left_ref, right_ref, a_ref, part_ref):
    h = TIME_STEP
    fields = u_ref.shape[0]
    modes = ms_ref.shape[0]
    pitch = u_ref.shape[1]
    jac = read_jacobians(ax_ref, pt_ref, fields)
    vel = [vel_ref[0, m] for m in range(modes)]
    u0, ms, gl, gu = assemble(u_ref, ms_ref, glo_ref, gup_ref, left_ref, right_ref, fields, modes, pitch)
    inside, owned = lane_masks(peers, u0[0].shape, u_ref.shape[-1])
    push = vel[0] * ms[0]
    for m in range(1, modes):
        push = push + vel[m] * ms[m]
    push = COUPLING * push
    gl1, gu1, gl2, gu2 = gl[0], gu[0], gl[1], gu[1]
    every = list(range(fields))
    k1 = kernel_rate(u0, gl1, gu1, jac, push, inside, every)
    mid = [u0[j] + h * k1[j] for j in every]
    k2 = kernel_rate(mid, gl1, gu1, jac, push, inside, every)
    a = [u0[j] + 0.5 * h * (k1[j] + k2[j]) for j in every]
    for j in every:
        a_ref[j] = a[j]
    (ra4,) = kernel_rate(a, gl2, gu2, jac, None, inside, [4])
    weighted = [ms[m] * owned for m in range(modes)]
    k = 0
    for field in (u0[4], mid[4], a[4], ra4):
        for m in range(modes):
            part_ref[k : k + 1, :] = lane_fold(weighted[m] * field)
            k += 1
    ax41, pt41 = jac[0][4][1], jac[1][4][1]
    rows = ms[0].shape[0]
    row = lax.broadcasted_iota(jnp.int32, ms[0].shape, 0)
    for n in range(modes):
        s = ms[n]
        ga = 0.5 * (lane_roll(s, -1) - lane_roll(s, 1))
        north = jnp.where(row == rows - 1, 0.0, row_roll(s, -1))
        south = jnp.where(row == 0, 0.0, row_roll(s, 1))
        gp = 0.5 * (north - south)
        t = -(ax41 * ga + pt41 * gp)
        for m in range(modes):
            part_ref[k + m * modes + n : k + m * modes + n + 1, :] = lane_fold(weighted[m] * t)


def modal_steps(force_scale, tot_ref, stiff_ref, disp_ref, vel_ref, modes):
    h = TIME_STEP
    t = [force_scale * tot_ref[k] for k in range(4 * modes + modes * modes)]
    force = [t[w * modes : (w + 1) * modes] for w in range(4)]
    couple = [t[4 * modes + m * modes : 4 * modes + (m + 1) * modes] for m in range(modes)]
    stiff = [stiff_ref[0, m] for m in range(modes)]
    disp0 = [disp_ref[0, m] for m in range(modes)]
    vel0 = [vel_ref[0, m] for m in range(modes)]

    def accel(f, q, v):
        return [f[m] - stiff[m] * q[m] - DAMPING * v[m] for m in range(modes)]

    def axpy(x, a, y):
        return [x[m] + a * y[m] for m in range(modes)]

    acc1 = accel(force[0], disp0, vel0)
    disp1m = axpy(disp0, h, vel0)
    vel1m = axpy(vel0, h, acc1)
    acc1m = accel(force[1], disp1m, vel1m)
    disp1 = [disp0[m] + 0.5 * h * (vel0[m] + vel1m[m]) for m in range(modes)]
    vel1 = [vel0[m] + 0.5 * h * (acc1[m] + acc1m[m]) for m in range(modes)]
    acc2 = accel(force[2], disp1, vel1)
    disp2m = axpy(disp1, h, vel1)
    vel2m = axpy(vel1, h, acc2)
    corr = 0.5 * h * h * COUPLING
    force2m = []
    for m in range(modes):
        coupled = couple[m][0] * acc1[0]
        for n in range(1, modes):
            coupled = coupled + couple[m][n] * acc1[n]
        force2m.append(force[2][m] + h * force[3][m] + h * corr * coupled)
    acc2m = accel(force2m, disp2m, vel2m)
    disp2 = [disp1[m] + 0.5 * h * (vel1[m] + vel2m[m]) for m in range(modes)]
    vel2 = [vel1[m] + 0.5 * h * (acc2[m] + acc2m[m]) for m in range(modes)]
    coef = [[corr * acc1[m] for m in range(modes)], vel1, vel2m]
    return coef, disp2, vel2


def second_kernel(
    peers,
    force_scale,
    tot_ref,
    stiff_ref,
    disp_ref,
    vel_ref,
    ax_ref,
    pt_ref,
    a_ref,
    u_ref,
    ms_ref,
    glo_ref,
    gup_ref,
    left_ref,
    right_ref,
    out_ref,
    disp_out_ref,
    vel_out_ref,
):
    h = TIME_STEP
    fields = a_ref.shape[0]
    modes = ms_ref.shape[0]
    pitch = u_ref.shape[1]
    jac = read_jacobians(ax_ref, pt_ref, fields)
    coef, disp2, vel2 = modal_steps(force_scale, tot_ref, stiff_ref, disp_ref, vel_ref, modes)
    for m in range(modes):
        disp_out_ref[0, m] = disp2[m]
        vel_out_ref[0, m] = vel2[m]
    _, ms, gl, gu = assemble(u_ref, ms_ref, glo_ref, gup_ref, left_ref, right_ref, fields, modes, pitch)
    inside, _ = lane_masks(peers, ms[0].shape, u_ref.shape[-1])

    def combine(weights):
        total = weights[0] * ms[0]
        for m in range(1, modes):
            total = total + weights[m] * ms[m]
        return total

    gl2, gu2 = gl[1], gu[1]
    every = list(range(fields))
    s1 = [a_ref[j] for j in every]
    s1[1] = s1[1] + combine(coef[0])
    k1 = kernel_rate(s1, gl2, gu2, jac, COUPLING * combine(coef[1]), inside, every)
    mid = [s1[j] + h * k1[j] for j in every]
    k2 = kernel_rate(mid, gl2, gu2, jac, COUPLING * combine(coef[2]), inside, every)
    width = out_ref.shape[-1]
    for j in every:
        s2 = s1[j] + 0.5 * h * (k1[j] + k2[j])
        out_ref[j] = s2[:, :width]


def vmem_spec():
    return pl.BlockSpec(memory_space=pltpu.VMEM)


def smem_spec():
    return pl.BlockSpec(memory_space=pltpu.SMEM)


def on_device(
    flow_field,
    lower_row_history,
    upper_row_history,
    lower_lag_slot,
    upper_lag_slot,
    axial_jacobian,
    pitch_jacobian,
    mode_shape,
    stiffness,
    displacement,
    velocity,
):
    h = TIME_STEP
    state0 = flow_field[0]
    fields, pitch_cells, axial_cells = state0.shape
    modes = mode_shape.shape[0]
    mesh_peers = lax.axis_size("mesh")
    me = lax.axis_index("mesh")
    force_scale = 1.0 / math.sqrt(pitch_cells * axial_cells * mesh_peers)
    passages = lax.axis_size("blk")
    position = lax.axis_index("blk")
    blade_stiffness = stiffness[0]
    disp0 = displacement[0]
    vel0 = velocity[0]

    row_shape = jax.ShapeDtypeStruct((STEP_COUNT,) + upper_row_history.shape[2:], state0.dtype)
    rows_up, rows_down = pl.pallas_call(
        functools.partial(pick_kernel, passages),
        out_shape=(row_shape, row_shape),
        in_specs=[smem_spec(), smem_spec(), vmem_spec(), vmem_spec()],
        out_specs=(vmem_spec(), vmem_spec()),
    )(
        lower_lag_slot,
        upper_lag_slot,
        jnp.transpose(upper_row_history[0], (1, 0, 2)),
        jnp.transpose(lower_row_history[0], (1, 0, 2)),
    )
    lower_ghosts = shifted(rows_up, "blk", 1)
    upper_ghosts = shifted(rows_down, "blk", -1)

    reach = 2 * STEP_COUNT
    own = [state0, mode_shape, lower_ghosts, upper_ghosts]
    shapes = [part.shape[:-1] + (reach,) for part in own]
    from_left = shifted(pack([part[..., -reach:] for part in own], reach).reshape(-1), "mesh", 1)
    from_right = shifted(pack([part[..., :reach] for part in own], reach).reshape(-1), "mesh", -1)
    from_left = from_left.reshape(reach, -1)
    from_right = from_right.reshape(reach, -1)
    from_left = jnp.where(me > 0, from_left, jnp.zeros_like(from_left))
    from_right = jnp.where(me < mesh_peers - 1, from_right, jnp.zeros_like(from_right))
    pad = [(0, 0), (0, LANES - reach)]
    from_left = jnp.pad(from_left.T, pad)
    from_right = jnp.pad(from_right.T, pad)
    lanes_wide = axial_cells + LANES
    ins = (state0, mode_shape, lower_ghosts, upper_ghosts, from_left, from_right)

    base1, part_lanes = pl.pallas_call(
        functools.partial(first_kernel, mesh_peers),
        out_shape=(
            jax.ShapeDtypeStruct((fields, pitch_cells, lanes_wide), state0.dtype),
            jax.ShapeDtypeStruct((4 * modes + modes * modes, LANES), state0.dtype),
        ),
        in_specs=[smem_spec()] * 3 + [vmem_spec()] * 6,
        out_specs=(vmem_spec(), vmem_spec()),
    )(axial_jacobian, pitch_jacobian, velocity, *ins)

    totals = mesh_sum(jnp.sum(part_lanes, axis=1))

    small = jax.ShapeDtypeStruct(displacement.shape, displacement.dtype)
    state2, disp2, vel2 = pl.pallas_call(
        functools.partial(second_kernel, mesh_peers, force_scale),
        out_shape=(jax.ShapeDtypeStruct(state0.shape, state0.dtype), small, small),
        in_specs=[smem_spec()] * 6 + [vmem_spec()] * 7,
        out_specs=(vmem_spec(), smem_spec(), smem_spec()),
    )(totals, stiffness, displacement, velocity, axial_jacobian, pitch_jacobian, base1, *ins)
    return (state2[None], disp2, vel2)


def solution(mesh):
    return jax.shard_map(
        on_device,
        mesh=mesh,
        in_specs=(
            P("blk", None, None, "mesh"),
            P("blk", None, None, "mesh"),
            P("blk", None, None, "mesh"),
            P(),
            P(),
            P(),
            P(),
            P(None, None, "mesh"),
            P("blk", None),
            P("blk", None),
            P("blk", None),
        ),
        out_specs=(P("blk", None, None, "mesh"), P("blk", None), P("blk", None)),
        check_vma=False,
    )
```

```python
import functools
import math

import jax
import jax.numpy as jnp
from jax import lax
from jax.experimental import pallas as pl
from jax.experimental.pallas import tpu as pltpu
from jax.sharding import PartitionSpec as P

STEP_COUNT = 2


PRECISE = lax.Precision.HIGHEST
TIME_STEP = 0.4
DIFFUSION = 0.1
COUPLING = 0.3
DAMPING = 0.1


def shifted(value, axis, by):
    peers = lax.axis_size(axis)
    return lax.ppermute(value, axis, [(i, (i + by) % peers) for i in range(peers)])


def halo(value):
    peers = lax.axis_size("mesh")
    me = lax.axis_index("mesh")
    before = shifted(value[..., -1:], "mesh", 1)
    after = shifted(value[..., :1], "mesh", -1)
    before = jnp.where(me > 0, before, jnp.zeros_like(before))
    after = jnp.where(me < peers - 1, after, jnp.zeros_like(after))
    return before, after


def mesh_sum(value):
    peers = lax.axis_size("mesh")
    if peers & (peers - 1):
        return lax.psum(value, "mesh")
    step = 1
    while step < peers:
        value = value + lax.ppermute(value, "mesh", [(i, i ^ step) for i in range(peers)])
        step *= 2
    return value


def pick_rows(table, index, count):
    slots = table.shape[0]
    slot = jnp.arange(slots, dtype=jnp.int32).reshape((slots,) + (1,) * (table.ndim - 1))
    rows = []
    for s in range(count):
        hit = slot == (index + s) % slots
        rows.append(jnp.sum(jnp.where(hit, table, jnp.zeros_like(table)), axis=0))
    return jnp.stack(rows)


def pick_entry(values, index):
    hit = jnp.arange(values.shape[0], dtype=jnp.int32) == index
    return jnp.sum(jnp.where(hit, values, jnp.zeros_like(values)))


def axial_pad(value, before, after):
    return jnp.concatenate([before, value, after], axis=-1)


def pitch_pad(value, lower, upper):
    return jnp.concatenate([lower[:, None, :], value, upper[:, None, :]], axis=1)


def flow_rate(state, before, after, lower_ghost, upper_ghost, axial_jacobian, pitch_jacobian):
    padded_axial = axial_pad(state, before, after)
    padded_pitch = pitch_pad(state, lower_ghost, upper_ghost)
    grad_axial = 0.5 * (padded_axial[:, :, 2:] - padded_axial[:, :, :-2])
    grad_pitch = 0.5 * (padded_pitch[:, 2:, :] - padded_pitch[:, :-2, :])
    laplacian = (
        padded_axial[:, :, 2:]
        + padded_axial[:, :, :-2]
        + padded_pitch[:, 2:, :]
        + padded_pitch[:, :-2, :]
        - 4.0 * state
    )
    flux = jnp.einsum("ij,jpx->ipx", axial_jacobian, grad_axial, precision=PRECISE)
    flux = flux + jnp.einsum("ij,jpx->ipx", pitch_jacobian, grad_pitch, precision=PRECISE)
    return DIFFUSION * laplacian - flux


def single_field_grads(field, before, after):
    padded_axial = jnp.concatenate([before, field, after], axis=-1)
    zero_row = jnp.zeros_like(field[..., :1, :])
    padded_pitch = jnp.concatenate([zero_row, field, zero_row], axis=-2)
    grad_axial = 0.5 * (padded_axial[..., 2:] - padded_axial[..., :-2])
    grad_pitch = 0.5 * (padded_pitch[..., 2:, :] - padded_pitch[..., :-2, :])
    laplacian = (
        padded_axial[..., 2:]
        + padded_axial[..., :-2]
        + padded_pitch[..., 2:, :]
        + padded_pitch[..., :-2, :]
        - 4.0 * field
    )
    return grad_axial, grad_pitch, laplacian


def modal_field(weights, mode_shape):
    return jnp.einsum("m,mpx->px", weights, mode_shape, precision=PRECISE)


def projection(mode_shape, field):
    return jnp.einsum("mpx,px->m", mode_shape, field, precision=PRECISE)


def add_field_one(rate, extra):
    return rate.at[1].add(extra)


def rate_field4(state, lower_ghost, upper_ghost, axial_jacobian, pitch_jacobian):
    zero_col = jnp.zeros_like(state[..., :1])
    padded_axial = jnp.concatenate([zero_col, state, zero_col], axis=-1)
    padded_pitch = pitch_pad(state, lower_ghost, upper_ghost)
    grad_axial = 0.5 * (padded_axial[:, :, 2:] - padded_axial[:, :, :-2])
    grad_pitch = 0.5 * (padded_pitch[:, 2:, :] - padded_pitch[:, :-2, :])
    laplacian = (
        padded_axial[4, :, 2:]
        + padded_axial[4, :, :-2]
        + padded_pitch[4, 2:, :]
        + padded_pitch[4, :-2, :]
        - 4.0 * state[4]
    )
    flux = jnp.einsum("j,jpx->px", axial_jacobian[4], grad_axial, precision=PRECISE)
    flux = flux + jnp.einsum("j,jpx->px", pitch_jacobian[4], grad_pitch, precision=PRECISE)
    return DIFFUSION * laplacian - flux


def pack(parts, width):
    flat = [jnp.moveaxis(part, -1, 0).reshape(width, -1) for part in parts]
    return jnp.concatenate(flat, axis=1)


def unpack(buffer, shapes):
    out, offset = [], 0
    for shape in shapes:
        count = math.prod(shape[:-1])
        out.append(buffer[offset : offset + count].reshape(shape))
        offset += count
    return out


LANES = 128


def lane_roll(x, shift):
    return pltpu.roll(x, shift % x.shape[-1], x.ndim - 1)


def row_roll(x, shift):
    return pltpu.roll(x, shift % x.shape[0], 0)


def kernel_rate(state, lower, upper, jac, push, inside, fields_out):
    ax, pt = jac
    rows = state[0].shape[0]
    row = lax.broadcasted_iota(jnp.int32, state[0].shape, 0)
    grads_a, grads_p, laps = [], [], []
    for j, s in enumerate(state):
        east = lane_roll(s, -1)
        west = lane_roll(s, 1)
        north = jnp.where(row == rows - 1, upper[j], row_roll(s, -1))
        south = jnp.where(row == 0, lower[j], row_roll(s, 1))
        grads_a.append(0.5 * (east - west))
        grads_p.append(0.5 * (north - south))
        laps.append(east + west + north + south - 4.0 * s)
    out = []
    for i in fields_out:
        r = DIFFUSION * laps[i]
        for j in range(len(state)):
            r = r - ax[i][j] * grads_a[j] - pt[i][j] * grads_p[j]
        if i == 1 and push is not None:
            r = r + push
        out.append(r * inside)
    return out


def read_jacobians(ax_ref, pt_ref, fields):
    ax = [[ax_ref[i, j] for j in range(fields)] for i in range(fields)]
    pt = [[pt_ref[i, j] for j in range(fields)] for i in range(fields)]
    return ax, pt


def lane_fold(x):
    x = jnp.sum(x, axis=0, keepdims=True)
    total = x[:, :LANES]
    for t in range(1, x.shape[1] // LANES):
        total = total + x[:, t * LANES : (t + 1) * LANES]
    return total


def pick_kernel(peers, lower_slot_ref, upper_slot_ref, upper_hist_ref, lower_hist_ref, up_ref, down_ref):
    fields, slots = upper_hist_ref.shape[0], upper_hist_ref.shape[1]
    position = lax.axis_index("blk")
    slot_next = lower_slot_ref[(position + 1) % peers]
    slot_prev = upper_slot_ref[(position + peers - 1) % peers]
    for s in range(up_ref.shape[0]):
        up_at = (slot_next + s) % slots
        down_at = (slot_prev + s) % slots
        for f in range(fields):
            up_ref[s, f : f + 1, :] = upper_hist_ref[f, pl.ds(up_at, 1), :]
            down_ref[s, f : f + 1, :] = lower_hist_ref[f, pl.ds(down_at, 1), :]


def widened(own, tile):
    return jnp.concatenate([own, tile], axis=-1)


def lane_masks(peers, shape, own_width):
    reach = 2 * STEP_COUNT
    me = lax.axis_index("mesh")
    lane = lax.broadcasted_iota(jnp.int32, shape, len(shape) - 1)
    width = shape[-1]
    right_ok = (lane >= own_width) & (lane < own_width + reach) & (me < peers - 1)
    left_ok = (lane >= width - reach) & (me > 0)
    owned = lane < own_width
    inside = owned | right_ok | left_ok
    return inside.astype(jnp.float32), owned.astype(jnp.float32)


def assemble(u_ref, ms_ref, glo_ref, gup_ref, halo_ref, fields, modes, pitch):
    u = []
    for j in range(fields):
        rows = slice(j * pitch, (j + 1) * pitch)
        u.append(widened(u_ref[j], halo_ref[rows, :]))
    ms = []
    for m in range(modes):
        rows = slice((fields + m) * pitch, (fields + m + 1) * pitch)
        ms.append(widened(ms_ref[m], halo_ref[rows, :]))
    base = (fields + modes) * pitch
    steps = glo_ref.shape[0]
    ghosts = []
    for side, ref in enumerate((glo_ref, gup_ref)):
        per_step = []
        for s in range(steps):
            start = base + (side * steps + s) * fields
            rows = slice(start, start + fields)
            block = widened(ref[s], halo_ref[rows, :])
            per_step.append([block[j : j + 1, :] for j in range(fields)])
        ghosts.append(per_step)
    return u, ms, ghosts[0], ghosts[1]


def first_kernel(peers, ax_ref, pt_ref, vel_ref, u_ref, ms_ref, glo_ref, gup_ref, halo_ref, a_ref, part_ref):
    h = TIME_STEP
    fields = u_ref.shape[0]
    modes = ms_ref.shape[0]
    pitch = u_ref.shape[1]
    jac = read_jacobians(ax_ref, pt_ref, fields)
    vel = [vel_ref[0, m] for m in range(modes)]
    u0, ms, gl, gu = assemble(u_ref, ms_ref, glo_ref, gup_ref, halo_ref, fields, modes, pitch)
    inside, owned = lane_masks(peers, u0[0].shape, u_ref.shape[-1])
    push = vel[0] * ms[0]
    for m in range(1, modes):
        push = push + vel[m] * ms[m]
    push = COUPLING * push
    gl1, gu1, gl2, gu2 = gl[0], gu[0], gl[1], gu[1]
    every = list(range(fields))
    k1 = kernel_rate(u0, gl1, gu1, jac, push, inside, every)
    mid = [u0[j] + h * k1[j] for j in every]
    k2 = kernel_rate(mid, gl1, gu1, jac, push, inside, every)
    a = [u0[j] + 0.5 * h * (k1[j] + k2[j]) for j in every]
    for j in every:
        a_ref[j] = a[j]
    (ra4,) = kernel_rate(a, gl2, gu2, jac, None, inside, [4])
    weighted = [ms[m] * owned for m in range(modes)]
    k = 0
    for field in (u0[4], mid[4], a[4], ra4):
        for m in range(modes):
            part_ref[k : k + 1, :] = lane_fold(weighted[m] * field)
            k += 1
    ax41, pt41 = jac[0][4][1], jac[1][4][1]
    rows = ms[0].shape[0]
    row = lax.broadcasted_iota(jnp.int32, ms[0].shape, 0)
    for n in range(modes):
        s = ms[n]
        ga = 0.5 * (lane_roll(s, -1) - lane_roll(s, 1))
        north = jnp.where(row == rows - 1, 0.0, row_roll(s, -1))
        south = jnp.where(row == 0, 0.0, row_roll(s, 1))
        gp = 0.5 * (north - south)
        t = -(ax41 * ga + pt41 * gp)
        for m in range(modes):
            part_ref[k + m * modes + n : k + m * modes + n + 1, :] = lane_fold(weighted[m] * t)


def modal_steps(force_scale, tot_ref, stiff_ref, disp_ref, vel_ref, modes):
    h = TIME_STEP
    t = [force_scale * tot_ref[k] for k in range(4 * modes + modes * modes)]
    force = [t[w * modes : (w + 1) * modes] for w in range(4)]
    couple = [t[4 * modes + m * modes : 4 * modes + (m + 1) * modes] for m in range(modes)]
    stiff = [stiff_ref[0, m] for m in range(modes)]
    disp0 = [disp_ref[0, m] for m in range(modes)]
    vel0 = [vel_ref[0, m] for m in range(modes)]

    def accel(f, q, v):
        return [f[m] - stiff[m] * q[m] - DAMPING * v[m] for m in range(modes)]

    def axpy(x, a, y):
        return [x[m] + a * y[m] for m in range(modes)]

    acc1 = accel(force[0], disp0, vel0)
    disp1m = axpy(disp0, h, vel0)
    vel1m = axpy(vel0, h, acc1)
    acc1m = accel(force[1], disp1m, vel1m)
    disp1 = [disp0[m] + 0.5 * h * (vel0[m] + vel1m[m]) for m in range(modes)]
    vel1 = [vel0[m] + 0.5 * h * (acc1[m] + acc1m[m]) for m in range(modes)]
    acc2 = accel(force[2], disp1, vel1)
    disp2m = axpy(disp1, h, vel1)
    vel2m = axpy(vel1, h, acc2)
    corr = 0.5 * h * h * COUPLING
    force2m = []
    for m in range(modes):
        coupled = couple[m][0] * acc1[0]
        for n in range(1, modes):
            coupled = coupled + couple[m][n] * acc1[n]
        force2m.append(force[2][m] + h * force[3][m] + h * corr * coupled)
    acc2m = accel(force2m, disp2m, vel2m)
    disp2 = [disp1[m] + 0.5 * h * (vel1[m] + vel2m[m]) for m in range(modes)]
    vel2 = [vel1[m] + 0.5 * h * (acc2[m] + acc2m[m]) for m in range(modes)]
    coef = [[corr * acc1[m] for m in range(modes)], vel1, vel2m]
    return coef, disp2, vel2


def second_kernel(
    peers,
    force_scale,
    tot_ref,
    stiff_ref,
    disp_ref,
    vel_ref,
    ax_ref,
    pt_ref,
    a_ref,
    u_ref,
    ms_ref,
    glo_ref,
    gup_ref,
    halo_ref,
    out_ref,
    disp_out_ref,
    vel_out_ref,
):
    h = TIME_STEP
    fields = a_ref.shape[0]
    modes = ms_ref.shape[0]
    pitch = u_ref.shape[1]
    jac = read_jacobians(ax_ref, pt_ref, fields)
    coef, disp2, vel2 = modal_steps(force_scale, tot_ref, stiff_ref, disp_ref, vel_ref, modes)
    for m in range(modes):
        disp_out_ref[0, m] = disp2[m]
        vel_out_ref[0, m] = vel2[m]
    _, ms, gl, gu = assemble(u_ref, ms_ref, glo_ref, gup_ref, halo_ref, fields, modes, pitch)
    inside, _ = lane_masks(peers, ms[0].shape, u_ref.shape[-1])

    def combine(weights):
        total = weights[0] * ms[0]
        for m in range(1, modes):
            total = total + weights[m] * ms[m]
        return total

    gl2, gu2 = gl[1], gu[1]
    every = list(range(fields))
    s1 = [a_ref[j] for j in every]
    s1[1] = s1[1] + combine(coef[0])
    k1 = kernel_rate(s1, gl2, gu2, jac, COUPLING * combine(coef[1]), inside, every)
    mid = [s1[j] + h * k1[j] for j in every]
    k2 = kernel_rate(mid, gl2, gu2, jac, COUPLING * combine(coef[2]), inside, every)
    width = out_ref.shape[-1]
    for j in every:
        s2 = s1[j] + 0.5 * h * (k1[j] + k2[j])
        out_ref[j] = s2[:, :width]


def vmem_spec():
    return pl.BlockSpec(memory_space=pltpu.VMEM)


def smem_spec():
    return pl.BlockSpec(memory_space=pltpu.SMEM)


def on_device(
    flow_field,
    lower_row_history,
    upper_row_history,
    lower_lag_slot,
    upper_lag_slot,
    axial_jacobian,
    pitch_jacobian,
    mode_shape,
    stiffness,
    displacement,
    velocity,
):
    h = TIME_STEP
    state0 = flow_field[0]
    fields, pitch_cells, axial_cells = state0.shape
    modes = mode_shape.shape[0]
    mesh_peers = lax.axis_size("mesh")
    me = lax.axis_index("mesh")
    force_scale = 1.0 / math.sqrt(pitch_cells * axial_cells * mesh_peers)
    passages = lax.axis_size("blk")
    position = lax.axis_index("blk")
    blade_stiffness = stiffness[0]
    disp0 = displacement[0]
    vel0 = velocity[0]

    row_shape = jax.ShapeDtypeStruct((STEP_COUNT,) + upper_row_history.shape[2:], state0.dtype)
    rows_up, rows_down = pl.pallas_call(
        functools.partial(pick_kernel, passages),
        out_shape=(row_shape, row_shape),
        in_specs=[smem_spec(), smem_spec(), vmem_spec(), vmem_spec()],
        out_specs=(vmem_spec(), vmem_spec()),
    )(
        lower_lag_slot,
        upper_lag_slot,
        jnp.transpose(upper_row_history[0], (1, 0, 2)),
        jnp.transpose(lower_row_history[0], (1, 0, 2)),
    )
    lower_ghosts = shifted(rows_up, "blk", 1)
    upper_ghosts = shifted(rows_down, "blk", -1)

    reach = 2 * STEP_COUNT
    own = [state0, mode_shape, lower_ghosts, upper_ghosts]
    shapes = [part.shape[:-1] + (reach,) for part in own]
    from_left = shifted(pack([part[..., -reach:] for part in own], reach).reshape(-1), "mesh", 1)
    from_right = shifted(pack([part[..., :reach] for part in own], reach).reshape(-1), "mesh", -1)
    from_left = from_left.reshape(reach, -1)
    from_right = from_right.reshape(reach, -1)
    from_left = jnp.where(me > 0, from_left, jnp.zeros_like(from_left))
    from_right = jnp.where(me < mesh_peers - 1, from_right, jnp.zeros_like(from_right))
    gap = jnp.zeros((from_left.shape[1], LANES - 2 * reach), from_left.dtype)
    halo_tile = jnp.concatenate([from_right.T, gap, from_left.T], axis=1)
    lanes_wide = axial_cells + LANES
    ins = (state0, mode_shape, lower_ghosts, upper_ghosts, halo_tile)

    base1, part_lanes = pl.pallas_call(
        functools.partial(first_kernel, mesh_peers),
        out_shape=(
            jax.ShapeDtypeStruct((fields, pitch_cells, lanes_wide), state0.dtype),
            jax.ShapeDtypeStruct((4 * modes + modes * modes, LANES), state0.dtype),
        ),
        in_specs=[smem_spec()] * 3 + [vmem_spec()] * 5,
        out_specs=(vmem_spec(), vmem_spec()),
    )(axial_jacobian, pitch_jacobian, velocity, *ins)

    totals = mesh_sum(jnp.sum(part_lanes, axis=1))

    small = jax.ShapeDtypeStruct(displacement.shape, displacement.dtype)
    state2, disp2, vel2 = pl.pallas_call(
        functools.partial(second_kernel, mesh_peers, force_scale),
        out_shape=(jax.ShapeDtypeStruct(state0.shape, state0.dtype), small, small),
        in_specs=[smem_spec()] * 6 + [vmem_spec()] * 6,
        out_specs=(vmem_spec(), smem_spec(), smem_spec()),
    )(totals, stiffness, displacement, velocity, axial_jacobian, pitch_jacobian, base1, *ins)
    return (state2[None], disp2, vel2)


def solution(mesh):
    return jax.shard_map(
        on_device,
        mesh=mesh,
        in_specs=(
            P("blk", None, None, "mesh"),
            P("blk", None, None, "mesh"),
            P("blk", None, None, "mesh"),
            P(),
            P(),
            P(),
            P(),
            P(None, None, "mesh"),
            P("blk", None),
            P("blk", None),
            P("blk", None),
        ),
        out_specs=(P("blk", None, None, "mesh"), P("blk", None), P("blk", None)),
        check_vma=False,
    )
```

```python
import functools
import math

import jax
import jax.numpy as jnp
from jax import lax
from jax.experimental import pallas as pl
from jax.experimental.pallas import tpu as pltpu
from jax.sharding import PartitionSpec as P

STEP_COUNT = 2


PRECISE = lax.Precision.HIGHEST
TIME_STEP = 0.4
DIFFUSION = 0.1
COUPLING = 0.3
DAMPING = 0.1


def shifted(value, axis, by):
    peers = lax.axis_size(axis)
    return lax.ppermute(value, axis, [(i, (i + by) % peers) for i in range(peers)])


def halo(value):
    peers = lax.axis_size("mesh")
    me = lax.axis_index("mesh")
    before = shifted(value[..., -1:], "mesh", 1)
    after = shifted(value[..., :1], "mesh", -1)
    before = jnp.where(me > 0, before, jnp.zeros_like(before))
    after = jnp.where(me < peers - 1, after, jnp.zeros_like(after))
    return before, after


def mesh_sum(value):
    peers = lax.axis_size("mesh")
    if peers & (peers - 1):
        return lax.psum(value, "mesh")
    step = 1
    while step < peers:
        value = value + lax.ppermute(value, "mesh", [(i, i ^ step) for i in range(peers)])
        step *= 2
    return value


def pick_rows(table, index, count):
    slots = table.shape[0]
    slot = jnp.arange(slots, dtype=jnp.int32).reshape((slots,) + (1,) * (table.ndim - 1))
    rows = []
    for s in range(count):
        hit = slot == (index + s) % slots
        rows.append(jnp.sum(jnp.where(hit, table, jnp.zeros_like(table)), axis=0))
    return jnp.stack(rows)


def pick_entry(values, index):
    hit = jnp.arange(values.shape[0], dtype=jnp.int32) == index
    return jnp.sum(jnp.where(hit, values, jnp.zeros_like(values)))


def axial_pad(value, before, after):
    return jnp.concatenate([before, value, after], axis=-1)


def pitch_pad(value, lower, upper):
    return jnp.concatenate([lower[:, None, :], value, upper[:, None, :]], axis=1)


def flow_rate(state, before, after, lower_ghost, upper_ghost, axial_jacobian, pitch_jacobian):
    padded_axial = axial_pad(state, before, after)
    padded_pitch = pitch_pad(state, lower_ghost, upper_ghost)
    grad_axial = 0.5 * (padded_axial[:, :, 2:] - padded_axial[:, :, :-2])
    grad_pitch = 0.5 * (padded_pitch[:, 2:, :] - padded_pitch[:, :-2, :])
    laplacian = (
        padded_axial[:, :, 2:]
        + padded_axial[:, :, :-2]
        + padded_pitch[:, 2:, :]
        + padded_pitch[:, :-2, :]
        - 4.0 * state
    )
    flux = jnp.einsum("ij,jpx->ipx", axial_jacobian, grad_axial, precision=PRECISE)
    flux = flux + jnp.einsum("ij,jpx->ipx", pitch_jacobian, grad_pitch, precision=PRECISE)
    return DIFFUSION * laplacian - flux


def single_field_grads(field, before, after):
    padded_axial = jnp.concatenate([before, field, after], axis=-1)
    zero_row = jnp.zeros_like(field[..., :1, :])
    padded_pitch = jnp.concatenate([zero_row, field, zero_row], axis=-2)
    grad_axial = 0.5 * (padded_axial[..., 2:] - padded_axial[..., :-2])
    grad_pitch = 0.5 * (padded_pitch[..., 2:, :] - padded_pitch[..., :-2, :])
    laplacian = (
        padded_axial[..., 2:]
        + padded_axial[..., :-2]
        + padded_pitch[..., 2:, :]
        + padded_pitch[..., :-2, :]
        - 4.0 * field
    )
    return grad_axial, grad_pitch, laplacian


def modal_field(weights, mode_shape):
    return jnp.einsum("m,mpx->px", weights, mode_shape, precision=PRECISE)


def projection(mode_shape, field):
    return jnp.einsum("mpx,px->m", mode_shape, field, precision=PRECISE)


def add_field_one(rate, extra):
    return rate.at[1].add(extra)


def rate_field4(state, lower_ghost, upper_ghost, axial_jacobian, pitch_jacobian):
    zero_col = jnp.zeros_like(state[..., :1])
    padded_axial = jnp.concatenate([zero_col, state, zero_col], axis=-1)
    padded_pitch = pitch_pad(state, lower_ghost, upper_ghost)
    grad_axial = 0.5 * (padded_axial[:, :, 2:] - padded_axial[:, :, :-2])
    grad_pitch = 0.5 * (padded_pitch[:, 2:, :] - padded_pitch[:, :-2, :])
    laplacian = (
        padded_axial[4, :, 2:]
        + padded_axial[4, :, :-2]
        + padded_pitch[4, 2:, :]
        + padded_pitch[4, :-2, :]
        - 4.0 * state[4]
    )
    flux = jnp.einsum("j,jpx->px", axial_jacobian[4], grad_axial, precision=PRECISE)
    flux = flux + jnp.einsum("j,jpx->px", pitch_jacobian[4], grad_pitch, precision=PRECISE)
    return DIFFUSION * laplacian - flux


def pack(parts, width):
    flat = [jnp.moveaxis(part, -1, 0).reshape(width, -1) for part in parts]
    return jnp.concatenate(flat, axis=1)


def unpack(buffer, shapes):
    out, offset = [], 0
    for shape in shapes:
        count = math.prod(shape[:-1])
        out.append(buffer[offset : offset + count].reshape(shape))
        offset += count
    return out


LANES = 128


def lane_roll(x, shift):
    return pltpu.roll(x, shift % x.shape[-1], x.ndim - 1)


def row_roll(x, shift):
    return pltpu.roll(x, shift % x.shape[0], 0)


def kernel_rate(state, lower, upper, jac, push, inside, fields_out):
    ax, pt = jac
    rows = state[0].shape[0]
    row = lax.broadcasted_iota(jnp.int32, state[0].shape, 0)
    grads_a, grads_p, laps = [], [], []
    for j, s in enumerate(state):
        east = lane_roll(s, -1)
        west = lane_roll(s, 1)
        north = jnp.where(row == rows - 1, upper[j], row_roll(s, -1))
        south = jnp.where(row == 0, lower[j], row_roll(s, 1))
        grads_a.append(0.5 * (east - west))
        grads_p.append(0.5 * (north - south))
        laps.append(east + west + north + south - 4.0 * s)
    out = []
    for i in fields_out:
        r = DIFFUSION * laps[i]
        for j in range(len(state)):
            r = r - ax[i][j] * grads_a[j] - pt[i][j] * grads_p[j]
        if i == 1 and push is not None:
            r = r + push
        out.append(r * inside)
    return out


def read_jacobians(ax_ref, pt_ref, fields):
    ax = [[ax_ref[i, j] for j in range(fields)] for i in range(fields)]
    pt = [[pt_ref[i, j] for j in range(fields)] for i in range(fields)]
    return ax, pt


def lane_fold(x):
    x = jnp.sum(x, axis=0, keepdims=True)
    total = x[:, :LANES]
    for t in range(1, x.shape[1] // LANES):
        total = total + x[:, t * LANES : (t + 1) * LANES]
    return total


def pick_kernel(peers, lower_slot_ref, upper_slot_ref, upper_hist_ref, lower_hist_ref, up_ref, down_ref):
    fields, slots = upper_hist_ref.shape[0], upper_hist_ref.shape[1]
    position = lax.axis_index("blk")
    slot_next = lower_slot_ref[(position + 1) % peers]
    slot_prev = upper_slot_ref[(position + peers - 1) % peers]
    for s in range(up_ref.shape[0]):
        up_at = (slot_next + s) % slots
        down_at = (slot_prev + s) % slots
        for f in range(fields):
            up_ref[s, f : f + 1, :] = upper_hist_ref[f, pl.ds(up_at, 1), :]
            down_ref[s, f : f + 1, :] = lower_hist_ref[f, pl.ds(down_at, 1), :]


def widened(own, tile):
    return jnp.concatenate([own, tile], axis=-1)


def lane_masks(peers, shape, own_width):
    reach = 2 * STEP_COUNT
    me = lax.axis_index("mesh")
    lane = lax.broadcasted_iota(jnp.int32, shape, len(shape) - 1)
    width = shape[-1]
    right_ok = (lane >= own_width) & (lane < own_width + reach) & (me < peers - 1)
    left_ok = (lane >= width - reach) & (me > 0)
    owned = lane < own_width
    inside = owned | right_ok | left_ok
    return inside.astype(jnp.float32), owned.astype(jnp.float32)


def assemble(u_ref, ms_ref, glo_ref, gup_ref, halo_ref, fields, modes, pitch):
    u = []
    for j in range(fields):
        rows = slice(j * pitch, (j + 1) * pitch)
        u.append(widened(u_ref[j], halo_ref[rows, :]))
    ms = []
    for m in range(modes):
        rows = slice((fields + m) * pitch, (fields + m + 1) * pitch)
        ms.append(widened(ms_ref[m], halo_ref[rows, :]))
    base = (fields + modes) * pitch
    steps = glo_ref.shape[0]
    ghosts = []
    for side, ref in enumerate((glo_ref, gup_ref)):
        per_step = []
        for s in range(steps):
            start = base + (side * steps + s) * fields
            rows = slice(start, start + fields)
            block = widened(ref[s], halo_ref[rows, :])
            per_step.append([block[j : j + 1, :] for j in range(fields)])
        ghosts.append(per_step)
    return u, ms, ghosts[0], ghosts[1]


def first_kernel(peers, ax_ref, pt_ref, vel_ref, u_ref, ms_ref, glo_ref, gup_ref, halo_ref, a_ref, part_ref):
    h = TIME_STEP
    fields = u_ref.shape[0]
    modes = ms_ref.shape[0]
    pitch = u_ref.shape[1]
    jac = read_jacobians(ax_ref, pt_ref, fields)
    vel = [vel_ref[0, m] for m in range(modes)]
    u0, ms, gl, gu = assemble(u_ref, ms_ref, glo_ref, gup_ref, halo_ref, fields, modes, pitch)
    inside, owned = lane_masks(peers, u0[0].shape, u_ref.shape[-1])
    push = vel[0] * ms[0]
    for m in range(1, modes):
        push = push + vel[m] * ms[m]
    push = COUPLING * push
    gl1, gu1, gl2, gu2 = gl[0], gu[0], gl[1], gu[1]
    every = list(range(fields))
    k1 = kernel_rate(u0, gl1, gu1, jac, push, inside, every)
    mid = [u0[j] + h * k1[j] for j in every]
    k2 = kernel_rate(mid, gl1, gu1, jac, push, inside, every)
    a = [u0[j] + 0.5 * h * (k1[j] + k2[j]) for j in every]
    for j in every:
        a_ref[j] = a[j]
    (ra4,) = kernel_rate(a, gl2, gu2, jac, None, inside, [4])
    weighted = [ms[m] * owned for m in range(modes)]
    k = 0
    for field in (u0[4], mid[4], a[4], ra4):
        for m in range(modes):
            part_ref[k : k + 1, :] = lane_fold(weighted[m] * field)
            k += 1
    ax41, pt41 = jac[0][4][1], jac[1][4][1]
    rows = ms[0].shape[0]
    row = lax.broadcasted_iota(jnp.int32, ms[0].shape, 0)
    for n in range(modes):
        s = ms[n]
        ga = 0.5 * (lane_roll(s, -1) - lane_roll(s, 1))
        north = jnp.where(row == rows - 1, 0.0, row_roll(s, -1))
        south = jnp.where(row == 0, 0.0, row_roll(s, 1))
        gp = 0.5 * (north - south)
        t = -(ax41 * ga + pt41 * gp)
        for m in range(modes):
            part_ref[k + m * modes + n : k + m * modes + n + 1, :] = lane_fold(weighted[m] * t)


def modal_steps(force_scale, tot_ref, stiff_ref, disp_ref, vel_ref, modes):
    h = TIME_STEP
    t = [force_scale * tot_ref[k] for k in range(4 * modes + modes * modes)]
    force = [t[w * modes : (w + 1) * modes] for w in range(4)]
    couple = [t[4 * modes + m * modes : 4 * modes + (m + 1) * modes] for m in range(modes)]
    stiff = [stiff_ref[0, m] for m in range(modes)]
    disp0 = [disp_ref[0, m] for m in range(modes)]
    vel0 = [vel_ref[0, m] for m in range(modes)]

    def accel(f, q, v):
        return [f[m] - stiff[m] * q[m] - DAMPING * v[m] for m in range(modes)]

    def axpy(x, a, y):
        return [x[m] + a * y[m] for m in range(modes)]

    acc1 = accel(force[0], disp0, vel0)
    disp1m = axpy(disp0, h, vel0)
    vel1m = axpy(vel0, h, acc1)
    acc1m = accel(force[1], disp1m, vel1m)
    disp1 = [disp0[m] + 0.5 * h * (vel0[m] + vel1m[m]) for m in range(modes)]
    vel1 = [vel0[m] + 0.5 * h * (acc1[m] + acc1m[m]) for m in range(modes)]
    acc2 = accel(force[2], disp1, vel1)
    disp2m = axpy(disp1, h, vel1)
    vel2m = axpy(vel1, h, acc2)
    corr = 0.5 * h * h * COUPLING
    force2m = []
    for m in range(modes):
        coupled = couple[m][0] * acc1[0]
        for n in range(1, modes):
            coupled = coupled + couple[m][n] * acc1[n]
        force2m.append(force[2][m] + h * force[3][m] + h * corr * coupled)
    acc2m = accel(force2m, disp2m, vel2m)
    disp2 = [disp1[m] + 0.5 * h * (vel1[m] + vel2m[m]) for m in range(modes)]
    vel2 = [vel1[m] + 0.5 * h * (acc2[m] + acc2m[m]) for m in range(modes)]
    coef = [[corr * acc1[m] for m in range(modes)], vel1, vel2m]
    return coef, disp2, vel2


def step2_rate_kernel(peers, ax_ref, pt_ref, a_ref, u_ref, ms_ref, glo_ref, gup_ref, halo_ref, ra_ref):
    fields = a_ref.shape[0]
    modes = ms_ref.shape[0]
    pitch = u_ref.shape[1]
    jac = read_jacobians(ax_ref, pt_ref, fields)
    _, ms, gl, gu = assemble(u_ref, ms_ref, glo_ref, gup_ref, halo_ref, fields, modes, pitch)
    inside, _ = lane_masks(peers, ms[0].shape, u_ref.shape[-1])
    every = list(range(fields))
    a = [a_ref[j] for j in every]
    ra = kernel_rate(a, gl[1], gu[1], jac, None, inside, every)
    for j in every:
        ra_ref[j] = ra[j]


def second_kernel(
    peers,
    force_scale,
    tot_ref,
    stiff_ref,
    disp_ref,
    vel_ref,
    ax_ref,
    pt_ref,
    a_ref,
    ra_ref,
    u_ref,
    ms_ref,
    glo_ref,
    gup_ref,
    halo_ref,
    out_ref,
    disp_out_ref,
    vel_out_ref,
):
    h = TIME_STEP
    fields = a_ref.shape[0]
    modes = ms_ref.shape[0]
    pitch = u_ref.shape[1]
    jac = read_jacobians(ax_ref, pt_ref, fields)
    coef, disp2, vel2 = modal_steps(force_scale, tot_ref, stiff_ref, disp_ref, vel_ref, modes)
    for m in range(modes):
        disp_out_ref[0, m] = disp2[m]
        vel_out_ref[0, m] = vel2[m]
    _, ms, gl, gu = assemble(u_ref, ms_ref, glo_ref, gup_ref, halo_ref, fields, modes, pitch)
    inside, _ = lane_masks(peers, ms[0].shape, u_ref.shape[-1])

    def combine(weights):
        total = weights[0] * ms[0]
        for m in range(1, modes):
            total = total + weights[m] * ms[m]
        return total

    gl2, gu2 = gl[1], gu[1]
    every = list(range(fields))
    s1 = [a_ref[j] for j in every]
    correction = combine(coef[0])
    s1[1] = s1[1] + correction
    rows = correction.shape[0]
    row = lax.broadcasted_iota(jnp.int32, correction.shape, 0)
    east, west = lane_roll(correction, -1), lane_roll(correction, 1)
    north = jnp.where(row == rows - 1, 0.0, row_roll(correction, -1))
    south = jnp.where(row == 0, 0.0, row_roll(correction, 1))
    ga = 0.5 * (east - west)
    gp = 0.5 * (north - south)
    lap = east + west + north + south - 4.0 * correction
    ax, pt = jac
    push1 = COUPLING * combine(coef[1])
    k1 = []
    for i in every:
        r = -ax[i][1] * ga - pt[i][1] * gp
        if i == 1:
            r = r + DIFFUSION * lap + push1
        k1.append(ra_ref[i] + r * inside)
    mid = [s1[j] + h * k1[j] for j in every]
    k2 = kernel_rate(mid, gl2, gu2, jac, COUPLING * combine(coef[2]), inside, every)
    width = out_ref.shape[-1]
    for j in every:
        s2 = s1[j] + 0.5 * h * (k1[j] + k2[j])
        out_ref[j] = s2[:, :width]


def vmem_spec():
    return pl.BlockSpec(memory_space=pltpu.VMEM)


def smem_spec():
    return pl.BlockSpec(memory_space=pltpu.SMEM)


def on_device(
    flow_field,
    lower_row_history,
    upper_row_history,
    lower_lag_slot,
    upper_lag_slot,
    axial_jacobian,
    pitch_jacobian,
    mode_shape,
    stiffness,
    displacement,
    velocity,
):
    h = TIME_STEP
    state0 = flow_field[0]
    fields, pitch_cells, axial_cells = state0.shape
    modes = mode_shape.shape[0]
    mesh_peers = lax.axis_size("mesh")
    me = lax.axis_index("mesh")
    force_scale = 1.0 / math.sqrt(pitch_cells * axial_cells * mesh_peers)
    passages = lax.axis_size("blk")
    position = lax.axis_index("blk")
    blade_stiffness = stiffness[0]
    disp0 = displacement[0]
    vel0 = velocity[0]

    row_shape = jax.ShapeDtypeStruct((STEP_COUNT,) + upper_row_history.shape[2:], state0.dtype)
    rows_up, rows_down = pl.pallas_call(
        functools.partial(pick_kernel, passages),
        out_shape=(row_shape, row_shape),
        in_specs=[smem_spec(), smem_spec(), vmem_spec(), vmem_spec()],
        out_specs=(vmem_spec(), vmem_spec()),
    )(
        lower_lag_slot,
        upper_lag_slot,
        jnp.transpose(upper_row_history[0], (1, 0, 2)),
        jnp.transpose(lower_row_history[0], (1, 0, 2)),
    )
    lower_ghosts = shifted(rows_up, "blk", 1)
    upper_ghosts = shifted(rows_down, "blk", -1)

    reach = 2 * STEP_COUNT
    own = [state0, mode_shape, lower_ghosts, upper_ghosts]
    shapes = [part.shape[:-1] + (reach,) for part in own]
    from_left = shifted(pack([part[..., -reach:] for part in own], reach).reshape(-1), "mesh", 1)
    from_right = shifted(pack([part[..., :reach] for part in own], reach).reshape(-1), "mesh", -1)
    from_left = from_left.reshape(reach, -1)
    from_right = from_right.reshape(reach, -1)
    from_left = jnp.where(me > 0, from_left, jnp.zeros_like(from_left))
    from_right = jnp.where(me < mesh_peers - 1, from_right, jnp.zeros_like(from_right))
    gap = jnp.zeros((from_left.shape[1], LANES - 2 * reach), from_left.dtype)
    halo_tile = jnp.concatenate([from_right.T, gap, from_left.T], axis=1)
    lanes_wide = axial_cells + LANES
    ins = (state0, mode_shape, lower_ghosts, upper_ghosts, halo_tile)

    base1, part_lanes = pl.pallas_call(
        functools.partial(first_kernel, mesh_peers),
        out_shape=(
            jax.ShapeDtypeStruct((fields, pitch_cells, lanes_wide), state0.dtype),
            jax.ShapeDtypeStruct((4 * modes + modes * modes, LANES), state0.dtype),
        ),
        in_specs=[smem_spec()] * 3 + [vmem_spec()] * 5,
        out_specs=(vmem_spec(), vmem_spec()),
    )(axial_jacobian, pitch_jacobian, velocity, *ins)

    totals = mesh_sum(jnp.sum(part_lanes, axis=1))

    rate_a = pl.pallas_call(
        functools.partial(step2_rate_kernel, mesh_peers),
        out_shape=jax.ShapeDtypeStruct(base1.shape, base1.dtype),
        in_specs=[smem_spec()] * 2 + [vmem_spec()] * 6,
        out_specs=vmem_spec(),
    )(axial_jacobian, pitch_jacobian, base1, *ins)

    small = jax.ShapeDtypeStruct(displacement.shape, displacement.dtype)
    state2, disp2, vel2 = pl.pallas_call(
        functools.partial(second_kernel, mesh_peers, force_scale),
        out_shape=(jax.ShapeDtypeStruct(state0.shape, state0.dtype), small, small),
        in_specs=[smem_spec()] * 6 + [vmem_spec()] * 7,
        out_specs=(vmem_spec(), smem_spec(), smem_spec()),
    )(totals, stiffness, displacement, velocity, axial_jacobian, pitch_jacobian, base1, rate_a, *ins)
    return (state2[None], disp2, vel2)


def solution(mesh):
    return jax.shard_map(
        on_device,
        mesh=mesh,
        in_specs=(
            P("blk", None, None, "mesh"),
            P("blk", None, None, "mesh"),
            P("blk", None, None, "mesh"),
            P(),
            P(),
            P(),
            P(),
            P(None, None, "mesh"),
            P("blk", None),
            P("blk", None),
            P("blk", None),
        ),
        out_specs=(P("blk", None, None, "mesh"), P("blk", None), P("blk", None)),
        check_vma=False,
    )
```

```python
import functools
import math

import jax
import jax.numpy as jnp
from jax import lax
from jax.experimental import pallas as pl
from jax.experimental.pallas import tpu as pltpu
from jax.sharding import PartitionSpec as P

STEP_COUNT = 2


PRECISE = lax.Precision.HIGHEST
TIME_STEP = 0.4
DIFFUSION = 0.1
COUPLING = 0.3
DAMPING = 0.1


def shifted(value, axis, by):
    peers = lax.axis_size(axis)
    return lax.ppermute(value, axis, [(i, (i + by) % peers) for i in range(peers)])


def halo(value):
    peers = lax.axis_size("mesh")
    me = lax.axis_index("mesh")
    before = shifted(value[..., -1:], "mesh", 1)
    after = shifted(value[..., :1], "mesh", -1)
    before = jnp.where(me > 0, before, jnp.zeros_like(before))
    after = jnp.where(me < peers - 1, after, jnp.zeros_like(after))
    return before, after


def mesh_sum(value):
    peers = lax.axis_size("mesh")
    if peers & (peers - 1):
        return lax.psum(value, "mesh")
    step = 1
    while step < peers:
        value = value + lax.ppermute(value, "mesh", [(i, i ^ step) for i in range(peers)])
        step *= 2
    return value


def pick_rows(table, index, count):
    slots = table.shape[0]
    slot = jnp.arange(slots, dtype=jnp.int32).reshape((slots,) + (1,) * (table.ndim - 1))
    rows = []
    for s in range(count):
        hit = slot == (index + s) % slots
        rows.append(jnp.sum(jnp.where(hit, table, jnp.zeros_like(table)), axis=0))
    return jnp.stack(rows)


def pick_entry(values, index):
    hit = jnp.arange(values.shape[0], dtype=jnp.int32) == index
    return jnp.sum(jnp.where(hit, values, jnp.zeros_like(values)))


def axial_pad(value, before, after):
    return jnp.concatenate([before, value, after], axis=-1)


def pitch_pad(value, lower, upper):
    return jnp.concatenate([lower[:, None, :], value, upper[:, None, :]], axis=1)


def flow_rate(state, before, after, lower_ghost, upper_ghost, axial_jacobian, pitch_jacobian):
    padded_axial = axial_pad(state, before, after)
    padded_pitch = pitch_pad(state, lower_ghost, upper_ghost)
    grad_axial = 0.5 * (padded_axial[:, :, 2:] - padded_axial[:, :, :-2])
    grad_pitch = 0.5 * (padded_pitch[:, 2:, :] - padded_pitch[:, :-2, :])
    laplacian = (
        padded_axial[:, :, 2:]
        + padded_axial[:, :, :-2]
        + padded_pitch[:, 2:, :]
        + padded_pitch[:, :-2, :]
        - 4.0 * state
    )
    flux = jnp.einsum("ij,jpx->ipx", axial_jacobian, grad_axial, precision=PRECISE)
    flux = flux + jnp.einsum("ij,jpx->ipx", pitch_jacobian, grad_pitch, precision=PRECISE)
    return DIFFUSION * laplacian - flux


def single_field_grads(field, before, after):
    padded_axial = jnp.concatenate([before, field, after], axis=-1)
    zero_row = jnp.zeros_like(field[..., :1, :])
    padded_pitch = jnp.concatenate([zero_row, field, zero_row], axis=-2)
    grad_axial = 0.5 * (padded_axial[..., 2:] - padded_axial[..., :-2])
    grad_pitch = 0.5 * (padded_pitch[..., 2:, :] - padded_pitch[..., :-2, :])
    laplacian = (
        padded_axial[..., 2:]
        + padded_axial[..., :-2]
        + padded_pitch[..., 2:, :]
        + padded_pitch[..., :-2, :]
        - 4.0 * field
    )
    return grad_axial, grad_pitch, laplacian


def modal_field(weights, mode_shape):
    return jnp.einsum("m,mpx->px", weights, mode_shape, precision=PRECISE)


def projection(mode_shape, field):
    return jnp.einsum("mpx,px->m", mode_shape, field, precision=PRECISE)


def add_field_one(rate, extra):
    return rate.at[1].add(extra)


def rate_field4(state, lower_ghost, upper_ghost, axial_jacobian, pitch_jacobian):
    zero_col = jnp.zeros_like(state[..., :1])
    padded_axial = jnp.concatenate([zero_col, state, zero_col], axis=-1)
    padded_pitch = pitch_pad(state, lower_ghost, upper_ghost)
    grad_axial = 0.5 * (padded_axial[:, :, 2:] - padded_axial[:, :, :-2])
    grad_pitch = 0.5 * (padded_pitch[:, 2:, :] - padded_pitch[:, :-2, :])
    laplacian = (
        padded_axial[4, :, 2:]
        + padded_axial[4, :, :-2]
        + padded_pitch[4, 2:, :]
        + padded_pitch[4, :-2, :]
        - 4.0 * state[4]
    )
    flux = jnp.einsum("j,jpx->px", axial_jacobian[4], grad_axial, precision=PRECISE)
    flux = flux + jnp.einsum("j,jpx->px", pitch_jacobian[4], grad_pitch, precision=PRECISE)
    return DIFFUSION * laplacian - flux


def pack(parts, width):
    flat = [jnp.moveaxis(part, -1, 0).reshape(width, -1) for part in parts]
    return jnp.concatenate(flat, axis=1)


def unpack(buffer, shapes):
    out, offset = [], 0
    for shape in shapes:
        count = math.prod(shape[:-1])
        out.append(buffer[offset : offset + count].reshape(shape))
        offset += count
    return out


LANES = 128


def lane_roll(x, shift):
    return pltpu.roll(x, shift % x.shape[-1], x.ndim - 1)


def row_roll(x, shift):
    return pltpu.roll(x, shift % x.shape[0], 0)


def pitch_neighbours(s, lower, upper):
    rows = s.shape[0]
    tile = 8
    edge = lax.broadcasted_iota(jnp.int32, (tile,) + s.shape[1:], 0)
    north = row_roll(s, -1)
    south = row_roll(s, 1)
    north = jnp.concatenate(
        [north[: rows - tile], jnp.where(edge == tile - 1, upper, north[rows - tile :])], axis=0
    )
    south = jnp.concatenate([jnp.where(edge == 0, lower, south[:tile]), south[tile:]], axis=0)
    return north, south


def masked(r, inside):
    cut = r.shape[-1] - LANES
    return jnp.concatenate([r[:, :cut], r[:, cut:] * inside[:, cut:]], axis=1)


def kernel_rate(state, lower, upper, jac, push, inside, fields_out):
    ax, pt = jac
    diffs_a, diffs_p, laps = [], [], []
    for j, s in enumerate(state):
        east = lane_roll(s, -1)
        west = lane_roll(s, 1)
        north, south = pitch_neighbours(s, lower[j], upper[j])
        diffs_a.append(east - west)
        diffs_p.append(north - south)
        laps.append((east + west) + (north + south) - 4.0 * s)
    out = []
    for i in fields_out:
        r = DIFFUSION * laps[i]
        for j in range(len(state)):
            r = r - (0.5 * ax[i][j]) * diffs_a[j] - (0.5 * pt[i][j]) * diffs_p[j]
        if i == 1 and push is not None:
            r = r + push
        out.append(masked(r, inside))
    return out


def read_jacobians(ax_ref, pt_ref, fields):
    ax = [[ax_ref[i, j] for j in range(fields)] for i in range(fields)]
    pt = [[pt_ref[i, j] for j in range(fields)] for i in range(fields)]
    return ax, pt


def lane_fold(x):
    x = jnp.sum(x, axis=0, keepdims=True)
    total = x[:, :LANES]
    for t in range(1, x.shape[1] // LANES):
        total = total + x[:, t * LANES : (t + 1) * LANES]
    return total


def pick_kernel(peers, lower_slot_ref, upper_slot_ref, upper_hist_ref, lower_hist_ref, up_ref, down_ref):
    fields, slots = upper_hist_ref.shape[0], upper_hist_ref.shape[1]
    position = lax.axis_index("blk")
    slot_next = lower_slot_ref[(position + 1) % peers]
    slot_prev = upper_slot_ref[(position + peers - 1) % peers]
    for s in range(up_ref.shape[0]):
        up_at = (slot_next + s) % slots
        down_at = (slot_prev + s) % slots
        for f in range(fields):
            up_ref[s, f : f + 1, :] = upper_hist_ref[f, pl.ds(up_at, 1), :]
            down_ref[s, f : f + 1, :] = lower_hist_ref[f, pl.ds(down_at, 1), :]


def widened(own, tile):
    return jnp.concatenate([own, tile], axis=-1)


def lane_masks(peers, shape, own_width):
    reach = 2 * STEP_COUNT
    me = lax.axis_index("mesh")
    lane = lax.broadcasted_iota(jnp.int32, shape, len(shape) - 1)
    width = shape[-1]
    right_ok = (lane >= own_width) & (lane < own_width + reach) & (me < peers - 1)
    left_ok = (lane >= width - reach) & (me > 0)
    owned = lane < own_width
    inside = owned | right_ok | left_ok
    return inside.astype(jnp.float32), owned.astype(jnp.float32)


def assemble(u_ref, ms_ref, glo_ref, gup_ref, halo_ref, fields, modes, pitch):
    u = []
    for j in range(fields if u_ref is not None else 0):
        rows = slice(j * pitch, (j + 1) * pitch)
        u.append(widened(u_ref[j], halo_ref[rows, :]))
    ms = []
    for m in range(modes):
        rows = slice((fields + m) * pitch, (fields + m + 1) * pitch)
        ms.append(widened(ms_ref[m], halo_ref[rows, :]))
    base = (fields + modes) * pitch
    steps = glo_ref.shape[0]
    ghosts = []
    for side, ref in enumerate((glo_ref, gup_ref)):
        per_step = []
        for s in range(steps):
            start = base + (side * steps + s) * fields
            rows = slice(start, start + fields)
            block = widened(ref[s], halo_ref[rows, :])
            per_step.append([block[j : j + 1, :] for j in range(fields)])
        ghosts.append(per_step)
    return u, ms, ghosts[0], ghosts[1]


def first_kernel(peers, ax_ref, pt_ref, vel_ref, u_ref, ms_ref, glo_ref, gup_ref, halo_ref, a_ref, part_ref):
    h = TIME_STEP
    fields = u_ref.shape[0]
    modes = ms_ref.shape[0]
    pitch = u_ref.shape[1]
    jac = read_jacobians(ax_ref, pt_ref, fields)
    vel = [vel_ref[0, m] for m in range(modes)]
    u0, ms, gl, gu = assemble(u_ref, ms_ref, glo_ref, gup_ref, halo_ref, fields, modes, pitch)
    inside, owned = lane_masks(peers, u0[0].shape, u_ref.shape[-1])
    push = vel[0] * ms[0]
    for m in range(1, modes):
        push = push + vel[m] * ms[m]
    push = COUPLING * push
    gl1, gu1, gl2, gu2 = gl[0], gu[0], gl[1], gu[1]
    every = list(range(fields))
    k1 = kernel_rate(u0, gl1, gu1, jac, push, inside, every)
    mid = [u0[j] + h * k1[j] for j in every]
    k2 = kernel_rate(mid, gl1, gu1, jac, push, inside, every)
    a = [u0[j] + 0.5 * h * (k1[j] + k2[j]) for j in every]
    for j in every:
        a_ref[j] = a[j]
    (ra4,) = kernel_rate(a, gl2, gu2, jac, None, inside, [4])
    weighted = [ms[m] * owned for m in range(modes)]
    k = 0
    for field in (u0[4], mid[4], a[4], ra4):
        for m in range(modes):
            part_ref[k : k + 1, :] = lane_fold(weighted[m] * field)
            k += 1
    ax41, pt41 = jac[0][4][1], jac[1][4][1]
    rows = ms[0].shape[0]
    row = lax.broadcasted_iota(jnp.int32, ms[0].shape, 0)
    for n in range(modes):
        s = ms[n]
        ga = 0.5 * (lane_roll(s, -1) - lane_roll(s, 1))
        north = jnp.where(row == rows - 1, 0.0, row_roll(s, -1))
        south = jnp.where(row == 0, 0.0, row_roll(s, 1))
        gp = 0.5 * (north - south)
        t = -(ax41 * ga + pt41 * gp)
        for m in range(modes):
            part_ref[k + m * modes + n : k + m * modes + n + 1, :] = lane_fold(weighted[m] * t)


def modal_steps(force_scale, tot_ref, stiff_ref, disp_ref, vel_ref, modes):
    h = TIME_STEP
    t = [force_scale * tot_ref[k] for k in range(4 * modes + modes * modes)]
    force = [t[w * modes : (w + 1) * modes] for w in range(4)]
    couple = [t[4 * modes + m * modes : 4 * modes + (m + 1) * modes] for m in range(modes)]
    stiff = [stiff_ref[0, m] for m in range(modes)]
    disp0 = [disp_ref[0, m] for m in range(modes)]
    vel0 = [vel_ref[0, m] for m in range(modes)]

    def accel(f, q, v):
        return [f[m] - stiff[m] * q[m] - DAMPING * v[m] for m in range(modes)]

    def axpy(x, a, y):
        return [x[m] + a * y[m] for m in range(modes)]

    acc1 = accel(force[0], disp0, vel0)
    disp1m = axpy(disp0, h, vel0)
    vel1m = axpy(vel0, h, acc1)
    acc1m = accel(force[1], disp1m, vel1m)
    disp1 = [disp0[m] + 0.5 * h * (vel0[m] + vel1m[m]) for m in range(modes)]
    vel1 = [vel0[m] + 0.5 * h * (acc1[m] + acc1m[m]) for m in range(modes)]
    acc2 = accel(force[2], disp1, vel1)
    disp2m = axpy(disp1, h, vel1)
    vel2m = axpy(vel1, h, acc2)
    corr = 0.5 * h * h * COUPLING
    force2m = []
    for m in range(modes):
        coupled = couple[m][0] * acc1[0]
        for n in range(1, modes):
            coupled = coupled + couple[m][n] * acc1[n]
        force2m.append(force[2][m] + h * force[3][m] + h * corr * coupled)
    acc2m = accel(force2m, disp2m, vel2m)
    disp2 = [disp1[m] + 0.5 * h * (vel1[m] + vel2m[m]) for m in range(modes)]
    vel2 = [vel1[m] + 0.5 * h * (acc2[m] + acc2m[m]) for m in range(modes)]
    coef = [[corr * acc1[m] for m in range(modes)], vel1, vel2m]
    return coef, disp2, vel2


def step2_rate_kernel(peers, ax_ref, pt_ref, a_ref, ms_ref, glo_ref, gup_ref, halo_ref, ra_ref):
    fields = a_ref.shape[0]
    modes = ms_ref.shape[0]
    pitch = ms_ref.shape[1]
    jac = read_jacobians(ax_ref, pt_ref, fields)
    _, ms, gl, gu = assemble(None, ms_ref, glo_ref, gup_ref, halo_ref, fields, modes, pitch)
    inside, _ = lane_masks(peers, ms[0].shape, ms_ref.shape[-1])
    every = list(range(fields))
    a = [a_ref[j] for j in every]
    ra = kernel_rate(a, gl[1], gu[1], jac, None, inside, every)
    for j in every:
        ra_ref[j] = ra[j]


def second_kernel(
    peers,
    force_scale,
    tot_ref,
    stiff_ref,
    disp_ref,
    vel_ref,
    ax_ref,
    pt_ref,
    a_ref,
    ra_ref,
    ms_ref,
    glo_ref,
    gup_ref,
    halo_ref,
    out_ref,
    disp_out_ref,
    vel_out_ref,
):
    h = TIME_STEP
    fields = a_ref.shape[0]
    modes = ms_ref.shape[0]
    pitch = ms_ref.shape[1]
    jac = read_jacobians(ax_ref, pt_ref, fields)
    coef, disp2, vel2 = modal_steps(force_scale, tot_ref, stiff_ref, disp_ref, vel_ref, modes)
    for m in range(modes):
        disp_out_ref[0, m] = disp2[m]
        vel_out_ref[0, m] = vel2[m]
    _, ms, gl, gu = assemble(None, ms_ref, glo_ref, gup_ref, halo_ref, fields, modes, pitch)
    inside, _ = lane_masks(peers, ms[0].shape, ms_ref.shape[-1])

    def combine(weights):
        total = weights[0] * ms[0]
        for m in range(1, modes):
            total = total + weights[m] * ms[m]
        return total

    gl2, gu2 = gl[1], gu[1]
    every = list(range(fields))
    s1 = [a_ref[j] for j in every]
    correction = combine(coef[0])
    s1[1] = s1[1] + correction
    rows = correction.shape[0]
    row = lax.broadcasted_iota(jnp.int32, correction.shape, 0)
    east, west = lane_roll(correction, -1), lane_roll(correction, 1)
    north = jnp.where(row == rows - 1, 0.0, row_roll(correction, -1))
    south = jnp.where(row == 0, 0.0, row_roll(correction, 1))
    ga = 0.5 * (east - west)
    gp = 0.5 * (north - south)
    lap = east + west + north + south - 4.0 * correction
    ax, pt = jac
    push1 = COUPLING * combine(coef[1])
    k1 = []
    for i in every:
        r = -ax[i][1] * ga - pt[i][1] * gp
        if i == 1:
            r = r + DIFFUSION * lap + push1
        k1.append(ra_ref[i] + masked(r, inside))
    mid = [s1[j] + h * k1[j] for j in every]
    k2 = kernel_rate(mid, gl2, gu2, jac, COUPLING * combine(coef[2]), inside, every)
    width = out_ref.shape[-1]
    for j in every:
        s2 = s1[j] + 0.5 * h * (k1[j] + k2[j])
        out_ref[j] = s2[:, :width]


def vmem_spec():
    return pl.BlockSpec(memory_space=pltpu.VMEM)


def smem_spec():
    return pl.BlockSpec(memory_space=pltpu.SMEM)


def on_device(
    flow_field,
    lower_row_history,
    upper_row_history,
    lower_lag_slot,
    upper_lag_slot,
    axial_jacobian,
    pitch_jacobian,
    mode_shape,
    stiffness,
    displacement,
    velocity,
):
    h = TIME_STEP
    state0 = flow_field[0]
    fields, pitch_cells, axial_cells = state0.shape
    modes = mode_shape.shape[0]
    mesh_peers = lax.axis_size("mesh")
    me = lax.axis_index("mesh")
    force_scale = 1.0 / math.sqrt(pitch_cells * axial_cells * mesh_peers)
    passages = lax.axis_size("blk")
    position = lax.axis_index("blk")
    blade_stiffness = stiffness[0]
    disp0 = displacement[0]
    vel0 = velocity[0]

    row_shape = jax.ShapeDtypeStruct((STEP_COUNT,) + upper_row_history.shape[2:], state0.dtype)
    rows_up, rows_down = pl.pallas_call(
        functools.partial(pick_kernel, passages),
        out_shape=(row_shape, row_shape),
        in_specs=[smem_spec(), smem_spec(), vmem_spec(), vmem_spec()],
        out_specs=(vmem_spec(), vmem_spec()),
    )(
        lower_lag_slot,
        upper_lag_slot,
        jnp.transpose(upper_row_history[0], (1, 0, 2)),
        jnp.transpose(lower_row_history[0], (1, 0, 2)),
    )
    lower_ghosts = shifted(rows_up, "blk", 1)
    upper_ghosts = shifted(rows_down, "blk", -1)

    reach = 2 * STEP_COUNT
    own = [state0, mode_shape, lower_ghosts, upper_ghosts]
    shapes = [part.shape[:-1] + (reach,) for part in own]
    from_left = shifted(pack([part[..., -reach:] for part in own], reach).reshape(-1), "mesh", 1)
    from_right = shifted(pack([part[..., :reach] for part in own], reach).reshape(-1), "mesh", -1)
    from_left = from_left.reshape(reach, -1)
    from_right = from_right.reshape(reach, -1)
    from_left = jnp.where(me > 0, from_left, jnp.zeros_like(from_left))
    from_right = jnp.where(me < mesh_peers - 1, from_right, jnp.zeros_like(from_right))
    gap = jnp.zeros((from_left.shape[1], LANES - 2 * reach), from_left.dtype)
    halo_tile = jnp.concatenate([from_right.T, gap, from_left.T], axis=1)
    lanes_wide = axial_cells + LANES
    ins = (state0, mode_shape, lower_ghosts, upper_ghosts, halo_tile)

    base1, part_lanes = pl.pallas_call(
        functools.partial(first_kernel, mesh_peers),
        out_shape=(
            jax.ShapeDtypeStruct((fields, pitch_cells, lanes_wide), state0.dtype),
            jax.ShapeDtypeStruct((4 * modes + modes * modes, LANES), state0.dtype),
        ),
        in_specs=[smem_spec()] * 3 + [vmem_spec()] * 5,
        out_specs=(vmem_spec(), vmem_spec()),
    )(axial_jacobian, pitch_jacobian, velocity, *ins)

    totals = mesh_sum(jnp.sum(part_lanes, axis=1))

    rate_a = pl.pallas_call(
        functools.partial(step2_rate_kernel, mesh_peers),
        out_shape=jax.ShapeDtypeStruct(base1.shape, base1.dtype),
        in_specs=[smem_spec()] * 2 + [vmem_spec()] * 5,
        out_specs=vmem_spec(),
    )(axial_jacobian, pitch_jacobian, base1, *ins[1:])

    small = jax.ShapeDtypeStruct(displacement.shape, displacement.dtype)
    state2, disp2, vel2 = pl.pallas_call(
        functools.partial(second_kernel, mesh_peers, force_scale),
        out_shape=(jax.ShapeDtypeStruct(state0.shape, state0.dtype), small, small),
        in_specs=[smem_spec()] * 6 + [vmem_spec()] * 6,
        out_specs=(vmem_spec(), smem_spec(), smem_spec()),
    )(totals, stiffness, displacement, velocity, axial_jacobian, pitch_jacobian, base1, rate_a, *ins[1:])
    return (state2[None], disp2, vel2)


def solution(mesh):
    return jax.shard_map(
        on_device,
        mesh=mesh,
        in_specs=(
            P("blk", None, None, "mesh"),
            P("blk", None, None, "mesh"),
            P("blk", None, None, "mesh"),
            P(),
            P(),
            P(),
            P(),
            P(None, None, "mesh"),
            P("blk", None),
            P("blk", None),
            P("blk", None),
        ),
        out_specs=(P("blk", None, None, "mesh"), P("blk", None), P("blk", None)),
        check_vma=False,
    )
```

```python
import functools
import math

import jax
import jax.numpy as jnp
from jax import lax
from jax.experimental import pallas as pl
from jax.experimental.pallas import tpu as pltpu
from jax.sharding import PartitionSpec as P

STEP_COUNT = 2


PRECISE = lax.Precision.HIGHEST
TIME_STEP = 0.4
DIFFUSION = 0.1
COUPLING = 0.3
DAMPING = 0.1


def shifted(value, axis, by):
    peers = lax.axis_size(axis)
    return lax.ppermute(value, axis, [(i, (i + by) % peers) for i in range(peers)])


def halo(value):
    peers = lax.axis_size("mesh")
    me = lax.axis_index("mesh")
    before = shifted(value[..., -1:], "mesh", 1)
    after = shifted(value[..., :1], "mesh", -1)
    before = jnp.where(me > 0, before, jnp.zeros_like(before))
    after = jnp.where(me < peers - 1, after, jnp.zeros_like(after))
    return before, after


def mesh_sum(value):
    peers = lax.axis_size("mesh")
    if peers & (peers - 1):
        return lax.psum(value, "mesh")
    step = 1
    while step < peers:
        value = value + lax.ppermute(value, "mesh", [(i, i ^ step) for i in range(peers)])
        step *= 2
    return value


def pick_rows(table, index, count):
    slots = table.shape[0]
    slot = jnp.arange(slots, dtype=jnp.int32).reshape((slots,) + (1,) * (table.ndim - 1))
    rows = []
    for s in range(count):
        hit = slot == (index + s) % slots
        rows.append(jnp.sum(jnp.where(hit, table, jnp.zeros_like(table)), axis=0))
    return jnp.stack(rows)


def pick_entry(values, index):
    hit = jnp.arange(values.shape[0], dtype=jnp.int32) == index
    return jnp.sum(jnp.where(hit, values, jnp.zeros_like(values)))


def axial_pad(value, before, after):
    return jnp.concatenate([before, value, after], axis=-1)


def pitch_pad(value, lower, upper):
    return jnp.concatenate([lower[:, None, :], value, upper[:, None, :]], axis=1)


def flow_rate(state, before, after, lower_ghost, upper_ghost, axial_jacobian, pitch_jacobian):
    padded_axial = axial_pad(state, before, after)
    padded_pitch = pitch_pad(state, lower_ghost, upper_ghost)
    grad_axial = 0.5 * (padded_axial[:, :, 2:] - padded_axial[:, :, :-2])
    grad_pitch = 0.5 * (padded_pitch[:, 2:, :] - padded_pitch[:, :-2, :])
    laplacian = (
        padded_axial[:, :, 2:]
        + padded_axial[:, :, :-2]
        + padded_pitch[:, 2:, :]
        + padded_pitch[:, :-2, :]
        - 4.0 * state
    )
    flux = jnp.einsum("ij,jpx->ipx", axial_jacobian, grad_axial, precision=PRECISE)
    flux = flux + jnp.einsum("ij,jpx->ipx", pitch_jacobian, grad_pitch, precision=PRECISE)
    return DIFFUSION * laplacian - flux


def single_field_grads(field, before, after):
    padded_axial = jnp.concatenate([before, field, after], axis=-1)
    zero_row = jnp.zeros_like(field[..., :1, :])
    padded_pitch = jnp.concatenate([zero_row, field, zero_row], axis=-2)
    grad_axial = 0.5 * (padded_axial[..., 2:] - padded_axial[..., :-2])
    grad_pitch = 0.5 * (padded_pitch[..., 2:, :] - padded_pitch[..., :-2, :])
    laplacian = (
        padded_axial[..., 2:]
        + padded_axial[..., :-2]
        + padded_pitch[..., 2:, :]
        + padded_pitch[..., :-2, :]
        - 4.0 * field
    )
    return grad_axial, grad_pitch, laplacian


def modal_field(weights, mode_shape):
    return jnp.einsum("m,mpx->px", weights, mode_shape, precision=PRECISE)


def projection(mode_shape, field):
    return jnp.einsum("mpx,px->m", mode_shape, field, precision=PRECISE)


def add_field_one(rate, extra):
    return rate.at[1].add(extra)


def rate_field4(state, lower_ghost, upper_ghost, axial_jacobian, pitch_jacobian):
    zero_col = jnp.zeros_like(state[..., :1])
    padded_axial = jnp.concatenate([zero_col, state, zero_col], axis=-1)
    padded_pitch = pitch_pad(state, lower_ghost, upper_ghost)
    grad_axial = 0.5 * (padded_axial[:, :, 2:] - padded_axial[:, :, :-2])
    grad_pitch = 0.5 * (padded_pitch[:, 2:, :] - padded_pitch[:, :-2, :])
    laplacian = (
        padded_axial[4, :, 2:]
        + padded_axial[4, :, :-2]
        + padded_pitch[4, 2:, :]
        + padded_pitch[4, :-2, :]
        - 4.0 * state[4]
    )
    flux = jnp.einsum("j,jpx->px", axial_jacobian[4], grad_axial, precision=PRECISE)
    flux = flux + jnp.einsum("j,jpx->px", pitch_jacobian[4], grad_pitch, precision=PRECISE)
    return DIFFUSION * laplacian - flux


def pack(parts, width):
    flat = [jnp.moveaxis(part, -1, 0).reshape(width, -1) for part in parts]
    return jnp.concatenate(flat, axis=1)


def unpack(buffer, shapes):
    out, offset = [], 0
    for shape in shapes:
        count = math.prod(shape[:-1])
        out.append(buffer[offset : offset + count].reshape(shape))
        offset += count
    return out


LANES = 128


def lane_roll(x, shift):
    return pltpu.roll(x, shift % x.shape[-1], x.ndim - 1)


def row_roll(x, shift):
    return pltpu.roll(x, shift % x.shape[0], 0)


def pitch_neighbours(s, lower, upper):
    rows = s.shape[0]
    tile = 8
    edge = lax.broadcasted_iota(jnp.int32, (tile,) + s.shape[1:], 0)
    north = row_roll(s, -1)
    south = row_roll(s, 1)
    north = jnp.concatenate(
        [north[: rows - tile], jnp.where(edge == tile - 1, upper, north[rows - tile :])], axis=0
    )
    south = jnp.concatenate([jnp.where(edge == 0, lower, south[:tile]), south[tile:]], axis=0)
    return north, south


def masked(r, inside):
    cut = r.shape[-1] - LANES
    return jnp.concatenate([r[:, :cut], r[:, cut:] * inside[:, cut:]], axis=1)


def kernel_rate(state, lower, upper, jac, push, inside, fields_out):
    ax, pt = jac
    diffs_a, diffs_p, laps = [], [], []
    for j, s in enumerate(state):
        east = lane_roll(s, -1)
        west = lane_roll(s, 1)
        north, south = pitch_neighbours(s, lower[j], upper[j])
        diffs_a.append(east - west)
        diffs_p.append(north - south)
        laps.append((east + west) + (north + south) - 4.0 * s)
    out = []
    for i in fields_out:
        r = DIFFUSION * laps[i]
        for j in range(len(state)):
            r = r - (0.5 * ax[i][j]) * diffs_a[j] - (0.5 * pt[i][j]) * diffs_p[j]
        if i == 1 and push is not None:
            r = r + push
        out.append(masked(r, inside))
    return out


def read_jacobians(ax_ref, pt_ref, fields):
    ax = [[ax_ref[i, j] for j in range(fields)] for i in range(fields)]
    pt = [[pt_ref[i, j] for j in range(fields)] for i in range(fields)]
    return ax, pt


def lane_fold(x):
    x = jnp.sum(x, axis=0, keepdims=True)
    total = x[:, :LANES]
    for t in range(1, x.shape[1] // LANES):
        total = total + x[:, t * LANES : (t + 1) * LANES]
    return total


def pick_kernel(peers, lower_slot_ref, upper_slot_ref, upper_hist_ref, lower_hist_ref, up_ref, down_ref):
    fields, slots = upper_hist_ref.shape[0], upper_hist_ref.shape[1]
    position = lax.axis_index("blk")
    slot_next = lower_slot_ref[(position + 1) % peers]
    slot_prev = upper_slot_ref[(position + peers - 1) % peers]
    for s in range(up_ref.shape[0]):
        up_at = (slot_next + s) % slots
        down_at = (slot_prev + s) % slots
        for f in range(fields):
            up_ref[s, f : f + 1, :] = upper_hist_ref[f, pl.ds(up_at, 1), :]
            down_ref[s, f : f + 1, :] = lower_hist_ref[f, pl.ds(down_at, 1), :]


def widened(own, tile):
    return jnp.concatenate([own, tile], axis=-1)


def lane_masks(peers, shape, own_width):
    reach = 2 * STEP_COUNT
    me = lax.axis_index("mesh")
    lane = lax.broadcasted_iota(jnp.int32, shape, len(shape) - 1)
    width = shape[-1]
    right_ok = (lane >= own_width) & (lane < own_width + reach) & (me < peers - 1)
    left_ok = (lane >= width - reach) & (me > 0)
    owned = lane < own_width
    inside = owned | right_ok | left_ok
    return inside.astype(jnp.float32), owned.astype(jnp.float32)


def assemble(u_ref, ms_ref, glo_ref, gup_ref, halo_ref, fields, modes, pitch):
    u = []
    for j in range(fields if u_ref is not None else 0):
        rows = slice(j * pitch, (j + 1) * pitch)
        u.append(widened(u_ref[j], halo_ref[rows, :]))
    ms = []
    for m in range(modes):
        rows = slice((fields + m) * pitch, (fields + m + 1) * pitch)
        ms.append(widened(ms_ref[m], halo_ref[rows, :]))
    base = (fields + modes) * pitch
    steps = glo_ref.shape[0]
    ghosts = []
    for side, ref in enumerate((glo_ref, gup_ref)):
        per_step = []
        for s in range(steps):
            start = base + (side * steps + s) * fields
            rows = slice(start, start + fields)
            block = widened(ref[s], halo_ref[rows, :])
            per_step.append([block[j : j + 1, :] for j in range(fields)])
        ghosts.append(per_step)
    return u, ms, ghosts[0], ghosts[1]


def first_kernel(peers, ax_ref, pt_ref, vel_ref, u_ref, ms_ref, glo_ref, gup_ref, halo_ref, a_ref, part_ref):
    h = TIME_STEP
    fields = u_ref.shape[0]
    modes = ms_ref.shape[0]
    pitch = u_ref.shape[1]
    jac = read_jacobians(ax_ref, pt_ref, fields)
    vel = [vel_ref[0, m] for m in range(modes)]
    u0, ms, gl, gu = assemble(u_ref, ms_ref, glo_ref, gup_ref, halo_ref, fields, modes, pitch)
    inside, _ = lane_masks(peers, u0[0].shape, u_ref.shape[-1])
    push = vel[0] * ms[0]
    for m in range(1, modes):
        push = push + vel[m] * ms[m]
    push = COUPLING * push
    gl1, gu1, gl2, gu2 = gl[0], gu[0], gl[1], gu[1]
    every = list(range(fields))
    k1 = kernel_rate(u0, gl1, gu1, jac, push, inside, every)
    mid = [u0[j] + h * k1[j] for j in every]
    k2 = kernel_rate(mid, gl1, gu1, jac, push, inside, every)
    a = [u0[j] + 0.5 * h * (k1[j] + k2[j]) for j in every]
    for j in every:
        a_ref[j] = a[j]
    (ra4,) = kernel_rate(a, gl2, gu2, jac, None, inside, [4])
    own = u_ref.shape[-1]
    weighted = [ms_ref[m] for m in range(modes)]
    k = 0
    for field in (u0[4], mid[4], a[4], ra4):
        field = field[:, :own]
        for m in range(modes):
            part_ref[k : k + 1, :] = lane_fold(weighted[m] * field)
            k += 1
    ax41, pt41 = 0.5 * jac[0][4][1], 0.5 * jac[1][4][1]
    no_ghost = jnp.zeros((1, ms[0].shape[1]), ms[0].dtype)
    for n in range(modes):
        s = ms[n]
        north, south = pitch_neighbours(s, no_ghost, no_ghost)
        t = -(ax41 * (lane_roll(s, -1) - lane_roll(s, 1)) + pt41 * (north - south))
        t = t[:, :own]
        for m in range(modes):
            part_ref[k + m * modes + n : k + m * modes + n + 1, :] = lane_fold(weighted[m] * t)


def modal_steps(force_scale, tot_ref, stiff_ref, disp_ref, vel_ref, modes):
    h = TIME_STEP
    t = [force_scale * tot_ref[k] for k in range(4 * modes + modes * modes)]
    force = [t[w * modes : (w + 1) * modes] for w in range(4)]
    couple = [t[4 * modes + m * modes : 4 * modes + (m + 1) * modes] for m in range(modes)]
    stiff = [stiff_ref[0, m] for m in range(modes)]
    disp0 = [disp_ref[0, m] for m in range(modes)]
    vel0 = [vel_ref[0, m] for m in range(modes)]

    def accel(f, q, v):
        return [f[m] - stiff[m] * q[m] - DAMPING * v[m] for m in range(modes)]

    def axpy(x, a, y):
        return [x[m] + a * y[m] for m in range(modes)]

    acc1 = accel(force[0], disp0, vel0)
    disp1m = axpy(disp0, h, vel0)
    vel1m = axpy(vel0, h, acc1)
    acc1m = accel(force[1], disp1m, vel1m)
    disp1 = [disp0[m] + 0.5 * h * (vel0[m] + vel1m[m]) for m in range(modes)]
    vel1 = [vel0[m] + 0.5 * h * (acc1[m] + acc1m[m]) for m in range(modes)]
    acc2 = accel(force[2], disp1, vel1)
    disp2m = axpy(disp1, h, vel1)
    vel2m = axpy(vel1, h, acc2)
    corr = 0.5 * h * h * COUPLING
    force2m = []
    for m in range(modes):
        coupled = couple[m][0] * acc1[0]
        for n in range(1, modes):
            coupled = coupled + couple[m][n] * acc1[n]
        force2m.append(force[2][m] + h * force[3][m] + h * corr * coupled)
    acc2m = accel(force2m, disp2m, vel2m)
    disp2 = [disp1[m] + 0.5 * h * (vel1[m] + vel2m[m]) for m in range(modes)]
    vel2 = [vel1[m] + 0.5 * h * (acc2[m] + acc2m[m]) for m in range(modes)]
    coef = [[corr * acc1[m] for m in range(modes)], vel1, vel2m]
    return coef, disp2, vel2


def step2_rate_kernel(peers, ax_ref, pt_ref, a_ref, ms_ref, glo_ref, gup_ref, halo_ref, ra_ref):
    fields = a_ref.shape[0]
    modes = ms_ref.shape[0]
    pitch = ms_ref.shape[1]
    jac = read_jacobians(ax_ref, pt_ref, fields)
    _, ms, gl, gu = assemble(None, ms_ref, glo_ref, gup_ref, halo_ref, fields, modes, pitch)
    inside, _ = lane_masks(peers, ms[0].shape, ms_ref.shape[-1])
    every = list(range(fields))
    a = [a_ref[j] for j in every]
    ra = kernel_rate(a, gl[1], gu[1], jac, None, inside, every)
    for j in every:
        ra_ref[j] = ra[j]


def second_kernel(
    peers,
    force_scale,
    tot_ref,
    stiff_ref,
    disp_ref,
    vel_ref,
    ax_ref,
    pt_ref,
    a_ref,
    ra_ref,
    ms_ref,
    glo_ref,
    gup_ref,
    halo_ref,
    out_ref,
    disp_out_ref,
    vel_out_ref,
):
    h = TIME_STEP
    fields = a_ref.shape[0]
    modes = ms_ref.shape[0]
    pitch = ms_ref.shape[1]
    jac = read_jacobians(ax_ref, pt_ref, fields)
    coef, disp2, vel2 = modal_steps(force_scale, tot_ref, stiff_ref, disp_ref, vel_ref, modes)
    for m in range(modes):
        disp_out_ref[0, m] = disp2[m]
        vel_out_ref[0, m] = vel2[m]
    _, ms, gl, gu = assemble(None, ms_ref, glo_ref, gup_ref, halo_ref, fields, modes, pitch)
    inside, _ = lane_masks(peers, ms[0].shape, ms_ref.shape[-1])

    def combine(weights):
        total = weights[0] * ms[0]
        for m in range(1, modes):
            total = total + weights[m] * ms[m]
        return total

    gl2, gu2 = gl[1], gu[1]
    every = list(range(fields))
    s1 = [a_ref[j] for j in every]
    correction = combine(coef[0])
    s1[1] = s1[1] + correction
    rows = correction.shape[0]
    row = lax.broadcasted_iota(jnp.int32, correction.shape, 0)
    east, west = lane_roll(correction, -1), lane_roll(correction, 1)
    north = jnp.where(row == rows - 1, 0.0, row_roll(correction, -1))
    south = jnp.where(row == 0, 0.0, row_roll(correction, 1))
    ga = 0.5 * (east - west)
    gp = 0.5 * (north - south)
    lap = east + west + north + south - 4.0 * correction
    ax, pt = jac
    push1 = COUPLING * combine(coef[1])
    k1 = []
    for i in every:
        r = -ax[i][1] * ga - pt[i][1] * gp
        if i == 1:
            r = r + DIFFUSION * lap + push1
        k1.append(ra_ref[i] + masked(r, inside))
    mid = [s1[j] + h * k1[j] for j in every]
    k2 = kernel_rate(mid, gl2, gu2, jac, COUPLING * combine(coef[2]), inside, every)
    width = out_ref.shape[-1]
    for j in every:
        s2 = s1[j] + 0.5 * h * (k1[j] + k2[j])
        out_ref[j] = s2[:, :width]


def vmem_spec():
    return pl.BlockSpec(memory_space=pltpu.VMEM)


def smem_spec():
    return pl.BlockSpec(memory_space=pltpu.SMEM)


def on_device(
    flow_field,
    lower_row_history,
    upper_row_history,
    lower_lag_slot,
    upper_lag_slot,
    axial_jacobian,
    pitch_jacobian,
    mode_shape,
    stiffness,
    displacement,
    velocity,
):
    h = TIME_STEP
    state0 = flow_field[0]
    fields, pitch_cells, axial_cells = state0.shape
    modes = mode_shape.shape[0]
    mesh_peers = lax.axis_size("mesh")
    me = lax.axis_index("mesh")
    force_scale = 1.0 / math.sqrt(pitch_cells * axial_cells * mesh_peers)
    passages = lax.axis_size("blk")
    position = lax.axis_index("blk")
    blade_stiffness = stiffness[0]
    disp0 = displacement[0]
    vel0 = velocity[0]

    row_shape = jax.ShapeDtypeStruct((STEP_COUNT,) + upper_row_history.shape[2:], state0.dtype)
    rows_up, rows_down = pl.pallas_call(
        functools.partial(pick_kernel, passages),
        out_shape=(row_shape, row_shape),
        in_specs=[smem_spec(), smem_spec(), vmem_spec(), vmem_spec()],
        out_specs=(vmem_spec(), vmem_spec()),
    )(
        lower_lag_slot,
        upper_lag_slot,
        jnp.transpose(upper_row_history[0], (1, 0, 2)),
        jnp.transpose(lower_row_history[0], (1, 0, 2)),
    )
    lower_ghosts = shifted(rows_up, "blk", 1)
    upper_ghosts = shifted(rows_down, "blk", -1)

    reach = 2 * STEP_COUNT
    own = [state0, mode_shape, lower_ghosts, upper_ghosts]
    shapes = [part.shape[:-1] + (reach,) for part in own]
    from_left = shifted(pack([part[..., -reach:] for part in own], reach).reshape(-1), "mesh", 1)
    from_right = shifted(pack([part[..., :reach] for part in own], reach).reshape(-1), "mesh", -1)
    from_left = from_left.reshape(reach, -1)
    from_right = from_right.reshape(reach, -1)
    from_left = jnp.where(me > 0, from_left, jnp.zeros_like(from_left))
    from_right = jnp.where(me < mesh_peers - 1, from_right, jnp.zeros_like(from_right))
    gap = jnp.zeros((from_left.shape[1], LANES - 2 * reach), from_left.dtype)
    halo_tile = jnp.concatenate([from_right.T, gap, from_left.T], axis=1)
    lanes_wide = axial_cells + LANES
    ins = (state0, mode_shape, lower_ghosts, upper_ghosts, halo_tile)

    base1, part_lanes = pl.pallas_call(
        functools.partial(first_kernel, mesh_peers),
        out_shape=(
            jax.ShapeDtypeStruct((fields, pitch_cells, lanes_wide), state0.dtype),
            jax.ShapeDtypeStruct((4 * modes + modes * modes, LANES), state0.dtype),
        ),
        in_specs=[smem_spec()] * 3 + [vmem_spec()] * 5,
        out_specs=(vmem_spec(), vmem_spec()),
    )(axial_jacobian, pitch_jacobian, velocity, *ins)

    totals = mesh_sum(jnp.sum(part_lanes, axis=1))

    rate_a = pl.pallas_call(
        functools.partial(step2_rate_kernel, mesh_peers),
        out_shape=jax.ShapeDtypeStruct(base1.shape, base1.dtype),
        in_specs=[smem_spec()] * 2 + [vmem_spec()] * 5,
        out_specs=vmem_spec(),
    )(axial_jacobian, pitch_jacobian, base1, *ins[1:])

    small = jax.ShapeDtypeStruct(displacement.shape, displacement.dtype)
    state2, disp2, vel2 = pl.pallas_call(
        functools.partial(second_kernel, mesh_peers, force_scale),
        out_shape=(jax.ShapeDtypeStruct(state0.shape, state0.dtype), small, small),
        in_specs=[smem_spec()] * 6 + [vmem_spec()] * 6,
        out_specs=(vmem_spec(), smem_spec(), smem_spec()),
    )(totals, stiffness, displacement, velocity, axial_jacobian, pitch_jacobian, base1, rate_a, *ins[1:])
    return (state2[None], disp2, vel2)


def solution(mesh):
    return jax.shard_map(
        on_device,
        mesh=mesh,
        in_specs=(
            P("blk", None, None, "mesh"),
            P("blk", None, None, "mesh"),
            P("blk", None, None, "mesh"),
            P(),
            P(),
            P(),
            P(),
            P(None, None, "mesh"),
            P("blk", None),
            P("blk", None),
            P("blk", None),
        ),
        out_specs=(P("blk", None, None, "mesh"), P("blk", None), P("blk", None)),
        check_vma=False,
    )
```

```python
import functools
import math

import jax
import jax.numpy as jnp
from jax import lax
from jax.experimental import pallas as pl
from jax.experimental.pallas import tpu as pltpu
from jax.sharding import PartitionSpec as P

STEP_COUNT = 2


PRECISE = lax.Precision.HIGHEST
TIME_STEP = 0.4
DIFFUSION = 0.1
COUPLING = 0.3
DAMPING = 0.1


def shifted(value, axis, by):
    peers = lax.axis_size(axis)
    return lax.ppermute(value, axis, [(i, (i + by) % peers) for i in range(peers)])


def halo(value):
    peers = lax.axis_size("mesh")
    me = lax.axis_index("mesh")
    before = shifted(value[..., -1:], "mesh", 1)
    after = shifted(value[..., :1], "mesh", -1)
    before = jnp.where(me > 0, before, jnp.zeros_like(before))
    after = jnp.where(me < peers - 1, after, jnp.zeros_like(after))
    return before, after


def mesh_sum(value):
    peers = lax.axis_size("mesh")
    if peers & (peers - 1):
        return lax.psum(value, "mesh")
    step = 1
    while step < peers:
        value = value + lax.ppermute(value, "mesh", [(i, i ^ step) for i in range(peers)])
        step *= 2
    return value


def pick_rows(table, index, count):
    slots = table.shape[0]
    slot = jnp.arange(slots, dtype=jnp.int32).reshape((slots,) + (1,) * (table.ndim - 1))
    rows = []
    for s in range(count):
        hit = slot == (index + s) % slots
        rows.append(jnp.sum(jnp.where(hit, table, jnp.zeros_like(table)), axis=0))
    return jnp.stack(rows)


def pick_entry(values, index):
    hit = jnp.arange(values.shape[0], dtype=jnp.int32) == index
    return jnp.sum(jnp.where(hit, values, jnp.zeros_like(values)))


def axial_pad(value, before, after):
    return jnp.concatenate([before, value, after], axis=-1)


def pitch_pad(value, lower, upper):
    return jnp.concatenate([lower[:, None, :], value, upper[:, None, :]], axis=1)


def flow_rate(state, before, after, lower_ghost, upper_ghost, axial_jacobian, pitch_jacobian):
    padded_axial = axial_pad(state, before, after)
    padded_pitch = pitch_pad(state, lower_ghost, upper_ghost)
    grad_axial = 0.5 * (padded_axial[:, :, 2:] - padded_axial[:, :, :-2])
    grad_pitch = 0.5 * (padded_pitch[:, 2:, :] - padded_pitch[:, :-2, :])
    laplacian = (
        padded_axial[:, :, 2:]
        + padded_axial[:, :, :-2]
        + padded_pitch[:, 2:, :]
        + padded_pitch[:, :-2, :]
        - 4.0 * state
    )
    flux = jnp.einsum("ij,jpx->ipx", axial_jacobian, grad_axial, precision=PRECISE)
    flux = flux + jnp.einsum("ij,jpx->ipx", pitch_jacobian, grad_pitch, precision=PRECISE)
    return DIFFUSION * laplacian - flux


def single_field_grads(field, before, after):
    padded_axial = jnp.concatenate([before, field, after], axis=-1)
    zero_row = jnp.zeros_like(field[..., :1, :])
    padded_pitch = jnp.concatenate([zero_row, field, zero_row], axis=-2)
    grad_axial = 0.5 * (padded_axial[..., 2:] - padded_axial[..., :-2])
    grad_pitch = 0.5 * (padded_pitch[..., 2:, :] - padded_pitch[..., :-2, :])
    laplacian = (
        padded_axial[..., 2:]
        + padded_axial[..., :-2]
        + padded_pitch[..., 2:, :]
        + padded_pitch[..., :-2, :]
        - 4.0 * field
    )
    return grad_axial, grad_pitch, laplacian


def modal_field(weights, mode_shape):
    return jnp.einsum("m,mpx->px", weights, mode_shape, precision=PRECISE)


def projection(mode_shape, field):
    return jnp.einsum("mpx,px->m", mode_shape, field, precision=PRECISE)


def add_field_one(rate, extra):
    return rate.at[1].add(extra)


def rate_field4(state, lower_ghost, upper_ghost, axial_jacobian, pitch_jacobian):
    zero_col = jnp.zeros_like(state[..., :1])
    padded_axial = jnp.concatenate([zero_col, state, zero_col], axis=-1)
    padded_pitch = pitch_pad(state, lower_ghost, upper_ghost)
    grad_axial = 0.5 * (padded_axial[:, :, 2:] - padded_axial[:, :, :-2])
    grad_pitch = 0.5 * (padded_pitch[:, 2:, :] - padded_pitch[:, :-2, :])
    laplacian = (
        padded_axial[4, :, 2:]
        + padded_axial[4, :, :-2]
        + padded_pitch[4, 2:, :]
        + padded_pitch[4, :-2, :]
        - 4.0 * state[4]
    )
    flux = jnp.einsum("j,jpx->px", axial_jacobian[4], grad_axial, precision=PRECISE)
    flux = flux + jnp.einsum("j,jpx->px", pitch_jacobian[4], grad_pitch, precision=PRECISE)
    return DIFFUSION * laplacian - flux


def pack(parts, width):
    flat = [jnp.moveaxis(part, -1, 0).reshape(width, -1) for part in parts]
    return jnp.concatenate(flat, axis=1)


def unpack(buffer, shapes):
    out, offset = [], 0
    for shape in shapes:
        count = math.prod(shape[:-1])
        out.append(buffer[offset : offset + count].reshape(shape))
        offset += count
    return out


LANES = 128


def lane_roll(x, shift):
    return pltpu.roll(x, shift % x.shape[-1], x.ndim - 1)


def row_roll(x, shift):
    return pltpu.roll(x, shift % x.shape[0], 0)


def pitch_neighbours(s, lower, upper):
    rows = s.shape[0]
    tile = 8
    edge = lax.broadcasted_iota(jnp.int32, (tile,) + s.shape[1:], 0)
    north = row_roll(s, -1)
    south = row_roll(s, 1)
    north = jnp.concatenate(
        [north[: rows - tile], jnp.where(edge == tile - 1, upper, north[rows - tile :])], axis=0
    )
    south = jnp.concatenate([jnp.where(edge == 0, lower, south[:tile]), south[tile:]], axis=0)
    return north, south


def masked(r, inside):
    cut = r.shape[-1] - LANES
    return jnp.concatenate([r[:, :cut], r[:, cut:] * inside[:, cut:]], axis=1)


def kernel_rate(state, lower, upper, jac, push, inside, fields_out):
    ax, pt = jac
    diffs_a, diffs_p, laps = [], [], []
    for j, s in enumerate(state):
        east = lane_roll(s, -1)
        west = lane_roll(s, 1)
        north, south = pitch_neighbours(s, lower[j], upper[j])
        diffs_a.append(east - west)
        diffs_p.append(north - south)
        laps.append((east + west) + (north + south) - 4.0 * s)
    out = []
    for i in fields_out:
        r = DIFFUSION * laps[i]
        for j in range(len(state)):
            r = r - (0.5 * ax[i][j]) * diffs_a[j] - (0.5 * pt[i][j]) * diffs_p[j]
        if i == 1 and push is not None:
            r = r + push
        out.append(masked(r, inside))
    return out


def read_jacobians(ax_ref, pt_ref, fields):
    ax = [[ax_ref[i, j] for j in range(fields)] for i in range(fields)]
    pt = [[pt_ref[i, j] for j in range(fields)] for i in range(fields)]
    return ax, pt


def lane_fold(x):
    x = jnp.sum(x, axis=0, keepdims=True)
    total = x[:, :LANES]
    for t in range(1, x.shape[1] // LANES):
        total = total + x[:, t * LANES : (t + 1) * LANES]
    return total


def pick_kernel(peers, lower_slot_ref, upper_slot_ref, upper_hist_ref, lower_hist_ref, up_ref, down_ref):
    fields, slots = upper_hist_ref.shape[0], upper_hist_ref.shape[1]
    position = lax.axis_index("blk")
    slot_next = lower_slot_ref[(position + 1) % peers]
    slot_prev = upper_slot_ref[(position + peers - 1) % peers]
    for s in range(up_ref.shape[0]):
        up_at = (slot_next + s) % slots
        down_at = (slot_prev + s) % slots
        for f in range(fields):
            up_ref[s, f : f + 1, :] = upper_hist_ref[f, pl.ds(up_at, 1), :]
            down_ref[s, f : f + 1, :] = lower_hist_ref[f, pl.ds(down_at, 1), :]


def widened(own, tile):
    return jnp.concatenate([own, tile], axis=-1)


def lane_masks(peers, shape, own_width):
    reach = 2 * STEP_COUNT
    me = lax.axis_index("mesh")
    lane = lax.broadcasted_iota(jnp.int32, shape, len(shape) - 1)
    width = shape[-1]
    right_ok = (lane >= own_width) & (lane < own_width + reach) & (me < peers - 1)
    left_ok = (lane >= width - reach) & (me > 0)
    owned = lane < own_width
    inside = owned | right_ok | left_ok
    return inside.astype(jnp.float32), owned.astype(jnp.float32)


def assemble(u_ref, ms_ref, glo_ref, gup_ref, halo_ref, fields, modes, pitch):
    u = []
    for j in range(fields if u_ref is not None else 0):
        rows = slice(j * pitch, (j + 1) * pitch)
        u.append(widened(u_ref[j], halo_ref[rows, :]))
    ms = []
    for m in range(modes):
        rows = slice((fields + m) * pitch, (fields + m + 1) * pitch)
        ms.append(widened(ms_ref[m], halo_ref[rows, :]))
    base = (fields + modes) * pitch
    steps = glo_ref.shape[0]
    ghosts = []
    for side, ref in enumerate((glo_ref, gup_ref)):
        per_step = []
        for s in range(steps):
            start = base + (side * steps + s) * fields
            rows = slice(start, start + fields)
            block = widened(ref[s], halo_ref[rows, :])
            per_step.append([block[j : j + 1, :] for j in range(fields)])
        ghosts.append(per_step)
    return u, ms, ghosts[0], ghosts[1]


def first_kernel(peers, ax_ref, pt_ref, vel_ref, u_ref, ms_ref, glo_ref, gup_ref, halo_ref, a_ref, part_ref):
    h = TIME_STEP
    fields = u_ref.shape[0]
    modes = ms_ref.shape[0]
    pitch = u_ref.shape[1]
    jac = read_jacobians(ax_ref, pt_ref, fields)
    vel = [vel_ref[0, m] for m in range(modes)]
    u0, ms, gl, gu = assemble(u_ref, ms_ref, glo_ref, gup_ref, halo_ref, fields, modes, pitch)
    inside, _ = lane_masks(peers, u0[0].shape, u_ref.shape[-1])
    push = vel[0] * ms[0]
    for m in range(1, modes):
        push = push + vel[m] * ms[m]
    push = COUPLING * push
    gl1, gu1, gl2, gu2 = gl[0], gu[0], gl[1], gu[1]
    every = list(range(fields))
    k1 = kernel_rate(u0, gl1, gu1, jac, push, inside, every)
    mid = [u0[j] + h * k1[j] for j in every]
    k2 = kernel_rate(mid, gl1, gu1, jac, push, inside, every)
    a = [u0[j] + 0.5 * h * (k1[j] + k2[j]) for j in every]
    for j in every:
        a_ref[j] = a[j]
    (ra4,) = kernel_rate(a, gl2, gu2, jac, None, inside, [4])
    own = u_ref.shape[-1]
    weighted = [ms_ref[m] for m in range(modes)]
    k = 0
    for field in (u0[4], mid[4], a[4], ra4):
        field = field[:, :own]
        for m in range(modes):
            part_ref[k : k + 1, :] = lane_fold(weighted[m] * field)
            k += 1
    ax41, pt41 = 0.5 * jac[0][4][1], 0.5 * jac[1][4][1]
    no_ghost = jnp.zeros((1, ms[0].shape[1]), ms[0].dtype)
    for n in range(modes):
        s = ms[n]
        north, south = pitch_neighbours(s, no_ghost, no_ghost)
        t = -(ax41 * (lane_roll(s, -1) - lane_roll(s, 1)) + pt41 * (north - south))
        t = t[:, :own]
        for m in range(modes):
            part_ref[k + m * modes + n : k + m * modes + n + 1, :] = lane_fold(weighted[m] * t)


def modal_steps(force_scale, tot_ref, stiff_ref, disp_ref, vel_ref, modes):
    h = TIME_STEP
    t = [force_scale * tot_ref[k] for k in range(4 * modes + modes * modes)]
    force = [t[w * modes : (w + 1) * modes] for w in range(4)]
    couple = [t[4 * modes + m * modes : 4 * modes + (m + 1) * modes] for m in range(modes)]
    stiff = [stiff_ref[0, m] for m in range(modes)]
    disp0 = [disp_ref[0, m] for m in range(modes)]
    vel0 = [vel_ref[0, m] for m in range(modes)]

    def accel(f, q, v):
        return [f[m] - stiff[m] * q[m] - DAMPING * v[m] for m in range(modes)]

    def axpy(x, a, y):
        return [x[m] + a * y[m] for m in range(modes)]

    acc1 = accel(force[0], disp0, vel0)
    disp1m = axpy(disp0, h, vel0)
    vel1m = axpy(vel0, h, acc1)
    acc1m = accel(force[1], disp1m, vel1m)
    disp1 = [disp0[m] + 0.5 * h * (vel0[m] + vel1m[m]) for m in range(modes)]
    vel1 = [vel0[m] + 0.5 * h * (acc1[m] + acc1m[m]) for m in range(modes)]
    acc2 = accel(force[2], disp1, vel1)
    disp2m = axpy(disp1, h, vel1)
    vel2m = axpy(vel1, h, acc2)
    corr = 0.5 * h * h * COUPLING
    force2m = []
    for m in range(modes):
        coupled = couple[m][0] * acc1[0]
        for n in range(1, modes):
            coupled = coupled + couple[m][n] * acc1[n]
        force2m.append(force[2][m] + h * force[3][m] + h * corr * coupled)
    acc2m = accel(force2m, disp2m, vel2m)
    disp2 = [disp1[m] + 0.5 * h * (vel1[m] + vel2m[m]) for m in range(modes)]
    vel2 = [vel1[m] + 0.5 * h * (acc2[m] + acc2m[m]) for m in range(modes)]
    coef = [[corr * acc1[m] for m in range(modes)], vel1, vel2m]
    return coef, disp2, vel2


def step2_rate_kernel(peers, first, ax_ref, pt_ref, *refs):
    a_ref, ms_ref, glo_ref, gup_ref, halo_ref, ra_ref = refs[-6:]
    fields = a_ref.shape[0]
    modes = ms_ref.shape[0]
    pitch = ms_ref.shape[1]
    jac = read_jacobians(ax_ref, pt_ref, fields)
    _, ms, gl, gu = assemble(None, ms_ref, glo_ref, gup_ref, halo_ref, fields, modes, pitch)
    inside, _ = lane_masks(peers, ms[0].shape, ms_ref.shape[-1])
    every = list(range(fields))
    a = [a_ref[j] for j in every]
    wanted = list(range(first, first + ra_ref.shape[0]))
    ra = kernel_rate(a, gl[1], gu[1], jac, None, inside, wanted)
    for j, r in enumerate(ra):
        ra_ref[j] = r


def second_kernel(
    peers,
    force_scale,
    tot_ref,
    stiff_ref,
    disp_ref,
    vel_ref,
    ax_ref,
    pt_ref,
    a_ref,
    ra_low_ref,
    ra_high_ref,
    ms_ref,
    glo_ref,
    gup_ref,
    halo_ref,
    out_ref,
    disp_out_ref,
    vel_out_ref,
):
    h = TIME_STEP
    fields = a_ref.shape[0]
    modes = ms_ref.shape[0]
    pitch = ms_ref.shape[1]
    jac = read_jacobians(ax_ref, pt_ref, fields)
    coef, disp2, vel2 = modal_steps(force_scale, tot_ref, stiff_ref, disp_ref, vel_ref, modes)
    for m in range(modes):
        disp_out_ref[0, m] = disp2[m]
        vel_out_ref[0, m] = vel2[m]
    _, ms, gl, gu = assemble(None, ms_ref, glo_ref, gup_ref, halo_ref, fields, modes, pitch)
    inside, _ = lane_masks(peers, ms[0].shape, ms_ref.shape[-1])

    def combine(weights):
        total = weights[0] * ms[0]
        for m in range(1, modes):
            total = total + weights[m] * ms[m]
        return total

    gl2, gu2 = gl[1], gu[1]
    every = list(range(fields))
    s1 = [a_ref[j] for j in every]
    correction = combine(coef[0])
    s1[1] = s1[1] + correction
    rows = correction.shape[0]
    row = lax.broadcasted_iota(jnp.int32, correction.shape, 0)
    east, west = lane_roll(correction, -1), lane_roll(correction, 1)
    north = jnp.where(row == rows - 1, 0.0, row_roll(correction, -1))
    south = jnp.where(row == 0, 0.0, row_roll(correction, 1))
    ga = 0.5 * (east - west)
    gp = 0.5 * (north - south)
    lap = east + west + north + south - 4.0 * correction
    ax, pt = jac
    push1 = COUPLING * combine(coef[1])
    k1 = []
    for i in every:
        r = -ax[i][1] * ga - pt[i][1] * gp
        if i == 1:
            r = r + DIFFUSION * lap + push1
        split = ra_low_ref.shape[0]
        ra_i = ra_low_ref[i] if i < split else ra_high_ref[i - split]
        k1.append(ra_i + masked(r, inside))
    mid = [s1[j] + h * k1[j] for j in every]
    k2 = kernel_rate(mid, gl2, gu2, jac, COUPLING * combine(coef[2]), inside, every)
    width = out_ref.shape[-1]
    for j in every:
        s2 = s1[j] + 0.5 * h * (k1[j] + k2[j])
        out_ref[j] = s2[:, :width]


def vmem_spec():
    return pl.BlockSpec(memory_space=pltpu.VMEM)


def smem_spec():
    return pl.BlockSpec(memory_space=pltpu.SMEM)


def on_device(
    flow_field,
    lower_row_history,
    upper_row_history,
    lower_lag_slot,
    upper_lag_slot,
    axial_jacobian,
    pitch_jacobian,
    mode_shape,
    stiffness,
    displacement,
    velocity,
):
    h = TIME_STEP
    state0 = flow_field[0]
    fields, pitch_cells, axial_cells = state0.shape
    modes = mode_shape.shape[0]
    mesh_peers = lax.axis_size("mesh")
    me = lax.axis_index("mesh")
    force_scale = 1.0 / math.sqrt(pitch_cells * axial_cells * mesh_peers)
    passages = lax.axis_size("blk")
    position = lax.axis_index("blk")
    blade_stiffness = stiffness[0]
    disp0 = displacement[0]
    vel0 = velocity[0]

    row_shape = jax.ShapeDtypeStruct((STEP_COUNT,) + upper_row_history.shape[2:], state0.dtype)
    rows_up, rows_down = pl.pallas_call(
        functools.partial(pick_kernel, passages),
        out_shape=(row_shape, row_shape),
        in_specs=[smem_spec(), smem_spec(), vmem_spec(), vmem_spec()],
        out_specs=(vmem_spec(), vmem_spec()),
    )(
        lower_lag_slot,
        upper_lag_slot,
        jnp.transpose(upper_row_history[0], (1, 0, 2)),
        jnp.transpose(lower_row_history[0], (1, 0, 2)),
    )
    lower_ghosts = shifted(rows_up, "blk", 1)
    upper_ghosts = shifted(rows_down, "blk", -1)

    reach = 2 * STEP_COUNT
    own = [state0, mode_shape, lower_ghosts, upper_ghosts]
    shapes = [part.shape[:-1] + (reach,) for part in own]
    from_left = shifted(pack([part[..., -reach:] for part in own], reach).reshape(-1), "mesh", 1)
    from_right = shifted(pack([part[..., :reach] for part in own], reach).reshape(-1), "mesh", -1)
    from_left = from_left.reshape(reach, -1)
    from_right = from_right.reshape(reach, -1)
    from_left = jnp.where(me > 0, from_left, jnp.zeros_like(from_left))
    from_right = jnp.where(me < mesh_peers - 1, from_right, jnp.zeros_like(from_right))
    gap = jnp.zeros((from_left.shape[1], LANES - 2 * reach), from_left.dtype)
    halo_tile = jnp.concatenate([from_right.T, gap, from_left.T], axis=1)
    lanes_wide = axial_cells + LANES
    ins = (state0, mode_shape, lower_ghosts, upper_ghosts, halo_tile)

    base1, part_lanes = pl.pallas_call(
        functools.partial(first_kernel, mesh_peers),
        out_shape=(
            jax.ShapeDtypeStruct((fields, pitch_cells, lanes_wide), state0.dtype),
            jax.ShapeDtypeStruct((4 * modes + modes * modes, LANES), state0.dtype),
        ),
        in_specs=[smem_spec()] * 3 + [vmem_spec()] * 5,
        out_specs=(vmem_spec(), vmem_spec()),
    )(axial_jacobian, pitch_jacobian, velocity, *ins)

    split = fields // 2

    def rate_part(first, count, *order):
        return pl.pallas_call(
            functools.partial(step2_rate_kernel, mesh_peers, first),
            out_shape=jax.ShapeDtypeStruct((count,) + base1.shape[1:], base1.dtype),
            in_specs=[smem_spec()] * (2 + len(order)) + [vmem_spec()] * 5,
            out_specs=vmem_spec(),
        )(axial_jacobian, pitch_jacobian, *order, base1, *ins[1:])

    rate_low = rate_part(0, split)
    totals = jnp.sum(part_lanes, axis=1)
    peers = mesh_peers
    if peers & (peers - 1) or peers < 2:
        totals = lax.psum(totals, "mesh")
        rate_high = rate_part(split, fields - split)
    else:
        step = 1
        while step < peers:
            totals = totals + lax.ppermute(totals, "mesh", [(i, i ^ step) for i in range(peers)])
            if step == 1:
                totals, rate_low = lax.optimization_barrier((totals, rate_low))
                rate_high = rate_part(split, fields - split, totals)
            step *= 2

    small = jax.ShapeDtypeStruct(displacement.shape, displacement.dtype)
    state2, disp2, vel2 = pl.pallas_call(
        functools.partial(second_kernel, mesh_peers, force_scale),
        out_shape=(jax.ShapeDtypeStruct(state0.shape, state0.dtype), small, small),
        in_specs=[smem_spec()] * 6 + [vmem_spec()] * 7,
        out_specs=(vmem_spec(), smem_spec(), smem_spec()),
    )(totals, stiffness, displacement, velocity, axial_jacobian, pitch_jacobian, base1, rate_low, rate_high, *ins[1:])
    return (state2[None], disp2, vel2)


def solution(mesh):
    return jax.shard_map(
        on_device,
        mesh=mesh,
        in_specs=(
            P("blk", None, None, "mesh"),
            P("blk", None, None, "mesh"),
            P("blk", None, None, "mesh"),
            P(),
            P(),
            P(),
            P(),
            P(None, None, "mesh"),
            P("blk", None),
            P("blk", None),
            P("blk", None),
        ),
        out_specs=(P("blk", None, None, "mesh"), P("blk", None), P("blk", None)),
        check_vma=False,
    )
```

```python
import functools
import math

import jax
import jax.numpy as jnp
from jax import lax
from jax.experimental import pallas as pl
from jax.experimental.pallas import tpu as pltpu
from jax.sharding import PartitionSpec as P

STEP_COUNT = 2


PRECISE = lax.Precision.HIGHEST
TIME_STEP = 0.4
DIFFUSION = 0.1
COUPLING = 0.3
DAMPING = 0.1


def shifted(value, axis, by):
    peers = lax.axis_size(axis)
    return lax.ppermute(value, axis, [(i, (i + by) % peers) for i in range(peers)])


def halo(value):
    peers = lax.axis_size("mesh")
    me = lax.axis_index("mesh")
    before = shifted(value[..., -1:], "mesh", 1)
    after = shifted(value[..., :1], "mesh", -1)
    before = jnp.where(me > 0, before, jnp.zeros_like(before))
    after = jnp.where(me < peers - 1, after, jnp.zeros_like(after))
    return before, after


def mesh_sum(value):
    peers = lax.axis_size("mesh")
    if peers & (peers - 1):
        return lax.psum(value, "mesh")
    step = 1
    while step < peers:
        value = value + lax.ppermute(value, "mesh", [(i, i ^ step) for i in range(peers)])
        step *= 2
    return value


def pick_rows(table, index, count):
    slots = table.shape[0]
    slot = jnp.arange(slots, dtype=jnp.int32).reshape((slots,) + (1,) * (table.ndim - 1))
    rows = []
    for s in range(count):
        hit = slot == (index + s) % slots
        rows.append(jnp.sum(jnp.where(hit, table, jnp.zeros_like(table)), axis=0))
    return jnp.stack(rows)


def pick_entry(values, index):
    hit = jnp.arange(values.shape[0], dtype=jnp.int32) == index
    return jnp.sum(jnp.where(hit, values, jnp.zeros_like(values)))


def axial_pad(value, before, after):
    return jnp.concatenate([before, value, after], axis=-1)


def pitch_pad(value, lower, upper):
    return jnp.concatenate([lower[:, None, :], value, upper[:, None, :]], axis=1)


def flow_rate(state, before, after, lower_ghost, upper_ghost, axial_jacobian, pitch_jacobian):
    padded_axial = axial_pad(state, before, after)
    padded_pitch = pitch_pad(state, lower_ghost, upper_ghost)
    grad_axial = 0.5 * (padded_axial[:, :, 2:] - padded_axial[:, :, :-2])
    grad_pitch = 0.5 * (padded_pitch[:, 2:, :] - padded_pitch[:, :-2, :])
    laplacian = (
        padded_axial[:, :, 2:]
        + padded_axial[:, :, :-2]
        + padded_pitch[:, 2:, :]
        + padded_pitch[:, :-2, :]
        - 4.0 * state
    )
    flux = jnp.einsum("ij,jpx->ipx", axial_jacobian, grad_axial, precision=PRECISE)
    flux = flux + jnp.einsum("ij,jpx->ipx", pitch_jacobian, grad_pitch, precision=PRECISE)
    return DIFFUSION * laplacian - flux


def single_field_grads(field, before, after):
    padded_axial = jnp.concatenate([before, field, after], axis=-1)
    zero_row = jnp.zeros_like(field[..., :1, :])
    padded_pitch = jnp.concatenate([zero_row, field, zero_row], axis=-2)
    grad_axial = 0.5 * (padded_axial[..., 2:] - padded_axial[..., :-2])
    grad_pitch = 0.5 * (padded_pitch[..., 2:, :] - padded_pitch[..., :-2, :])
    laplacian = (
        padded_axial[..., 2:]
        + padded_axial[..., :-2]
        + padded_pitch[..., 2:, :]
        + padded_pitch[..., :-2, :]
        - 4.0 * field
    )
    return grad_axial, grad_pitch, laplacian


def modal_field(weights, mode_shape):
    return jnp.einsum("m,mpx->px", weights, mode_shape, precision=PRECISE)


def projection(mode_shape, field):
    return jnp.einsum("mpx,px->m", mode_shape, field, precision=PRECISE)


def add_field_one(rate, extra):
    return rate.at[1].add(extra)


def rate_field4(state, lower_ghost, upper_ghost, axial_jacobian, pitch_jacobian):
    zero_col = jnp.zeros_like(state[..., :1])
    padded_axial = jnp.concatenate([zero_col, state, zero_col], axis=-1)
    padded_pitch = pitch_pad(state, lower_ghost, upper_ghost)
    grad_axial = 0.5 * (padded_axial[:, :, 2:] - padded_axial[:, :, :-2])
    grad_pitch = 0.5 * (padded_pitch[:, 2:, :] - padded_pitch[:, :-2, :])
    laplacian = (
        padded_axial[4, :, 2:]
        + padded_axial[4, :, :-2]
        + padded_pitch[4, 2:, :]
        + padded_pitch[4, :-2, :]
        - 4.0 * state[4]
    )
    flux = jnp.einsum("j,jpx->px", axial_jacobian[4], grad_axial, precision=PRECISE)
    flux = flux + jnp.einsum("j,jpx->px", pitch_jacobian[4], grad_pitch, precision=PRECISE)
    return DIFFUSION * laplacian - flux


def pack(parts, width):
    flat = [jnp.moveaxis(part, -1, 0).reshape(width, -1) for part in parts]
    return jnp.concatenate(flat, axis=1)


def unpack(buffer, shapes):
    out, offset = [], 0
    for shape in shapes:
        count = math.prod(shape[:-1])
        out.append(buffer[offset : offset + count].reshape(shape))
        offset += count
    return out


LANES = 128


def lane_roll(x, shift):
    return pltpu.roll(x, shift % x.shape[-1], x.ndim - 1)


def row_roll(x, shift):
    return pltpu.roll(x, shift % x.shape[0], 0)


def pitch_neighbours(s, lower, upper):
    rows = s.shape[0]
    tile = 8
    edge = lax.broadcasted_iota(jnp.int32, (tile,) + s.shape[1:], 0)
    north = row_roll(s, -1)
    south = row_roll(s, 1)
    north = jnp.concatenate(
        [north[: rows - tile], jnp.where(edge == tile - 1, upper, north[rows - tile :])], axis=0
    )
    south = jnp.concatenate([jnp.where(edge == 0, lower, south[:tile]), south[tile:]], axis=0)
    return north, south


def masked(r, inside):
    cut = r.shape[-1] - LANES
    return jnp.concatenate([r[:, :cut], r[:, cut:] * inside[:, cut:]], axis=1)


def kernel_rate(state, lower, upper, jac, push, inside, fields_out):
    ax, pt = jac
    diffs_a, diffs_p, laps = [], [], []
    for j, s in enumerate(state):
        east = lane_roll(s, -1)
        west = lane_roll(s, 1)
        north, south = pitch_neighbours(s, lower[j], upper[j])
        diffs_a.append(east - west)
        diffs_p.append(north - south)
        laps.append((east + west) + (north + south) - 4.0 * s)
    out = []
    for i in fields_out:
        r = DIFFUSION * laps[i]
        for j in range(len(state)):
            r = r - (0.5 * ax[i][j]) * diffs_a[j] - (0.5 * pt[i][j]) * diffs_p[j]
        if i == 1 and push is not None:
            r = r + push
        out.append(masked(r, inside))
    return out


def read_jacobians(ax_ref, pt_ref, fields):
    ax = [[ax_ref[i, j] for j in range(fields)] for i in range(fields)]
    pt = [[pt_ref[i, j] for j in range(fields)] for i in range(fields)]
    return ax, pt


def lane_fold(x):
    x = jnp.sum(x, axis=0, keepdims=True)
    total = x[:, :LANES]
    for t in range(1, x.shape[1] // LANES):
        total = total + x[:, t * LANES : (t + 1) * LANES]
    return total


def pick_kernel(peers, lower_slot_ref, upper_slot_ref, upper_hist_ref, lower_hist_ref, up_ref, down_ref):
    fields, slots = upper_hist_ref.shape[0], upper_hist_ref.shape[1]
    position = lax.axis_index("blk")
    slot_next = lower_slot_ref[(position + 1) % peers]
    slot_prev = upper_slot_ref[(position + peers - 1) % peers]
    for s in range(up_ref.shape[0]):
        up_at = (slot_next + s) % slots
        down_at = (slot_prev + s) % slots
        for f in range(fields):
            up_ref[s, f : f + 1, :] = upper_hist_ref[f, pl.ds(up_at, 1), :]
            down_ref[s, f : f + 1, :] = lower_hist_ref[f, pl.ds(down_at, 1), :]


def widened(own, tile):
    return jnp.concatenate([own, lane_roll(tile, -2 * STEP_COUNT)], axis=-1)


def unfold_halo(halo_ref, columns_ref):
    block = halo_ref[...]
    spare = jnp.zeros((LANES - block.shape[0], block.shape[1]), block.dtype)
    columns_ref[...] = jnp.concatenate([block, spare], axis=0).T


def lane_masks(peers, shape, own_width):
    reach = 2 * STEP_COUNT
    me = lax.axis_index("mesh")
    lane = lax.broadcasted_iota(jnp.int32, shape, len(shape) - 1)
    width = shape[-1]
    right_ok = (lane >= own_width) & (lane < own_width + reach) & (me < peers - 1)
    left_ok = (lane >= width - reach) & (me > 0)
    owned = lane < own_width
    inside = owned | right_ok | left_ok
    return inside.astype(jnp.float32), owned.astype(jnp.float32)


def assemble(u_ref, ms_ref, glo_ref, gup_ref, halo_ref, fields, modes, pitch):
    u = []
    for j in range(fields if u_ref is not None else 0):
        rows = slice(j * pitch, (j + 1) * pitch)
        u.append(widened(u_ref[j], halo_ref[rows, :]))
    ms = []
    for m in range(modes):
        rows = slice((fields + m) * pitch, (fields + m + 1) * pitch)
        ms.append(widened(ms_ref[m], halo_ref[rows, :]))
    base = (fields + modes) * pitch
    steps = glo_ref.shape[0]
    ghosts = []
    for side, ref in enumerate((glo_ref, gup_ref)):
        per_step = []
        for s in range(steps):
            start = base + (side * steps + s) * fields
            rows = slice(start, start + fields)
            block = widened(ref[s], halo_ref[rows, :])
            per_step.append([block[j : j + 1, :] for j in range(fields)])
        ghosts.append(per_step)
    return u, ms, ghosts[0], ghosts[1]


def first_kernel(peers, ax_ref, pt_ref, vel_ref, u_ref, ms_ref, glo_ref, gup_ref, packed_ref, a_ref, part_ref, halo_ref):
    h = TIME_STEP
    unfold_halo(packed_ref, halo_ref)
    fields = u_ref.shape[0]
    modes = ms_ref.shape[0]
    pitch = u_ref.shape[1]
    jac = read_jacobians(ax_ref, pt_ref, fields)
    vel = [vel_ref[0, m] for m in range(modes)]
    u0, ms, gl, gu = assemble(u_ref, ms_ref, glo_ref, gup_ref, halo_ref, fields, modes, pitch)
    inside, _ = lane_masks(peers, u0[0].shape, u_ref.shape[-1])
    push = vel[0] * ms[0]
    for m in range(1, modes):
        push = push + vel[m] * ms[m]
    push = COUPLING * push
    gl1, gu1, gl2, gu2 = gl[0], gu[0], gl[1], gu[1]
    every = list(range(fields))
    k1 = kernel_rate(u0, gl1, gu1, jac, push, inside, every)
    mid = [u0[j] + h * k1[j] for j in every]
    k2 = kernel_rate(mid, gl1, gu1, jac, push, inside, every)
    a = [u0[j] + 0.5 * h * (k1[j] + k2[j]) for j in every]
    for j in every:
        a_ref[j] = a[j]
    (ra4,) = kernel_rate(a, gl2, gu2, jac, None, inside, [4])
    own = u_ref.shape[-1]
    weighted = [ms_ref[m] for m in range(modes)]
    k = 0
    for field in (u0[4], mid[4], a[4], ra4):
        field = field[:, :own]
        for m in range(modes):
            part_ref[k : k + 1, :] = lane_fold(weighted[m] * field)
            k += 1
    ax41, pt41 = 0.5 * jac[0][4][1], 0.5 * jac[1][4][1]
    no_ghost = jnp.zeros((1, ms[0].shape[1]), ms[0].dtype)
    for n in range(modes):
        s = ms[n]
        north, south = pitch_neighbours(s, no_ghost, no_ghost)
        t = -(ax41 * (lane_roll(s, -1) - lane_roll(s, 1)) + pt41 * (north - south))
        t = t[:, :own]
        for m in range(modes):
            part_ref[k + m * modes + n : k + m * modes + n + 1, :] = lane_fold(weighted[m] * t)


def modal_steps(force_scale, tot_ref, stiff_ref, disp_ref, vel_ref, modes):
    h = TIME_STEP
    t = [force_scale * tot_ref[k] for k in range(4 * modes + modes * modes)]
    force = [t[w * modes : (w + 1) * modes] for w in range(4)]
    couple = [t[4 * modes + m * modes : 4 * modes + (m + 1) * modes] for m in range(modes)]
    stiff = [stiff_ref[0, m] for m in range(modes)]
    disp0 = [disp_ref[0, m] for m in range(modes)]
    vel0 = [vel_ref[0, m] for m in range(modes)]

    def accel(f, q, v):
        return [f[m] - stiff[m] * q[m] - DAMPING * v[m] for m in range(modes)]

    def axpy(x, a, y):
        return [x[m] + a * y[m] for m in range(modes)]

    acc1 = accel(force[0], disp0, vel0)
    disp1m = axpy(disp0, h, vel0)
    vel1m = axpy(vel0, h, acc1)
    acc1m = accel(force[1], disp1m, vel1m)
    disp1 = [disp0[m] + 0.5 * h * (vel0[m] + vel1m[m]) for m in range(modes)]
    vel1 = [vel0[m] + 0.5 * h * (acc1[m] + acc1m[m]) for m in range(modes)]
    acc2 = accel(force[2], disp1, vel1)
    disp2m = axpy(disp1, h, vel1)
    vel2m = axpy(vel1, h, acc2)
    corr = 0.5 * h * h * COUPLING
    force2m = []
    for m in range(modes):
        coupled = couple[m][0] * acc1[0]
        for n in range(1, modes):
            coupled = coupled + couple[m][n] * acc1[n]
        force2m.append(force[2][m] + h * force[3][m] + h * corr * coupled)
    acc2m = accel(force2m, disp2m, vel2m)
    disp2 = [disp1[m] + 0.5 * h * (vel1[m] + vel2m[m]) for m in range(modes)]
    vel2 = [vel1[m] + 0.5 * h * (acc2[m] + acc2m[m]) for m in range(modes)]
    coef = [[corr * acc1[m] for m in range(modes)], vel1, vel2m]
    return coef, disp2, vel2


def step2_rate_kernel(peers, ax_ref, pt_ref, a_ref, ms_ref, glo_ref, gup_ref, packed_ref, ra_ref, halo_ref):
    unfold_halo(packed_ref, halo_ref)
    fields = a_ref.shape[0]
    modes = ms_ref.shape[0]
    pitch = ms_ref.shape[1]
    jac = read_jacobians(ax_ref, pt_ref, fields)
    _, ms, gl, gu = assemble(None, ms_ref, glo_ref, gup_ref, halo_ref, fields, modes, pitch)
    inside, _ = lane_masks(peers, ms[0].shape, ms_ref.shape[-1])
    every = list(range(fields))
    a = [a_ref[j] for j in every]
    ra = kernel_rate(a, gl[1], gu[1], jac, None, inside, every)
    for j in every:
        ra_ref[j] = ra[j]


def second_kernel(
    peers,
    force_scale,
    tot_ref,
    stiff_ref,
    disp_ref,
    vel_ref,
    ax_ref,
    pt_ref,
    a_ref,
    ra_ref,
    ms_ref,
    glo_ref,
    gup_ref,
    packed_ref,
    out_ref,
    disp_out_ref,
    vel_out_ref,
    halo_ref,
):
    h = TIME_STEP
    unfold_halo(packed_ref, halo_ref)
    fields = a_ref.shape[0]
    modes = ms_ref.shape[0]
    pitch = ms_ref.shape[1]
    jac = read_jacobians(ax_ref, pt_ref, fields)
    coef, disp2, vel2 = modal_steps(force_scale, tot_ref, stiff_ref, disp_ref, vel_ref, modes)
    for m in range(modes):
        disp_out_ref[0, m] = disp2[m]
        vel_out_ref[0, m] = vel2[m]
    _, ms, gl, gu = assemble(None, ms_ref, glo_ref, gup_ref, halo_ref, fields, modes, pitch)
    inside, _ = lane_masks(peers, ms[0].shape, ms_ref.shape[-1])

    def combine(weights):
        total = weights[0] * ms[0]
        for m in range(1, modes):
            total = total + weights[m] * ms[m]
        return total

    gl2, gu2 = gl[1], gu[1]
    every = list(range(fields))
    s1 = [a_ref[j] for j in every]
    correction = combine(coef[0])
    s1[1] = s1[1] + correction
    rows = correction.shape[0]
    row = lax.broadcasted_iota(jnp.int32, correction.shape, 0)
    east, west = lane_roll(correction, -1), lane_roll(correction, 1)
    north = jnp.where(row == rows - 1, 0.0, row_roll(correction, -1))
    south = jnp.where(row == 0, 0.0, row_roll(correction, 1))
    ga = 0.5 * (east - west)
    gp = 0.5 * (north - south)
    lap = east + west + north + south - 4.0 * correction
    ax, pt = jac
    push1 = COUPLING * combine(coef[1])
    k1 = []
    for i in every:
        r = -ax[i][1] * ga - pt[i][1] * gp
        if i == 1:
            r = r + DIFFUSION * lap + push1
        k1.append(ra_ref[i] + masked(r, inside))
    mid = [s1[j] + h * k1[j] for j in every]
    k2 = kernel_rate(mid, gl2, gu2, jac, COUPLING * combine(coef[2]), inside, every)
    width = out_ref.shape[-1]
    for j in every:
        s2 = s1[j] + 0.5 * h * (k1[j] + k2[j])
        out_ref[j] = s2[:, :width]


def vmem_spec():
    return pl.BlockSpec(memory_space=pltpu.VMEM)


def smem_spec():
    return pl.BlockSpec(memory_space=pltpu.SMEM)


def on_device(
    flow_field,
    lower_row_history,
    upper_row_history,
    lower_lag_slot,
    upper_lag_slot,
    axial_jacobian,
    pitch_jacobian,
    mode_shape,
    stiffness,
    displacement,
    velocity,
):
    h = TIME_STEP
    state0 = flow_field[0]
    fields, pitch_cells, axial_cells = state0.shape
    modes = mode_shape.shape[0]
    mesh_peers = lax.axis_size("mesh")
    me = lax.axis_index("mesh")
    force_scale = 1.0 / math.sqrt(pitch_cells * axial_cells * mesh_peers)
    passages = lax.axis_size("blk")
    position = lax.axis_index("blk")
    blade_stiffness = stiffness[0]
    disp0 = displacement[0]
    vel0 = velocity[0]

    row_shape = jax.ShapeDtypeStruct((STEP_COUNT,) + upper_row_history.shape[2:], state0.dtype)
    rows_up, rows_down = pl.pallas_call(
        functools.partial(pick_kernel, passages),
        out_shape=(row_shape, row_shape),
        in_specs=[smem_spec(), smem_spec(), vmem_spec(), vmem_spec()],
        out_specs=(vmem_spec(), vmem_spec()),
    )(
        lower_lag_slot,
        upper_lag_slot,
        jnp.transpose(upper_row_history[0], (1, 0, 2)),
        jnp.transpose(lower_row_history[0], (1, 0, 2)),
    )
    lower_ghosts = shifted(rows_up, "blk", 1)
    upper_ghosts = shifted(rows_down, "blk", -1)

    reach = 2 * STEP_COUNT
    own = [state0, mode_shape, lower_ghosts, upper_ghosts]
    shapes = [part.shape[:-1] + (reach,) for part in own]
    from_left = shifted(pack([part[..., -reach:] for part in own], reach).reshape(-1), "mesh", 1)
    from_right = shifted(pack([part[..., :reach] for part in own], reach).reshape(-1), "mesh", -1)
    from_left = from_left.reshape(reach, -1)
    from_right = from_right.reshape(reach, -1)
    from_left = jnp.where(me > 0, from_left, jnp.zeros_like(from_left))
    from_right = jnp.where(me < mesh_peers - 1, from_right, jnp.zeros_like(from_right))
    packed_rows = from_left.shape[1]
    padded_rows = -(-packed_rows // LANES) * LANES
    halo_tile = jnp.pad(
        jnp.concatenate([from_left, from_right], axis=0), [(0, 0), (0, padded_rows - packed_rows)]
    )
    columns = [pltpu.VMEM((padded_rows, LANES), state0.dtype)]
    lanes_wide = axial_cells + LANES
    ins = (state0, mode_shape, lower_ghosts, upper_ghosts, halo_tile)

    base1, part_lanes = pl.pallas_call(
        functools.partial(first_kernel, mesh_peers),
        out_shape=(
            jax.ShapeDtypeStruct((fields, pitch_cells, lanes_wide), state0.dtype),
            jax.ShapeDtypeStruct((4 * modes + modes * modes, LANES), state0.dtype),
        ),
        in_specs=[smem_spec()] * 3 + [vmem_spec()] * 5,
        out_specs=(vmem_spec(), vmem_spec()),
        scratch_shapes=columns,
    )(axial_jacobian, pitch_jacobian, velocity, *ins)

    totals = mesh_sum(jnp.sum(part_lanes, axis=1))

    rate_a = pl.pallas_call(
        functools.partial(step2_rate_kernel, mesh_peers),
        out_shape=jax.ShapeDtypeStruct(base1.shape, base1.dtype),
        in_specs=[smem_spec()] * 2 + [vmem_spec()] * 5,
        out_specs=vmem_spec(),
        scratch_shapes=columns,
    )(axial_jacobian, pitch_jacobian, base1, *ins[1:])

    small = jax.ShapeDtypeStruct(displacement.shape, displacement.dtype)
    state2, disp2, vel2 = pl.pallas_call(
        functools.partial(second_kernel, mesh_peers, force_scale),
        out_shape=(jax.ShapeDtypeStruct(state0.shape, state0.dtype), small, small),
        in_specs=[smem_spec()] * 6 + [vmem_spec()] * 6,
        out_specs=(vmem_spec(), smem_spec(), smem_spec()),
        scratch_shapes=columns,
    )(totals, stiffness, displacement, velocity, axial_jacobian, pitch_jacobian, base1, rate_a, *ins[1:])
    return (state2[None], disp2, vel2)


def solution(mesh):
    return jax.shard_map(
        on_device,
        mesh=mesh,
        in_specs=(
            P("blk", None, None, "mesh"),
            P("blk", None, None, "mesh"),
            P("blk", None, None, "mesh"),
            P(),
            P(),
            P(),
            P(),
            P(None, None, "mesh"),
            P("blk", None),
            P("blk", None),
            P("blk", None),
        ),
        out_specs=(P("blk", None, None, "mesh"), P("blk", None), P("blk", None)),
        check_vma=False,
    )
```

```python
import functools
import math

import jax
import jax.numpy as jnp
from jax import lax
from jax.experimental import pallas as pl
from jax.experimental.pallas import tpu as pltpu
from jax.sharding import PartitionSpec as P

STEP_COUNT = 2


PRECISE = lax.Precision.HIGHEST
TIME_STEP = 0.4
DIFFUSION = 0.1
COUPLING = 0.3
DAMPING = 0.1


def shifted(value, axis, by):
    peers = lax.axis_size(axis)
    return lax.ppermute(value, axis, [(i, (i + by) % peers) for i in range(peers)])


def halo(value):
    peers = lax.axis_size("mesh")
    me = lax.axis_index("mesh")
    before = shifted(value[..., -1:], "mesh", 1)
    after = shifted(value[..., :1], "mesh", -1)
    before = jnp.where(me > 0, before, jnp.zeros_like(before))
    after = jnp.where(me < peers - 1, after, jnp.zeros_like(after))
    return before, after


def mesh_sum(value):
    peers = lax.axis_size("mesh")
    if peers & (peers - 1):
        return lax.psum(value, "mesh")
    step = 1
    while step < peers:
        value = value + lax.ppermute(value, "mesh", [(i, i ^ step) for i in range(peers)])
        step *= 2
    return value


def pick_rows(table, index, count):
    slots = table.shape[0]
    slot = jnp.arange(slots, dtype=jnp.int32).reshape((slots,) + (1,) * (table.ndim - 1))
    rows = []
    for s in range(count):
        hit = slot == (index + s) % slots
        rows.append(jnp.sum(jnp.where(hit, table, jnp.zeros_like(table)), axis=0))
    return jnp.stack(rows)


def pick_entry(values, index):
    hit = jnp.arange(values.shape[0], dtype=jnp.int32) == index
    return jnp.sum(jnp.where(hit, values, jnp.zeros_like(values)))


def axial_pad(value, before, after):
    return jnp.concatenate([before, value, after], axis=-1)


def pitch_pad(value, lower, upper):
    return jnp.concatenate([lower[:, None, :], value, upper[:, None, :]], axis=1)


def flow_rate(state, before, after, lower_ghost, upper_ghost, axial_jacobian, pitch_jacobian):
    padded_axial = axial_pad(state, before, after)
    padded_pitch = pitch_pad(state, lower_ghost, upper_ghost)
    grad_axial = 0.5 * (padded_axial[:, :, 2:] - padded_axial[:, :, :-2])
    grad_pitch = 0.5 * (padded_pitch[:, 2:, :] - padded_pitch[:, :-2, :])
    laplacian = (
        padded_axial[:, :, 2:]
        + padded_axial[:, :, :-2]
        + padded_pitch[:, 2:, :]
        + padded_pitch[:, :-2, :]
        - 4.0 * state
    )
    flux = jnp.einsum("ij,jpx->ipx", axial_jacobian, grad_axial, precision=PRECISE)
    flux = flux + jnp.einsum("ij,jpx->ipx", pitch_jacobian, grad_pitch, precision=PRECISE)
    return DIFFUSION * laplacian - flux


def single_field_grads(field, before, after):
    padded_axial = jnp.concatenate([before, field, after], axis=-1)
    zero_row = jnp.zeros_like(field[..., :1, :])
    padded_pitch = jnp.concatenate([zero_row, field, zero_row], axis=-2)
    grad_axial = 0.5 * (padded_axial[..., 2:] - padded_axial[..., :-2])
    grad_pitch = 0.5 * (padded_pitch[..., 2:, :] - padded_pitch[..., :-2, :])
    laplacian = (
        padded_axial[..., 2:]
        + padded_axial[..., :-2]
        + padded_pitch[..., 2:, :]
        + padded_pitch[..., :-2, :]
        - 4.0 * field
    )
    return grad_axial, grad_pitch, laplacian


def modal_field(weights, mode_shape):
    return jnp.einsum("m,mpx->px", weights, mode_shape, precision=PRECISE)


def projection(mode_shape, field):
    return jnp.einsum("mpx,px->m", mode_shape, field, precision=PRECISE)


def add_field_one(rate, extra):
    return rate.at[1].add(extra)


def rate_field4(state, lower_ghost, upper_ghost, axial_jacobian, pitch_jacobian):
    zero_col = jnp.zeros_like(state[..., :1])
    padded_axial = jnp.concatenate([zero_col, state, zero_col], axis=-1)
    padded_pitch = pitch_pad(state, lower_ghost, upper_ghost)
    grad_axial = 0.5 * (padded_axial[:, :, 2:] - padded_axial[:, :, :-2])
    grad_pitch = 0.5 * (padded_pitch[:, 2:, :] - padded_pitch[:, :-2, :])
    laplacian = (
        padded_axial[4, :, 2:]
        + padded_axial[4, :, :-2]
        + padded_pitch[4, 2:, :]
        + padded_pitch[4, :-2, :]
        - 4.0 * state[4]
    )
    flux = jnp.einsum("j,jpx->px", axial_jacobian[4], grad_axial, precision=PRECISE)
    flux = flux + jnp.einsum("j,jpx->px", pitch_jacobian[4], grad_pitch, precision=PRECISE)
    return DIFFUSION * laplacian - flux


def pack(parts, width):
    flat = [jnp.moveaxis(part, -1, 0).reshape(width, -1) for part in parts]
    return jnp.concatenate(flat, axis=1)


def unpack(buffer, shapes):
    out, offset = [], 0
    for shape in shapes:
        count = math.prod(shape[:-1])
        out.append(buffer[offset : offset + count].reshape(shape))
        offset += count
    return out


LANES = 128


def lane_roll(x, shift):
    return pltpu.roll(x, shift % x.shape[-1], x.ndim - 1)


def row_roll(x, shift):
    return pltpu.roll(x, shift % x.shape[0], 0)


def pitch_neighbours(s, lower, upper):
    rows = s.shape[0]
    tile = 8
    edge = lax.broadcasted_iota(jnp.int32, (tile,) + s.shape[1:], 0)
    north = row_roll(s, -1)
    south = row_roll(s, 1)
    north = jnp.concatenate(
        [north[: rows - tile], jnp.where(edge == tile - 1, upper, north[rows - tile :])], axis=0
    )
    south = jnp.concatenate([jnp.where(edge == 0, lower, south[:tile]), south[tile:]], axis=0)
    return north, south


def masked(r, inside):
    cut = r.shape[-1] - LANES
    return jnp.concatenate([r[:, :cut], r[:, cut:] * inside[:, cut:]], axis=1)


def kernel_rate(state, lower, upper, jac, push, inside, fields_out):
    ax, pt = jac
    diffs_a, diffs_p, laps = [], [], []
    for j, s in enumerate(state):
        east = lane_roll(s, -1)
        west = lane_roll(s, 1)
        north, south = pitch_neighbours(s, lower[j], upper[j])
        diffs_a.append(east - west)
        diffs_p.append(north - south)
        laps.append((east + west) + (north + south) - 4.0 * s)
    out = []
    for i in fields_out:
        r = DIFFUSION * laps[i]
        for j in range(len(state)):
            r = r - (0.5 * ax[i][j]) * diffs_a[j] - (0.5 * pt[i][j]) * diffs_p[j]
        if i == 1 and push is not None:
            r = r + push
        out.append(masked(r, inside))
    return out


def read_jacobians(ax_ref, pt_ref, fields):
    ax = [[ax_ref[i, j] for j in range(fields)] for i in range(fields)]
    pt = [[pt_ref[i, j] for j in range(fields)] for i in range(fields)]
    return ax, pt


def lane_fold(x):
    x = jnp.sum(x, axis=0, keepdims=True)
    total = x[:, :LANES]
    for t in range(1, x.shape[1] // LANES):
        total = total + x[:, t * LANES : (t + 1) * LANES]
    return total


def pick_kernel(peers, lower_slot_ref, upper_slot_ref, upper_hist_ref, lower_hist_ref, up_ref, down_ref, sems):
    fields, slots = upper_hist_ref.shape[0], upper_hist_ref.shape[1]
    position = lax.axis_index("blk")
    slot_next = lower_slot_ref[(position + 1) % peers]
    slot_prev = upper_slot_ref[(position + peers - 1) % peers]
    copies = []
    for s in range(up_ref.shape[0]):
        up_at = (slot_next + s) % slots
        down_at = (slot_prev + s) % slots
        for f in range(fields):
            for hist, at, out in ((upper_hist_ref, up_at, up_ref), (lower_hist_ref, down_at, down_ref)):
                copy = pltpu.make_async_copy(
                    hist.at[f, pl.ds(at, 1), :], out.at[s, pl.ds(f, 1), :], sems.at[len(copies)]
                )
                copy.start()
                copies.append(copy)
    for copy in copies:
        copy.wait()


def widened(own, tile):
    return jnp.concatenate([own, lane_roll(tile, -2 * STEP_COUNT)], axis=-1)


def unfold_halo(halo_ref, columns_ref):
    block = halo_ref[...]
    spare = jnp.zeros((LANES - block.shape[0], block.shape[1]), block.dtype)
    columns_ref[...] = jnp.concatenate([block, spare], axis=0).T


def lane_masks(peers, shape, own_width):
    reach = 2 * STEP_COUNT
    me = lax.axis_index("mesh")
    lane = lax.broadcasted_iota(jnp.int32, shape, len(shape) - 1)
    width = shape[-1]
    right_ok = (lane >= own_width) & (lane < own_width + reach) & (me < peers - 1)
    left_ok = (lane >= width - reach) & (me > 0)
    owned = lane < own_width
    inside = owned | right_ok | left_ok
    return inside.astype(jnp.float32), owned.astype(jnp.float32)


def assemble(u_ref, ms_ref, glo_ref, gup_ref, halo_ref, fields, modes, pitch):
    u = []
    for j in range(fields if u_ref is not None else 0):
        rows = slice(j * pitch, (j + 1) * pitch)
        u.append(widened(u_ref[j], halo_ref[rows, :]))
    ms = []
    for m in range(modes):
        rows = slice((fields + m) * pitch, (fields + m + 1) * pitch)
        ms.append(widened(ms_ref[m], halo_ref[rows, :]))
    base = (fields + modes) * pitch
    steps = glo_ref.shape[0]
    ghosts = []
    for side, ref in enumerate((glo_ref, gup_ref)):
        per_step = []
        for s in range(steps):
            start = base + (side * steps + s) * fields
            rows = slice(start, start + fields)
            block = widened(ref[s], halo_ref[rows, :])
            per_step.append([block[j : j + 1, :] for j in range(fields)])
        ghosts.append(per_step)
    return u, ms, ghosts[0], ghosts[1]


def first_kernel(peers, ax_ref, pt_ref, vel_ref, u_ref, ms_ref, glo_ref, gup_ref, packed_ref, a_ref, part_ref, halo_ref):
    h = TIME_STEP
    unfold_halo(packed_ref, halo_ref)
    fields = u_ref.shape[0]
    modes = ms_ref.shape[0]
    pitch = u_ref.shape[1]
    jac = read_jacobians(ax_ref, pt_ref, fields)
    vel = [vel_ref[0, m] for m in range(modes)]
    u0, ms, gl, gu = assemble(u_ref, ms_ref, glo_ref, gup_ref, halo_ref, fields, modes, pitch)
    inside, _ = lane_masks(peers, u0[0].shape, u_ref.shape[-1])
    push = vel[0] * ms[0]
    for m in range(1, modes):
        push = push + vel[m] * ms[m]
    push = COUPLING * push
    gl1, gu1, gl2, gu2 = gl[0], gu[0], gl[1], gu[1]
    every = list(range(fields))
    k1 = kernel_rate(u0, gl1, gu1, jac, push, inside, every)
    mid = [u0[j] + h * k1[j] for j in every]
    k2 = kernel_rate(mid, gl1, gu1, jac, push, inside, every)
    a = [u0[j] + 0.5 * h * (k1[j] + k2[j]) for j in every]
    for j in every:
        a_ref[j] = a[j]
    (ra4,) = kernel_rate(a, gl2, gu2, jac, None, inside, [4])
    own = u_ref.shape[-1]
    weighted = [ms_ref[m] for m in range(modes)]
    k = 0
    for field in (u0[4], mid[4], a[4], ra4):
        field = field[:, :own]
        for m in range(modes):
            part_ref[k : k + 1, :] = lane_fold(weighted[m] * field)
            k += 1
    ax41, pt41 = 0.5 * jac[0][4][1], 0.5 * jac[1][4][1]
    no_ghost = jnp.zeros((1, ms[0].shape[1]), ms[0].dtype)
    for n in range(modes):
        s = ms[n]
        north, south = pitch_neighbours(s, no_ghost, no_ghost)
        t = -(ax41 * (lane_roll(s, -1) - lane_roll(s, 1)) + pt41 * (north - south))
        t = t[:, :own]
        for m in range(modes):
            part_ref[k + m * modes + n : k + m * modes + n + 1, :] = lane_fold(weighted[m] * t)


def modal_steps(force_scale, tot_ref, stiff_ref, disp_ref, vel_ref, modes):
    h = TIME_STEP
    t = [force_scale * tot_ref[k] for k in range(4 * modes + modes * modes)]
    force = [t[w * modes : (w + 1) * modes] for w in range(4)]
    couple = [t[4 * modes + m * modes : 4 * modes + (m + 1) * modes] for m in range(modes)]
    stiff = [stiff_ref[0, m] for m in range(modes)]
    disp0 = [disp_ref[0, m] for m in range(modes)]
    vel0 = [vel_ref[0, m] for m in range(modes)]

    def accel(f, q, v):
        return [f[m] - stiff[m] * q[m] - DAMPING * v[m] for m in range(modes)]

    def axpy(x, a, y):
        return [x[m] + a * y[m] for m in range(modes)]

    acc1 = accel(force[0], disp0, vel0)
    disp1m = axpy(disp0, h, vel0)
    vel1m = axpy(vel0, h, acc1)
    acc1m = accel(force[1], disp1m, vel1m)
    disp1 = [disp0[m] + 0.5 * h * (vel0[m] + vel1m[m]) for m in range(modes)]
    vel1 = [vel0[m] + 0.5 * h * (acc1[m] + acc1m[m]) for m in range(modes)]
    acc2 = accel(force[2], disp1, vel1)
    disp2m = axpy(disp1, h, vel1)
    vel2m = axpy(vel1, h, acc2)
    corr = 0.5 * h * h * COUPLING
    force2m = []
    for m in range(modes):
        coupled = couple[m][0] * acc1[0]
        for n in range(1, modes):
            coupled = coupled + couple[m][n] * acc1[n]
        force2m.append(force[2][m] + h * force[3][m] + h * corr * coupled)
    acc2m = accel(force2m, disp2m, vel2m)
    disp2 = [disp1[m] + 0.5 * h * (vel1[m] + vel2m[m]) for m in range(modes)]
    vel2 = [vel1[m] + 0.5 * h * (acc2[m] + acc2m[m]) for m in range(modes)]
    coef = [[corr * acc1[m] for m in range(modes)], vel1, vel2m]
    return coef, disp2, vel2


def step2_rate_kernel(peers, ax_ref, pt_ref, a_ref, ms_ref, glo_ref, gup_ref, packed_ref, ra_ref, halo_ref):
    unfold_halo(packed_ref, halo_ref)
    fields = a_ref.shape[0]
    modes = ms_ref.shape[0]
    pitch = ms_ref.shape[1]
    jac = read_jacobians(ax_ref, pt_ref, fields)
    _, ms, gl, gu = assemble(None, ms_ref, glo_ref, gup_ref, halo_ref, fields, modes, pitch)
    inside, _ = lane_masks(peers, ms[0].shape, ms_ref.shape[-1])
    every = list(range(fields))
    a = [a_ref[j] for j in every]
    ra = kernel_rate(a, gl[1], gu[1], jac, None, inside, every)
    for j in every:
        ra_ref[j] = ra[j]


def second_kernel(
    peers,
    force_scale,
    tot_ref,
    stiff_ref,
    disp_ref,
    vel_ref,
    ax_ref,
    pt_ref,
    a_ref,
    ra_ref,
    ms_ref,
    glo_ref,
    gup_ref,
    packed_ref,
    out_ref,
    disp_out_ref,
    vel_out_ref,
    halo_ref,
):
    h = TIME_STEP
    unfold_halo(packed_ref, halo_ref)
    fields = a_ref.shape[0]
    modes = ms_ref.shape[0]
    pitch = ms_ref.shape[1]
    jac = read_jacobians(ax_ref, pt_ref, fields)
    coef, disp2, vel2 = modal_steps(force_scale, tot_ref, stiff_ref, disp_ref, vel_ref, modes)
    for m in range(modes):
        disp_out_ref[0, m] = disp2[m]
        vel_out_ref[0, m] = vel2[m]
    _, ms, gl, gu = assemble(None, ms_ref, glo_ref, gup_ref, halo_ref, fields, modes, pitch)
    inside, _ = lane_masks(peers, ms[0].shape, ms_ref.shape[-1])

    def combine(weights):
        total = weights[0] * ms[0]
        for m in range(1, modes):
            total = total + weights[m] * ms[m]
        return total

    gl2, gu2 = gl[1], gu[1]
    every = list(range(fields))
    s1 = [a_ref[j] for j in every]
    correction = combine(coef[0])
    s1[1] = s1[1] + correction
    rows = correction.shape[0]
    row = lax.broadcasted_iota(jnp.int32, correction.shape, 0)
    east, west = lane_roll(correction, -1), lane_roll(correction, 1)
    north = jnp.where(row == rows - 1, 0.0, row_roll(correction, -1))
    south = jnp.where(row == 0, 0.0, row_roll(correction, 1))
    ga = 0.5 * (east - west)
    gp = 0.5 * (north - south)
    lap = east + west + north + south - 4.0 * correction
    ax, pt = jac
    push1 = COUPLING * combine(coef[1])
    k1 = []
    for i in every:
        r = -ax[i][1] * ga - pt[i][1] * gp
        if i == 1:
            r = r + DIFFUSION * lap + push1
        k1.append(ra_ref[i] + masked(r, inside))
    mid = [s1[j] + h * k1[j] for j in every]
    k2 = kernel_rate(mid, gl2, gu2, jac, COUPLING * combine(coef[2]), inside, every)
    width = out_ref.shape[-1]
    for j in every:
        s2 = s1[j] + 0.5 * h * (k1[j] + k2[j])
        out_ref[j] = s2[:, :width]


def vmem_spec():
    return pl.BlockSpec(memory_space=pltpu.VMEM)


def any_spec():
    return pl.BlockSpec(memory_space=pl.ANY)


def smem_spec():
    return pl.BlockSpec(memory_space=pltpu.SMEM)


def on_device(
    flow_field,
    lower_row_history,
    upper_row_history,
    lower_lag_slot,
    upper_lag_slot,
    axial_jacobian,
    pitch_jacobian,
    mode_shape,
    stiffness,
    displacement,
    velocity,
):
    h = TIME_STEP
    state0 = flow_field[0]
    fields, pitch_cells, axial_cells = state0.shape
    modes = mode_shape.shape[0]
    mesh_peers = lax.axis_size("mesh")
    me = lax.axis_index("mesh")
    force_scale = 1.0 / math.sqrt(pitch_cells * axial_cells * mesh_peers)
    passages = lax.axis_size("blk")
    position = lax.axis_index("blk")
    blade_stiffness = stiffness[0]
    disp0 = displacement[0]
    vel0 = velocity[0]

    row_shape = jax.ShapeDtypeStruct((STEP_COUNT,) + upper_row_history.shape[2:], state0.dtype)
    rows_up, rows_down = pl.pallas_call(
        functools.partial(pick_kernel, passages),
        out_shape=(row_shape, row_shape),
        in_specs=[smem_spec(), smem_spec(), any_spec(), any_spec()],
        out_specs=(vmem_spec(), vmem_spec()),
        scratch_shapes=[pltpu.SemaphoreType.DMA((2 * STEP_COUNT * upper_row_history.shape[2],))],
    )(
        lower_lag_slot,
        upper_lag_slot,
        jnp.transpose(upper_row_history[0], (1, 0, 2)),
        jnp.transpose(lower_row_history[0], (1, 0, 2)),
    )
    lower_ghosts = shifted(rows_up, "blk", 1)
    upper_ghosts = shifted(rows_down, "blk", -1)

    reach = 2 * STEP_COUNT
    own = [state0, mode_shape, lower_ghosts, upper_ghosts]
    shapes = [part.shape[:-1] + (reach,) for part in own]
    from_left = shifted(pack([part[..., -reach:] for part in own], reach).reshape(-1), "mesh", 1)
    from_right = shifted(pack([part[..., :reach] for part in own], reach).reshape(-1), "mesh", -1)
    from_left = from_left.reshape(reach, -1)
    from_right = from_right.reshape(reach, -1)
    from_left = jnp.where(me > 0, from_left, jnp.zeros_like(from_left))
    from_right = jnp.where(me < mesh_peers - 1, from_right, jnp.zeros_like(from_right))
    packed_rows = from_left.shape[1]
    padded_rows = -(-packed_rows // LANES) * LANES
    halo_tile = jnp.pad(
        jnp.concatenate([from_left, from_right], axis=0), [(0, 0), (0, padded_rows - packed_rows)]
    )
    columns = [pltpu.VMEM((padded_rows, LANES), state0.dtype)]
    lanes_wide = axial_cells + LANES
    ins = (state0, mode_shape, lower_ghosts, upper_ghosts, halo_tile)

    base1, part_lanes = pl.pallas_call(
        functools.partial(first_kernel, mesh_peers),
        out_shape=(
            jax.ShapeDtypeStruct((fields, pitch_cells, lanes_wide), state0.dtype),
            jax.ShapeDtypeStruct((4 * modes + modes * modes, LANES), state0.dtype),
        ),
        in_specs=[smem_spec()] * 3 + [vmem_spec()] * 5,
        out_specs=(vmem_spec(), vmem_spec()),
        scratch_shapes=columns,
    )(axial_jacobian, pitch_jacobian, velocity, *ins)

    totals = mesh_sum(jnp.sum(part_lanes, axis=1))

    rate_a = pl.pallas_call(
        functools.partial(step2_rate_kernel, mesh_peers),
        out_shape=jax.ShapeDtypeStruct(base1.shape, base1.dtype),
        in_specs=[smem_spec()] * 2 + [vmem_spec()] * 5,
        out_specs=vmem_spec(),
        scratch_shapes=columns,
    )(axial_jacobian, pitch_jacobian, base1, *ins[1:])

    small = jax.ShapeDtypeStruct(displacement.shape, displacement.dtype)
    state2, disp2, vel2 = pl.pallas_call(
        functools.partial(second_kernel, mesh_peers, force_scale),
        out_shape=(jax.ShapeDtypeStruct(state0.shape, state0.dtype), small, small),
        in_specs=[smem_spec()] * 6 + [vmem_spec()] * 6,
        out_specs=(vmem_spec(), smem_spec(), smem_spec()),
        scratch_shapes=columns,
    )(totals, stiffness, displacement, velocity, axial_jacobian, pitch_jacobian, base1, rate_a, *ins[1:])
    return (state2[None], disp2, vel2)


def solution(mesh):
    return jax.shard_map(
        on_device,
        mesh=mesh,
        in_specs=(
            P("blk", None, None, "mesh"),
            P("blk", None, None, "mesh"),
            P("blk", None, None, "mesh"),
            P(),
            P(),
            P(),
            P(),
            P(None, None, "mesh"),
            P("blk", None),
            P("blk", None),
            P("blk", None),
        ),
        out_specs=(P("blk", None, None, "mesh"), P("blk", None), P("blk", None)),
        check_vma=False,
    )
```

```python
import functools
import math

import jax
import jax.numpy as jnp
from jax import lax
from jax.experimental import pallas as pl
from jax.experimental.pallas import tpu as pltpu
from jax.sharding import PartitionSpec as P

STEP_COUNT = 2


PRECISE = lax.Precision.HIGHEST
TIME_STEP = 0.4
DIFFUSION = 0.1
COUPLING = 0.3
DAMPING = 0.1


def shifted(value, axis, by):
    peers = lax.axis_size(axis)
    return lax.ppermute(value, axis, [(i, (i + by) % peers) for i in range(peers)])


def halo(value):
    peers = lax.axis_size("mesh")
    me = lax.axis_index("mesh")
    before = shifted(value[..., -1:], "mesh", 1)
    after = shifted(value[..., :1], "mesh", -1)
    before = jnp.where(me > 0, before, jnp.zeros_like(before))
    after = jnp.where(me < peers - 1, after, jnp.zeros_like(after))
    return before, after


def mesh_sum(value):
    peers = lax.axis_size("mesh")
    if peers & (peers - 1):
        return lax.psum(value, "mesh")
    step = 1
    while step < peers:
        value = value + lax.ppermute(value, "mesh", [(i, i ^ step) for i in range(peers)])
        step *= 2
    return value


def pick_rows(table, index, count):
    slots = table.shape[0]
    slot = jnp.arange(slots, dtype=jnp.int32).reshape((slots,) + (1,) * (table.ndim - 1))
    rows = []
    for s in range(count):
        hit = slot == (index + s) % slots
        rows.append(jnp.sum(jnp.where(hit, table, jnp.zeros_like(table)), axis=0))
    return jnp.stack(rows)


def pick_entry(values, index):
    hit = jnp.arange(values.shape[0], dtype=jnp.int32) == index
    return jnp.sum(jnp.where(hit, values, jnp.zeros_like(values)))


def axial_pad(value, before, after):
    return jnp.concatenate([before, value, after], axis=-1)


def pitch_pad(value, lower, upper):
    return jnp.concatenate([lower[:, None, :], value, upper[:, None, :]], axis=1)


def flow_rate(state, before, after, lower_ghost, upper_ghost, axial_jacobian, pitch_jacobian):
    padded_axial = axial_pad(state, before, after)
    padded_pitch = pitch_pad(state, lower_ghost, upper_ghost)
    grad_axial = 0.5 * (padded_axial[:, :, 2:] - padded_axial[:, :, :-2])
    grad_pitch = 0.5 * (padded_pitch[:, 2:, :] - padded_pitch[:, :-2, :])
    laplacian = (
        padded_axial[:, :, 2:]
        + padded_axial[:, :, :-2]
        + padded_pitch[:, 2:, :]
        + padded_pitch[:, :-2, :]
        - 4.0 * state
    )
    flux = jnp.einsum("ij,jpx->ipx", axial_jacobian, grad_axial, precision=PRECISE)
    flux = flux + jnp.einsum("ij,jpx->ipx", pitch_jacobian, grad_pitch, precision=PRECISE)
    return DIFFUSION * laplacian - flux


def single_field_grads(field, before, after):
    padded_axial = jnp.concatenate([before, field, after], axis=-1)
    zero_row = jnp.zeros_like(field[..., :1, :])
    padded_pitch = jnp.concatenate([zero_row, field, zero_row], axis=-2)
    grad_axial = 0.5 * (padded_axial[..., 2:] - padded_axial[..., :-2])
    grad_pitch = 0.5 * (padded_pitch[..., 2:, :] - padded_pitch[..., :-2, :])
    laplacian = (
        padded_axial[..., 2:]
        + padded_axial[..., :-2]
        + padded_pitch[..., 2:, :]
        + padded_pitch[..., :-2, :]
        - 4.0 * field
    )
    return grad_axial, grad_pitch, laplacian


def modal_field(weights, mode_shape):
    return jnp.einsum("m,mpx->px", weights, mode_shape, precision=PRECISE)


def projection(mode_shape, field):
    return jnp.einsum("mpx,px->m", mode_shape, field, precision=PRECISE)


def add_field_one(rate, extra):
    return rate.at[1].add(extra)


def rate_field4(state, lower_ghost, upper_ghost, axial_jacobian, pitch_jacobian):
    zero_col = jnp.zeros_like(state[..., :1])
    padded_axial = jnp.concatenate([zero_col, state, zero_col], axis=-1)
    padded_pitch = pitch_pad(state, lower_ghost, upper_ghost)
    grad_axial = 0.5 * (padded_axial[:, :, 2:] - padded_axial[:, :, :-2])
    grad_pitch = 0.5 * (padded_pitch[:, 2:, :] - padded_pitch[:, :-2, :])
    laplacian = (
        padded_axial[4, :, 2:]
        + padded_axial[4, :, :-2]
        + padded_pitch[4, 2:, :]
        + padded_pitch[4, :-2, :]
        - 4.0 * state[4]
    )
    flux = jnp.einsum("j,jpx->px", axial_jacobian[4], grad_axial, precision=PRECISE)
    flux = flux + jnp.einsum("j,jpx->px", pitch_jacobian[4], grad_pitch, precision=PRECISE)
    return DIFFUSION * laplacian - flux


def pack(parts, width):
    flat = [jnp.moveaxis(part, -1, 0).reshape(width, -1) for part in parts]
    return jnp.concatenate(flat, axis=1)


def unpack(buffer, shapes):
    out, offset = [], 0
    for shape in shapes:
        count = math.prod(shape[:-1])
        out.append(buffer[offset : offset + count].reshape(shape))
        offset += count
    return out


LANES = 128


def lane_roll(x, shift):
    return pltpu.roll(x, shift % x.shape[-1], x.ndim - 1)


def row_roll(x, shift):
    return pltpu.roll(x, shift % x.shape[0], 0)


def pitch_neighbours(s, lower, upper):
    rows = s.shape[0]
    tile = 8
    edge = lax.broadcasted_iota(jnp.int32, (tile,) + s.shape[1:], 0)
    north = row_roll(s, -1)
    south = row_roll(s, 1)
    north = jnp.concatenate(
        [north[: rows - tile], jnp.where(edge == tile - 1, upper, north[rows - tile :])], axis=0
    )
    south = jnp.concatenate([jnp.where(edge == 0, lower, south[:tile]), south[tile:]], axis=0)
    return north, south


def masked(r, inside):
    cut = r.shape[-1] - LANES
    return jnp.concatenate([r[:, :cut], r[:, cut:] * inside[:, cut:]], axis=1)


def kernel_rate(state, lower, upper, jac, push, inside, fields_out):
    ax, pt = jac
    diffs_a, diffs_p, laps = [], [], []
    for j, s in enumerate(state):
        east = lane_roll(s, -1)
        west = lane_roll(s, 1)
        north, south = pitch_neighbours(s, lower[j], upper[j])
        diffs_a.append(east - west)
        diffs_p.append(north - south)
        laps.append((east + west) + (north + south) - 4.0 * s)
    out = []
    for i in fields_out:
        r = DIFFUSION * laps[i]
        for j in range(len(state)):
            r = r - (0.5 * ax[i][j]) * diffs_a[j] - (0.5 * pt[i][j]) * diffs_p[j]
        if i == 1 and push is not None:
            r = r + push
        out.append(masked(r, inside))
    return out


def read_jacobians(ax_ref, pt_ref, fields):
    ax = [[ax_ref[i, j] for j in range(fields)] for i in range(fields)]
    pt = [[pt_ref[i, j] for j in range(fields)] for i in range(fields)]
    return ax, pt


def lane_fold(x):
    x = jnp.sum(x, axis=0, keepdims=True)
    total = x[:, :LANES]
    for t in range(1, x.shape[1] // LANES):
        total = total + x[:, t * LANES : (t + 1) * LANES]
    return total


def pick_kernel(peers, lower_slot_ref, upper_slot_ref, upper_hist_ref, lower_hist_ref, up_ref, down_ref, sems):
    slots = upper_hist_ref.shape[1]
    position = lax.axis_index("blk")
    slot_next = lower_slot_ref[(position + 1) % peers]
    slot_prev = upper_slot_ref[(position + peers - 1) % peers]
    copies = []
    for s in range(up_ref.shape[1]):
        for hist, first, out in ((upper_hist_ref, slot_next, up_ref), (lower_hist_ref, slot_prev, down_ref)):
            at = (first + s) % slots
            copy = pltpu.make_async_copy(
                hist.at[:, pl.ds(at, 1), :], out.at[:, pl.ds(s, 1), :], sems.at[len(copies)]
            )
            copy.start()
            copies.append(copy)
    for copy in copies:
        copy.wait()


def widened(own, tile):
    return jnp.concatenate([own, lane_roll(tile, -2 * STEP_COUNT)], axis=-1)


def unfold_halo(halo_ref, columns_ref):
    block = halo_ref[...]
    spare = jnp.zeros((LANES - block.shape[0], block.shape[1]), block.dtype)
    columns_ref[...] = jnp.concatenate([block, spare], axis=0).T


def lane_masks(peers, shape, own_width):
    reach = 2 * STEP_COUNT
    me = lax.axis_index("mesh")
    lane = lax.broadcasted_iota(jnp.int32, shape, len(shape) - 1)
    width = shape[-1]
    right_ok = (lane >= own_width) & (lane < own_width + reach) & (me < peers - 1)
    left_ok = (lane >= width - reach) & (me > 0)
    owned = lane < own_width
    inside = owned | right_ok | left_ok
    return inside.astype(jnp.float32), owned.astype(jnp.float32)


def assemble(u_ref, ms_ref, glo_ref, gup_ref, halo_ref, fields, modes, pitch):
    u = []
    for j in range(fields if u_ref is not None else 0):
        rows = slice(j * pitch, (j + 1) * pitch)
        u.append(widened(u_ref[j], halo_ref[rows, :]))
    ms = []
    for m in range(modes):
        rows = slice((fields + m) * pitch, (fields + m + 1) * pitch)
        ms.append(widened(ms_ref[m], halo_ref[rows, :]))
    base = (fields + modes) * pitch
    steps = glo_ref.shape[1]
    ghosts = []
    for side, ref in enumerate((glo_ref, gup_ref)):
        per_step = []
        for s in range(steps):
            per_field = []
            for j in range(fields):
                row = base + side * steps * fields + j * steps + s
                per_field.append(widened(ref[j, pl.ds(s, 1), :], halo_ref[row : row + 1, :]))
            per_step.append(per_field)
        ghosts.append(per_step)
    return u, ms, ghosts[0], ghosts[1]


def first_kernel(peers, ax_ref, pt_ref, vel_ref, u_ref, ms_ref, glo_ref, gup_ref, packed_ref, a_ref, part_ref, halo_ref):
    h = TIME_STEP
    unfold_halo(packed_ref, halo_ref)
    fields = u_ref.shape[0]
    modes = ms_ref.shape[0]
    pitch = u_ref.shape[1]
    jac = read_jacobians(ax_ref, pt_ref, fields)
    vel = [vel_ref[0, m] for m in range(modes)]
    u0, ms, gl, gu = assemble(u_ref, ms_ref, glo_ref, gup_ref, halo_ref, fields, modes, pitch)
    inside, _ = lane_masks(peers, u0[0].shape, u_ref.shape[-1])
    push = vel[0] * ms[0]
    for m in range(1, modes):
        push = push + vel[m] * ms[m]
    push = COUPLING * push
    gl1, gu1, gl2, gu2 = gl[0], gu[0], gl[1], gu[1]
    every = list(range(fields))
    k1 = kernel_rate(u0, gl1, gu1, jac, push, inside, every)
    mid = [u0[j] + h * k1[j] for j in every]
    k2 = kernel_rate(mid, gl1, gu1, jac, push, inside, every)
    a = [u0[j] + 0.5 * h * (k1[j] + k2[j]) for j in every]
    for j in every:
        a_ref[j] = a[j]
    (ra4,) = kernel_rate(a, gl2, gu2, jac, None, inside, [4])
    own = u_ref.shape[-1]
    weighted = [ms_ref[m] for m in range(modes)]
    k = 0
    for field in (u0[4], mid[4], a[4], ra4):
        field = field[:, :own]
        for m in range(modes):
            part_ref[k : k + 1, :] = lane_fold(weighted[m] * field)
            k += 1
    ax41, pt41 = 0.5 * jac[0][4][1], 0.5 * jac[1][4][1]
    no_ghost = jnp.zeros((1, ms[0].shape[1]), ms[0].dtype)
    for n in range(modes):
        s = ms[n]
        north, south = pitch_neighbours(s, no_ghost, no_ghost)
        t = -(ax41 * (lane_roll(s, -1) - lane_roll(s, 1)) + pt41 * (north - south))
        t = t[:, :own]
        for m in range(modes):
            part_ref[k + m * modes + n : k + m * modes + n + 1, :] = lane_fold(weighted[m] * t)


def modal_steps(force_scale, tot_ref, stiff_ref, disp_ref, vel_ref, modes):
    h = TIME_STEP
    t = [force_scale * tot_ref[k] for k in range(4 * modes + modes * modes)]
    force = [t[w * modes : (w + 1) * modes] for w in range(4)]
    couple = [t[4 * modes + m * modes : 4 * modes + (m + 1) * modes] for m in range(modes)]
    stiff = [stiff_ref[0, m] for m in range(modes)]
    disp0 = [disp_ref[0, m] for m in range(modes)]
    vel0 = [vel_ref[0, m] for m in range(modes)]

    def accel(f, q, v):
        return [f[m] - stiff[m] * q[m] - DAMPING * v[m] for m in range(modes)]

    def axpy(x, a, y):
        return [x[m] + a * y[m] for m in range(modes)]

    acc1 = accel(force[0], disp0, vel0)
    disp1m = axpy(disp0, h, vel0)
    vel1m = axpy(vel0, h, acc1)
    acc1m = accel(force[1], disp1m, vel1m)
    disp1 = [disp0[m] + 0.5 * h * (vel0[m] + vel1m[m]) for m in range(modes)]
    vel1 = [vel0[m] + 0.5 * h * (acc1[m] + acc1m[m]) for m in range(modes)]
    acc2 = accel(force[2], disp1, vel1)
    disp2m = axpy(disp1, h, vel1)
    vel2m = axpy(vel1, h, acc2)
    corr = 0.5 * h * h * COUPLING
    force2m = []
    for m in range(modes):
        coupled = couple[m][0] * acc1[0]
        for n in range(1, modes):
            coupled = coupled + couple[m][n] * acc1[n]
        force2m.append(force[2][m] + h * force[3][m] + h * corr * coupled)
    acc2m = accel(force2m, disp2m, vel2m)
    disp2 = [disp1[m] + 0.5 * h * (vel1[m] + vel2m[m]) for m in range(modes)]
    vel2 = [vel1[m] + 0.5 * h * (acc2[m] + acc2m[m]) for m in range(modes)]
    coef = [[corr * acc1[m] for m in range(modes)], vel1, vel2m]
    return coef, disp2, vel2


def step2_rate_kernel(peers, ax_ref, pt_ref, a_ref, ms_ref, glo_ref, gup_ref, packed_ref, ra_ref, halo_ref):
    unfold_halo(packed_ref, halo_ref)
    fields = a_ref.shape[0]
    modes = ms_ref.shape[0]
    pitch = ms_ref.shape[1]
    jac = read_jacobians(ax_ref, pt_ref, fields)
    _, ms, gl, gu = assemble(None, ms_ref, glo_ref, gup_ref, halo_ref, fields, modes, pitch)
    inside, _ = lane_masks(peers, ms[0].shape, ms_ref.shape[-1])
    every = list(range(fields))
    a = [a_ref[j] for j in every]
    ra = kernel_rate(a, gl[1], gu[1], jac, None, inside, every)
    for j in every:
        ra_ref[j] = ra[j]


def second_kernel(
    peers,
    force_scale,
    tot_ref,
    stiff_ref,
    disp_ref,
    vel_ref,
    ax_ref,
    pt_ref,
    a_ref,
    ra_ref,
    ms_ref,
    glo_ref,
    gup_ref,
    packed_ref,
    out_ref,
    disp_out_ref,
    vel_out_ref,
    halo_ref,
):
    h = TIME_STEP
    unfold_halo(packed_ref, halo_ref)
    fields = a_ref.shape[0]
    modes = ms_ref.shape[0]
    pitch = ms_ref.shape[1]
    jac = read_jacobians(ax_ref, pt_ref, fields)
    coef, disp2, vel2 = modal_steps(force_scale, tot_ref, stiff_ref, disp_ref, vel_ref, modes)
    for m in range(modes):
        disp_out_ref[0, m] = disp2[m]
        vel_out_ref[0, m] = vel2[m]
    _, ms, gl, gu = assemble(None, ms_ref, glo_ref, gup_ref, halo_ref, fields, modes, pitch)
    inside, _ = lane_masks(peers, ms[0].shape, ms_ref.shape[-1])

    def combine(weights):
        total = weights[0] * ms[0]
        for m in range(1, modes):
            total = total + weights[m] * ms[m]
        return total

    gl2, gu2 = gl[1], gu[1]
    every = list(range(fields))
    s1 = [a_ref[j] for j in every]
    correction = combine(coef[0])
    s1[1] = s1[1] + correction
    rows = correction.shape[0]
    row = lax.broadcasted_iota(jnp.int32, correction.shape, 0)
    east, west = lane_roll(correction, -1), lane_roll(correction, 1)
    north = jnp.where(row == rows - 1, 0.0, row_roll(correction, -1))
    south = jnp.where(row == 0, 0.0, row_roll(correction, 1))
    ga = 0.5 * (east - west)
    gp = 0.5 * (north - south)
    lap = east + west + north + south - 4.0 * correction
    ax, pt = jac
    push1 = COUPLING * combine(coef[1])
    k1 = []
    for i in every:
        r = -ax[i][1] * ga - pt[i][1] * gp
        if i == 1:
            r = r + DIFFUSION * lap + push1
        k1.append(ra_ref[i] + masked(r, inside))
    mid = [s1[j] + h * k1[j] for j in every]
    k2 = kernel_rate(mid, gl2, gu2, jac, COUPLING * combine(coef[2]), inside, every)
    width = out_ref.shape[-1]
    for j in every:
        s2 = s1[j] + 0.5 * h * (k1[j] + k2[j])
        out_ref[j] = s2[:, :width]


def vmem_spec():
    return pl.BlockSpec(memory_space=pltpu.VMEM)


def any_spec():
    return pl.BlockSpec(memory_space=pl.ANY)


def smem_spec():
    return pl.BlockSpec(memory_space=pltpu.SMEM)


def on_device(
    flow_field,
    lower_row_history,
    upper_row_history,
    lower_lag_slot,
    upper_lag_slot,
    axial_jacobian,
    pitch_jacobian,
    mode_shape,
    stiffness,
    displacement,
    velocity,
):
    h = TIME_STEP
    state0 = flow_field[0]
    fields, pitch_cells, axial_cells = state0.shape
    modes = mode_shape.shape[0]
    mesh_peers = lax.axis_size("mesh")
    me = lax.axis_index("mesh")
    force_scale = 1.0 / math.sqrt(pitch_cells * axial_cells * mesh_peers)
    passages = lax.axis_size("blk")
    position = lax.axis_index("blk")
    blade_stiffness = stiffness[0]
    disp0 = displacement[0]
    vel0 = velocity[0]

    row_shape = jax.ShapeDtypeStruct(
        (upper_row_history.shape[2], STEP_COUNT, upper_row_history.shape[3]), state0.dtype
    )
    rows_up, rows_down = pl.pallas_call(
        functools.partial(pick_kernel, passages),
        out_shape=(row_shape, row_shape),
        in_specs=[smem_spec(), smem_spec(), any_spec(), any_spec()],
        out_specs=(vmem_spec(), vmem_spec()),
        scratch_shapes=[pltpu.SemaphoreType.DMA((2 * STEP_COUNT,))],
    )(
        lower_lag_slot,
        upper_lag_slot,
        jnp.transpose(upper_row_history[0], (1, 0, 2)),
        jnp.transpose(lower_row_history[0], (1, 0, 2)),
    )
    lower_ghosts = shifted(rows_up, "blk", 1)
    upper_ghosts = shifted(rows_down, "blk", -1)

    reach = 2 * STEP_COUNT
    own = [state0, mode_shape, lower_ghosts, upper_ghosts]
    shapes = [part.shape[:-1] + (reach,) for part in own]
    from_left = shifted(pack([part[..., -reach:] for part in own], reach).reshape(-1), "mesh", 1)
    from_right = shifted(pack([part[..., :reach] for part in own], reach).reshape(-1), "mesh", -1)
    from_left = from_left.reshape(reach, -1)
    from_right = from_right.reshape(reach, -1)
    from_left = jnp.where(me > 0, from_left, jnp.zeros_like(from_left))
    from_right = jnp.where(me < mesh_peers - 1, from_right, jnp.zeros_like(from_right))
    packed_rows = from_left.shape[1]
    padded_rows = -(-packed_rows // LANES) * LANES
    halo_tile = jnp.pad(
        jnp.concatenate([from_left, from_right], axis=0), [(0, 0), (0, padded_rows - packed_rows)]
    )
    columns = [pltpu.VMEM((padded_rows, LANES), state0.dtype)]
    lanes_wide = axial_cells + LANES
    ins = (state0, mode_shape, lower_ghosts, upper_ghosts, halo_tile)

    base1, part_lanes = pl.pallas_call(
        functools.partial(first_kernel, mesh_peers),
        out_shape=(
            jax.ShapeDtypeStruct((fields, pitch_cells, lanes_wide), state0.dtype),
            jax.ShapeDtypeStruct((4 * modes + modes * modes, LANES), state0.dtype),
        ),
        in_specs=[smem_spec()] * 3 + [vmem_spec()] * 5,
        out_specs=(vmem_spec(), vmem_spec()),
        scratch_shapes=columns,
    )(axial_jacobian, pitch_jacobian, velocity, *ins)

    totals = mesh_sum(jnp.sum(part_lanes, axis=1))

    rate_a = pl.pallas_call(
        functools.partial(step2_rate_kernel, mesh_peers),
        out_shape=jax.ShapeDtypeStruct(base1.shape, base1.dtype),
        in_specs=[smem_spec()] * 2 + [vmem_spec()] * 5,
        out_specs=vmem_spec(),
        scratch_shapes=columns,
    )(axial_jacobian, pitch_jacobian, base1, *ins[1:])

    small = jax.ShapeDtypeStruct(displacement.shape, displacement.dtype)
    state2, disp2, vel2 = pl.pallas_call(
        functools.partial(second_kernel, mesh_peers, force_scale),
        out_shape=(jax.ShapeDtypeStruct(state0.shape, state0.dtype), small, small),
        in_specs=[smem_spec()] * 6 + [vmem_spec()] * 6,
        out_specs=(vmem_spec(), smem_spec(), smem_spec()),
        scratch_shapes=columns,
    )(totals, stiffness, displacement, velocity, axial_jacobian, pitch_jacobian, base1, rate_a, *ins[1:])
    return (state2[None], disp2, vel2)


def solution(mesh):
    return jax.shard_map(
        on_device,
        mesh=mesh,
        in_specs=(
            P("blk", None, None, "mesh"),
            P("blk", None, None, "mesh"),
            P("blk", None, None, "mesh"),
            P(),
            P(),
            P(),
            P(),
            P(None, None, "mesh"),
            P("blk", None),
            P("blk", None),
            P("blk", None),
        ),
        out_specs=(P("blk", None, None, "mesh"), P("blk", None), P("blk", None)),
        check_vma=False,
    )
```

```python
import functools
import math

import jax
import jax.numpy as jnp
from jax import lax
from jax.experimental import pallas as pl
from jax.experimental.pallas import tpu as pltpu
from jax.sharding import PartitionSpec as P

STEP_COUNT = 2


PRECISE = lax.Precision.HIGHEST
TIME_STEP = 0.4
DIFFUSION = 0.1
COUPLING = 0.3
DAMPING = 0.1


def shifted(value, axis, by):
    peers = lax.axis_size(axis)
    return lax.ppermute(value, axis, [(i, (i + by) % peers) for i in range(peers)])


def halo(value):
    peers = lax.axis_size("mesh")
    me = lax.axis_index("mesh")
    before = shifted(value[..., -1:], "mesh", 1)
    after = shifted(value[..., :1], "mesh", -1)
    before = jnp.where(me > 0, before, jnp.zeros_like(before))
    after = jnp.where(me < peers - 1, after, jnp.zeros_like(after))
    return before, after


def mesh_sum_pair(value):
    peers = lax.axis_size("mesh")
    if peers & (peers - 1) or peers < 2:
        return lax.psum(value, "mesh"), jnp.zeros_like(value)
    step = 1
    while 2 * step < peers:
        value = value + lax.ppermute(value, "mesh", [(i, i ^ step) for i in range(peers)])
        step *= 2
    return value, lax.ppermute(value, "mesh", [(i, i ^ step) for i in range(peers)])


def pick_rows(table, index, count):
    slots = table.shape[0]
    slot = jnp.arange(slots, dtype=jnp.int32).reshape((slots,) + (1,) * (table.ndim - 1))
    rows = []
    for s in range(count):
        hit = slot == (index + s) % slots
        rows.append(jnp.sum(jnp.where(hit, table, jnp.zeros_like(table)), axis=0))
    return jnp.stack(rows)


def pick_entry(values, index):
    hit = jnp.arange(values.shape[0], dtype=jnp.int32) == index
    return jnp.sum(jnp.where(hit, values, jnp.zeros_like(values)))


def axial_pad(value, before, after):
    return jnp.concatenate([before, value, after], axis=-1)


def pitch_pad(value, lower, upper):
    return jnp.concatenate([lower[:, None, :], value, upper[:, None, :]], axis=1)


def flow_rate(state, before, after, lower_ghost, upper_ghost, axial_jacobian, pitch_jacobian):
    padded_axial = axial_pad(state, before, after)
    padded_pitch = pitch_pad(state, lower_ghost, upper_ghost)
    grad_axial = 0.5 * (padded_axial[:, :, 2:] - padded_axial[:, :, :-2])
    grad_pitch = 0.5 * (padded_pitch[:, 2:, :] - padded_pitch[:, :-2, :])
    laplacian = (
        padded_axial[:, :, 2:]
        + padded_axial[:, :, :-2]
        + padded_pitch[:, 2:, :]
        + padded_pitch[:, :-2, :]
        - 4.0 * state
    )
    flux = jnp.einsum("ij,jpx->ipx", axial_jacobian, grad_axial, precision=PRECISE)
    flux = flux + jnp.einsum("ij,jpx->ipx", pitch_jacobian, grad_pitch, precision=PRECISE)
    return DIFFUSION * laplacian - flux


def single_field_grads(field, before, after):
    padded_axial = jnp.concatenate([before, field, after], axis=-1)
    zero_row = jnp.zeros_like(field[..., :1, :])
    padded_pitch = jnp.concatenate([zero_row, field, zero_row], axis=-2)
    grad_axial = 0.5 * (padded_axial[..., 2:] - padded_axial[..., :-2])
    grad_pitch = 0.5 * (padded_pitch[..., 2:, :] - padded_pitch[..., :-2, :])
    laplacian = (
        padded_axial[..., 2:]
        + padded_axial[..., :-2]
        + padded_pitch[..., 2:, :]
        + padded_pitch[..., :-2, :]
        - 4.0 * field
    )
    return grad_axial, grad_pitch, laplacian


def modal_field(weights, mode_shape):
    return jnp.einsum("m,mpx->px", weights, mode_shape, precision=PRECISE)


def projection(mode_shape, field):
    return jnp.einsum("mpx,px->m", mode_shape, field, precision=PRECISE)


def add_field_one(rate, extra):
    return rate.at[1].add(extra)


def rate_field4(state, lower_ghost, upper_ghost, axial_jacobian, pitch_jacobian):
    zero_col = jnp.zeros_like(state[..., :1])
    padded_axial = jnp.concatenate([zero_col, state, zero_col], axis=-1)
    padded_pitch = pitch_pad(state, lower_ghost, upper_ghost)
    grad_axial = 0.5 * (padded_axial[:, :, 2:] - padded_axial[:, :, :-2])
    grad_pitch = 0.5 * (padded_pitch[:, 2:, :] - padded_pitch[:, :-2, :])
    laplacian = (
        padded_axial[4, :, 2:]
        + padded_axial[4, :, :-2]
        + padded_pitch[4, 2:, :]
        + padded_pitch[4, :-2, :]
        - 4.0 * state[4]
    )
    flux = jnp.einsum("j,jpx->px", axial_jacobian[4], grad_axial, precision=PRECISE)
    flux = flux + jnp.einsum("j,jpx->px", pitch_jacobian[4], grad_pitch, precision=PRECISE)
    return DIFFUSION * laplacian - flux


def pack(parts, width):
    flat = [jnp.moveaxis(part, -1, 0).reshape(width, -1) for part in parts]
    return jnp.concatenate(flat, axis=1)


def unpack(buffer, shapes):
    out, offset = [], 0
    for shape in shapes:
        count = math.prod(shape[:-1])
        out.append(buffer[offset : offset + count].reshape(shape))
        offset += count
    return out


LANES = 128


def lane_roll(x, shift):
    return pltpu.roll(x, shift % x.shape[-1], x.ndim - 1)


def row_roll(x, shift):
    return pltpu.roll(x, shift % x.shape[0], 0)


def pitch_neighbours(s, lower, upper):
    rows = s.shape[0]
    tile = 8
    edge = lax.broadcasted_iota(jnp.int32, (tile,) + s.shape[1:], 0)
    north = row_roll(s, -1)
    south = row_roll(s, 1)
    north = jnp.concatenate(
        [north[: rows - tile], jnp.where(edge == tile - 1, upper, north[rows - tile :])], axis=0
    )
    south = jnp.concatenate([jnp.where(edge == 0, lower, south[:tile]), south[tile:]], axis=0)
    return north, south


def masked(r, inside):
    cut = r.shape[-1] - LANES
    return jnp.concatenate([r[:, :cut], r[:, cut:] * inside[:, cut:]], axis=1)


def kernel_rate(state, lower, upper, jac, push, inside, fields_out):
    ax, pt = jac
    diffs_a, diffs_p, laps = [], [], []
    for j, s in enumerate(state):
        east = lane_roll(s, -1)
        west = lane_roll(s, 1)
        north, south = pitch_neighbours(s, lower[j], upper[j])
        diffs_a.append(east - west)
        diffs_p.append(north - south)
        laps.append((east + west) + (north + south) - 4.0 * s)
    out = []
    for i in fields_out:
        r = DIFFUSION * laps[i]
        for j in range(len(state)):
            r = r - (0.5 * ax[i][j]) * diffs_a[j] - (0.5 * pt[i][j]) * diffs_p[j]
        if i == 1 and push is not None:
            r = r + push
        out.append(masked(r, inside))
    return out


def read_jacobians(ax_ref, pt_ref, fields):
    ax = [[ax_ref[i, j] for j in range(fields)] for i in range(fields)]
    pt = [[pt_ref[i, j] for j in range(fields)] for i in range(fields)]
    return ax, pt


def lane_fold(x):
    x = jnp.sum(x, axis=0, keepdims=True)
    total = x[:, :LANES]
    for t in range(1, x.shape[1] // LANES):
        total = total + x[:, t * LANES : (t + 1) * LANES]
    return total


def pick_kernel(peers, lower_slot_ref, upper_slot_ref, upper_hist_ref, lower_hist_ref, up_ref, down_ref):
    fields, slots = upper_hist_ref.shape[0], upper_hist_ref.shape[1]
    position = lax.axis_index("blk")
    slot_next = lower_slot_ref[(position + 1) % peers]
    slot_prev = upper_slot_ref[(position + peers - 1) % peers]
    for s in range(up_ref.shape[0]):
        up_at = (slot_next + s) % slots
        down_at = (slot_prev + s) % slots
        for f in range(fields):
            up_ref[s, f : f + 1, :] = upper_hist_ref[f, pl.ds(up_at, 1), :]
            down_ref[s, f : f + 1, :] = lower_hist_ref[f, pl.ds(down_at, 1), :]


def widened(own, tile):
    return jnp.concatenate([own, lane_roll(tile, -2 * STEP_COUNT)], axis=-1)


def unfold_halo(halo_ref, columns_ref):
    block = halo_ref[...]
    spare = jnp.zeros((LANES - block.shape[0], block.shape[1]), block.dtype)
    columns_ref[...] = jnp.concatenate([block, spare], axis=0).T


def lane_masks(peers, shape, own_width):
    reach = 2 * STEP_COUNT
    me = lax.axis_index("mesh")
    lane = lax.broadcasted_iota(jnp.int32, shape, len(shape) - 1)
    width = shape[-1]
    right_ok = (lane >= own_width) & (lane < own_width + reach) & (me < peers - 1)
    left_ok = (lane >= width - reach) & (me > 0)
    owned = lane < own_width
    inside = owned | right_ok | left_ok
    return inside.astype(jnp.float32), owned.astype(jnp.float32)


def assemble(u_ref, ms_ref, glo_ref, gup_ref, halo_ref, fields, modes, pitch):
    u = []
    for j in range(fields if u_ref is not None else 0):
        rows = slice(j * pitch, (j + 1) * pitch)
        u.append(widened(u_ref[j], halo_ref[rows, :]))
    ms = []
    for m in range(modes):
        rows = slice((fields + m) * pitch, (fields + m + 1) * pitch)
        ms.append(widened(ms_ref[m], halo_ref[rows, :]))
    base = (fields + modes) * pitch
    steps = glo_ref.shape[0]
    ghosts = []
    for side, ref in enumerate((glo_ref, gup_ref)):
        per_step = []
        for s in range(steps):
            start = base + (side * steps + s) * fields
            rows = slice(start, start + fields)
            block = widened(ref[s], halo_ref[rows, :])
            per_step.append([block[j : j + 1, :] for j in range(fields)])
        ghosts.append(per_step)
    return u, ms, ghosts[0], ghosts[1]


def first_kernel(peers, ax_ref, pt_ref, vel_ref, u_ref, ms_ref, glo_ref, gup_ref, packed_ref, a_ref, part_ref, halo_ref):
    h = TIME_STEP
    unfold_halo(packed_ref, halo_ref)
    fields = u_ref.shape[0]
    modes = ms_ref.shape[0]
    pitch = u_ref.shape[1]
    jac = read_jacobians(ax_ref, pt_ref, fields)
    vel = [vel_ref[0, m] for m in range(modes)]
    u0, ms, gl, gu = assemble(u_ref, ms_ref, glo_ref, gup_ref, halo_ref, fields, modes, pitch)
    inside, _ = lane_masks(peers, u0[0].shape, u_ref.shape[-1])
    push = vel[0] * ms[0]
    for m in range(1, modes):
        push = push + vel[m] * ms[m]
    push = COUPLING * push
    gl1, gu1, gl2, gu2 = gl[0], gu[0], gl[1], gu[1]
    every = list(range(fields))
    k1 = kernel_rate(u0, gl1, gu1, jac, push, inside, every)
    mid = [u0[j] + h * k1[j] for j in every]
    k2 = kernel_rate(mid, gl1, gu1, jac, push, inside, every)
    a = [u0[j] + 0.5 * h * (k1[j] + k2[j]) for j in every]
    for j in every:
        a_ref[j] = a[j]
    (ra4,) = kernel_rate(a, gl2, gu2, jac, None, inside, [4])
    own = u_ref.shape[-1]
    weighted = [ms_ref[m] for m in range(modes)]
    k = 0
    for field in (u0[4], mid[4], a[4], ra4):
        field = field[:, :own]
        for m in range(modes):
            part_ref[k : k + 1, :] = lane_fold(weighted[m] * field)
            k += 1
    ax41, pt41 = 0.5 * jac[0][4][1], 0.5 * jac[1][4][1]
    no_ghost = jnp.zeros((1, ms[0].shape[1]), ms[0].dtype)
    for n in range(modes):
        s = ms[n]
        north, south = pitch_neighbours(s, no_ghost, no_ghost)
        t = -(ax41 * (lane_roll(s, -1) - lane_roll(s, 1)) + pt41 * (north - south))
        t = t[:, :own]
        for m in range(modes):
            part_ref[k + m * modes + n : k + m * modes + n + 1, :] = lane_fold(weighted[m] * t)


def modal_steps(force_scale, tot_ref, other_ref, stiff_ref, disp_ref, vel_ref, modes):
    h = TIME_STEP
    t = [force_scale * (tot_ref[k] + other_ref[k]) for k in range(4 * modes + modes * modes)]
    force = [t[w * modes : (w + 1) * modes] for w in range(4)]
    couple = [t[4 * modes + m * modes : 4 * modes + (m + 1) * modes] for m in range(modes)]
    stiff = [stiff_ref[0, m] for m in range(modes)]
    disp0 = [disp_ref[0, m] for m in range(modes)]
    vel0 = [vel_ref[0, m] for m in range(modes)]

    def accel(f, q, v):
        return [f[m] - stiff[m] * q[m] - DAMPING * v[m] for m in range(modes)]

    def axpy(x, a, y):
        return [x[m] + a * y[m] for m in range(modes)]

    acc1 = accel(force[0], disp0, vel0)
    disp1m = axpy(disp0, h, vel0)
    vel1m = axpy(vel0, h, acc1)
    acc1m = accel(force[1], disp1m, vel1m)
    disp1 = [disp0[m] + 0.5 * h * (vel0[m] + vel1m[m]) for m in range(modes)]
    vel1 = [vel0[m] + 0.5 * h * (acc1[m] + acc1m[m]) for m in range(modes)]
    acc2 = accel(force[2], disp1, vel1)
    disp2m = axpy(disp1, h, vel1)
    vel2m = axpy(vel1, h, acc2)
    corr = 0.5 * h * h * COUPLING
    force2m = []
    for m in range(modes):
        coupled = couple[m][0] * acc1[0]
        for n in range(1, modes):
            coupled = coupled + couple[m][n] * acc1[n]
        force2m.append(force[2][m] + h * force[3][m] + h * corr * coupled)
    acc2m = accel(force2m, disp2m, vel2m)
    disp2 = [disp1[m] + 0.5 * h * (vel1[m] + vel2m[m]) for m in range(modes)]
    vel2 = [vel1[m] + 0.5 * h * (acc2[m] + acc2m[m]) for m in range(modes)]
    coef = [[corr * acc1[m] for m in range(modes)], vel1, vel2m]
    return coef, disp2, vel2


def step2_rate_kernel(peers, ax_ref, pt_ref, a_ref, ms_ref, glo_ref, gup_ref, packed_ref, ra_ref, halo_ref):
    unfold_halo(packed_ref, halo_ref)
    fields = a_ref.shape[0]
    modes = ms_ref.shape[0]
    pitch = ms_ref.shape[1]
    jac = read_jacobians(ax_ref, pt_ref, fields)
    _, ms, gl, gu = assemble(None, ms_ref, glo_ref, gup_ref, halo_ref, fields, modes, pitch)
    inside, _ = lane_masks(peers, ms[0].shape, ms_ref.shape[-1])
    every = list(range(fields))
    a = [a_ref[j] for j in every]
    ra = kernel_rate(a, gl[1], gu[1], jac, None, inside, every)
    for j in every:
        ra_ref[j] = ra[j]


def second_kernel(
    peers,
    force_scale,
    tot_ref,
    other_ref,
    stiff_ref,
    disp_ref,
    vel_ref,
    ax_ref,
    pt_ref,
    a_ref,
    ra_ref,
    ms_ref,
    glo_ref,
    gup_ref,
    packed_ref,
    out_ref,
    disp_out_ref,
    vel_out_ref,
    halo_ref,
):
    h = TIME_STEP
    unfold_halo(packed_ref, halo_ref)
    fields = a_ref.shape[0]
    modes = ms_ref.shape[0]
    pitch = ms_ref.shape[1]
    jac = read_jacobians(ax_ref, pt_ref, fields)
    coef, disp2, vel2 = modal_steps(force_scale, tot_ref, other_ref, stiff_ref, disp_ref, vel_ref, modes)
    for m in range(modes):
        disp_out_ref[0, m] = disp2[m]
        vel_out_ref[0, m] = vel2[m]
    _, ms, gl, gu = assemble(None, ms_ref, glo_ref, gup_ref, halo_ref, fields, modes, pitch)
    inside, _ = lane_masks(peers, ms[0].shape, ms_ref.shape[-1])

    def combine(weights):
        total = weights[0] * ms[0]
        for m in range(1, modes):
            total = total + weights[m] * ms[m]
        return total

    gl2, gu2 = gl[1], gu[1]
    every = list(range(fields))
    s1 = [a_ref[j] for j in every]
    correction = combine(coef[0])
    s1[1] = s1[1] + correction
    rows = correction.shape[0]
    row = lax.broadcasted_iota(jnp.int32, correction.shape, 0)
    east, west = lane_roll(correction, -1), lane_roll(correction, 1)
    north = jnp.where(row == rows - 1, 0.0, row_roll(correction, -1))
    south = jnp.where(row == 0, 0.0, row_roll(correction, 1))
    ga = 0.5 * (east - west)
    gp = 0.5 * (north - south)
    lap = east + west + north + south - 4.0 * correction
    ax, pt = jac
    push1 = COUPLING * combine(coef[1])
    k1 = []
    for i in every:
        r = -ax[i][1] * ga - pt[i][1] * gp
        if i == 1:
            r = r + DIFFUSION * lap + push1
        k1.append(ra_ref[i] + masked(r, inside))
    mid = [s1[j] + h * k1[j] for j in every]
    k2 = kernel_rate(mid, gl2, gu2, jac, COUPLING * combine(coef[2]), inside, every)
    width = out_ref.shape[-1]
    for j in every:
        s2 = s1[j] + 0.5 * h * (k1[j] + k2[j])
        out_ref[j] = s2[:, :width]


def vmem_spec():
    return pl.BlockSpec(memory_space=pltpu.VMEM)


def smem_spec():
    return pl.BlockSpec(memory_space=pltpu.SMEM)


def on_device(
    flow_field,
    lower_row_history,
    upper_row_history,
    lower_lag_slot,
    upper_lag_slot,
    axial_jacobian,
    pitch_jacobian,
    mode_shape,
    stiffness,
    displacement,
    velocity,
):
    h = TIME_STEP
    state0 = flow_field[0]
    fields, pitch_cells, axial_cells = state0.shape
    modes = mode_shape.shape[0]
    mesh_peers = lax.axis_size("mesh")
    me = lax.axis_index("mesh")
    force_scale = 1.0 / math.sqrt(pitch_cells * axial_cells * mesh_peers)
    passages = lax.axis_size("blk")
    position = lax.axis_index("blk")
    blade_stiffness = stiffness[0]
    disp0 = displacement[0]
    vel0 = velocity[0]

    row_shape = jax.ShapeDtypeStruct((STEP_COUNT,) + upper_row_history.shape[2:], state0.dtype)
    rows_up, rows_down = pl.pallas_call(
        functools.partial(pick_kernel, passages),
        out_shape=(row_shape, row_shape),
        in_specs=[smem_spec(), smem_spec(), vmem_spec(), vmem_spec()],
        out_specs=(vmem_spec(), vmem_spec()),
    )(
        lower_lag_slot,
        upper_lag_slot,
        jnp.transpose(upper_row_history[0], (1, 0, 2)),
        jnp.transpose(lower_row_history[0], (1, 0, 2)),
    )
    lower_ghosts = shifted(rows_up, "blk", 1)
    upper_ghosts = shifted(rows_down, "blk", -1)

    reach = 2 * STEP_COUNT
    own = [state0, mode_shape, lower_ghosts, upper_ghosts]
    shapes = [part.shape[:-1] + (reach,) for part in own]
    from_left = shifted(pack([part[..., -reach:] for part in own], reach).reshape(-1), "mesh", 1)
    from_right = shifted(pack([part[..., :reach] for part in own], reach).reshape(-1), "mesh", -1)
    from_left = from_left.reshape(reach, -1)
    from_right = from_right.reshape(reach, -1)
    from_left = jnp.where(me > 0, from_left, jnp.zeros_like(from_left))
    from_right = jnp.where(me < mesh_peers - 1, from_right, jnp.zeros_like(from_right))
    packed_rows = from_left.shape[1]
    padded_rows = -(-packed_rows // LANES) * LANES
    halo_tile = jnp.pad(
        jnp.concatenate([from_left, from_right], axis=0), [(0, 0), (0, padded_rows - packed_rows)]
    )
    columns = [pltpu.VMEM((padded_rows, LANES), state0.dtype)]
    lanes_wide = axial_cells + LANES
    ins = (state0, mode_shape, lower_ghosts, upper_ghosts, halo_tile)

    base1, part_lanes = pl.pallas_call(
        functools.partial(first_kernel, mesh_peers),
        out_shape=(
            jax.ShapeDtypeStruct((fields, pitch_cells, lanes_wide), state0.dtype),
            jax.ShapeDtypeStruct((4 * modes + modes * modes, LANES), state0.dtype),
        ),
        in_specs=[smem_spec()] * 3 + [vmem_spec()] * 5,
        out_specs=(vmem_spec(), vmem_spec()),
        scratch_shapes=columns,
    )(axial_jacobian, pitch_jacobian, velocity, *ins)

    totals, totals_other = mesh_sum_pair(jnp.sum(part_lanes, axis=1))

    rate_a = pl.pallas_call(
        functools.partial(step2_rate_kernel, mesh_peers),
        out_shape=jax.ShapeDtypeStruct(base1.shape, base1.dtype),
        in_specs=[smem_spec()] * 2 + [vmem_spec()] * 5,
        out_specs=vmem_spec(),
        scratch_shapes=columns,
    )(axial_jacobian, pitch_jacobian, base1, *ins[1:])

    small = jax.ShapeDtypeStruct(displacement.shape, displacement.dtype)
    state2, disp2, vel2 = pl.pallas_call(
        functools.partial(second_kernel, mesh_peers, force_scale),
        out_shape=(jax.ShapeDtypeStruct(state0.shape, state0.dtype), small, small),
        in_specs=[smem_spec()] * 7 + [vmem_spec()] * 6,
        out_specs=(vmem_spec(), smem_spec(), smem_spec()),
        scratch_shapes=columns,
    )(totals, totals_other, stiffness, displacement, velocity, axial_jacobian, pitch_jacobian, base1, rate_a, *ins[1:])
    return (state2[None], disp2, vel2)


def solution(mesh):
    return jax.shard_map(
        on_device,
        mesh=mesh,
        in_specs=(
            P("blk", None, None, "mesh"),
            P("blk", None, None, "mesh"),
            P("blk", None, None, "mesh"),
            P(),
            P(),
            P(),
            P(),
            P(None, None, "mesh"),
            P("blk", None),
            P("blk", None),
            P("blk", None),
        ),
        out_specs=(P("blk", None, None, "mesh"), P("blk", None), P("blk", None)),
        check_vma=False,
    )
```

```python
import functools
import math

import jax
import jax.numpy as jnp
from jax import lax
from jax.experimental import pallas as pl
from jax.experimental.pallas import tpu as pltpu
from jax.sharding import PartitionSpec as P

STEP_COUNT = 2


PRECISE = lax.Precision.HIGHEST
TIME_STEP = 0.4
DIFFUSION = 0.1
COUPLING = 0.3
DAMPING = 0.1


def shifted(value, axis, by):
    peers = lax.axis_size(axis)
    return lax.ppermute(value, axis, [(i, (i + by) % peers) for i in range(peers)])


def halo(value):
    peers = lax.axis_size("mesh")
    me = lax.axis_index("mesh")
    before = shifted(value[..., -1:], "mesh", 1)
    after = shifted(value[..., :1], "mesh", -1)
    before = jnp.where(me > 0, before, jnp.zeros_like(before))
    after = jnp.where(me < peers - 1, after, jnp.zeros_like(after))
    return before, after


def mesh_sum(value):
    peers = lax.axis_size("mesh")
    if peers & (peers - 1):
        return lax.psum(value, "mesh")
    step = 1
    while step < peers:
        value = value + lax.ppermute(value, "mesh", [(i, i ^ step) for i in range(peers)])
        step *= 2
    return value


def pick_rows(table, index, count):
    slots = table.shape[0]
    slot = jnp.arange(slots, dtype=jnp.int32).reshape((slots,) + (1,) * (table.ndim - 1))
    rows = []
    for s in range(count):
        hit = slot == (index + s) % slots
        rows.append(jnp.sum(jnp.where(hit, table, jnp.zeros_like(table)), axis=0))
    return jnp.stack(rows)


def pick_entry(values, index):
    hit = jnp.arange(values.shape[0], dtype=jnp.int32) == index
    return jnp.sum(jnp.where(hit, values, jnp.zeros_like(values)))


def axial_pad(value, before, after):
    return jnp.concatenate([before, value, after], axis=-1)


def pitch_pad(value, lower, upper):
    return jnp.concatenate([lower[:, None, :], value, upper[:, None, :]], axis=1)


def flow_rate(state, before, after, lower_ghost, upper_ghost, axial_jacobian, pitch_jacobian):
    padded_axial = axial_pad(state, before, after)
    padded_pitch = pitch_pad(state, lower_ghost, upper_ghost)
    grad_axial = 0.5 * (padded_axial[:, :, 2:] - padded_axial[:, :, :-2])
    grad_pitch = 0.5 * (padded_pitch[:, 2:, :] - padded_pitch[:, :-2, :])
    laplacian = (
        padded_axial[:, :, 2:]
        + padded_axial[:, :, :-2]
        + padded_pitch[:, 2:, :]
        + padded_pitch[:, :-2, :]
        - 4.0 * state
    )
    flux = jnp.einsum("ij,jpx->ipx", axial_jacobian, grad_axial, precision=PRECISE)
    flux = flux + jnp.einsum("ij,jpx->ipx", pitch_jacobian, grad_pitch, precision=PRECISE)
    return DIFFUSION * laplacian - flux


def single_field_grads(field, before, after):
    padded_axial = jnp.concatenate([before, field, after], axis=-1)
    zero_row = jnp.zeros_like(field[..., :1, :])
    padded_pitch = jnp.concatenate([zero_row, field, zero_row], axis=-2)
    grad_axial = 0.5 * (padded_axial[..., 2:] - padded_axial[..., :-2])
    grad_pitch = 0.5 * (padded_pitch[..., 2:, :] - padded_pitch[..., :-2, :])
    laplacian = (
        padded_axial[..., 2:]
        + padded_axial[..., :-2]
        + padded_pitch[..., 2:, :]
        + padded_pitch[..., :-2, :]
        - 4.0 * field
    )
    return grad_axial, grad_pitch, laplacian


def modal_field(weights, mode_shape):
    return jnp.einsum("m,mpx->px", weights, mode_shape, precision=PRECISE)


def projection(mode_shape, field):
    return jnp.einsum("mpx,px->m", mode_shape, field, precision=PRECISE)


def add_field_one(rate, extra):
    return rate.at[1].add(extra)


def rate_field4(state, lower_ghost, upper_ghost, axial_jacobian, pitch_jacobian):
    zero_col = jnp.zeros_like(state[..., :1])
    padded_axial = jnp.concatenate([zero_col, state, zero_col], axis=-1)
    padded_pitch = pitch_pad(state, lower_ghost, upper_ghost)
    grad_axial = 0.5 * (padded_axial[:, :, 2:] - padded_axial[:, :, :-2])
    grad_pitch = 0.5 * (padded_pitch[:, 2:, :] - padded_pitch[:, :-2, :])
    laplacian = (
        padded_axial[4, :, 2:]
        + padded_axial[4, :, :-2]
        + padded_pitch[4, 2:, :]
        + padded_pitch[4, :-2, :]
        - 4.0 * state[4]
    )
    flux = jnp.einsum("j,jpx->px", axial_jacobian[4], grad_axial, precision=PRECISE)
    flux = flux + jnp.einsum("j,jpx->px", pitch_jacobian[4], grad_pitch, precision=PRECISE)
    return DIFFUSION * laplacian - flux


def pack(parts, width):
    flat = [jnp.moveaxis(part, -1, 0).reshape(width, -1) for part in parts]
    return jnp.concatenate(flat, axis=1)


def unpack(buffer, shapes):
    out, offset = [], 0
    for shape in shapes:
        count = math.prod(shape[:-1])
        out.append(buffer[offset : offset + count].reshape(shape))
        offset += count
    return out


LANES = 128


def lane_roll(x, shift):
    return pltpu.roll(x, shift % x.shape[-1], x.ndim - 1)


def row_roll(x, shift):
    return pltpu.roll(x, shift % x.shape[0], 0)


def pitch_neighbours(s, lower, upper):
    rows = s.shape[0]
    tile = 8
    edge = lax.broadcasted_iota(jnp.int32, (tile,) + s.shape[1:], 0)
    north = row_roll(s, -1)
    south = row_roll(s, 1)
    north = jnp.concatenate(
        [north[: rows - tile], jnp.where(edge == tile - 1, upper, north[rows - tile :])], axis=0
    )
    south = jnp.concatenate([jnp.where(edge == 0, lower, south[:tile]), south[tile:]], axis=0)
    return north, south


def masked(r, inside):
    cut = r.shape[-1] - LANES
    return jnp.concatenate([r[:, :cut], r[:, cut:] * inside[:, cut:]], axis=1)


def kernel_rate(state, lower, upper, jac, push, inside, fields_out):
    ax, pt = jac
    diffs_a, diffs_p, laps = [], [], []
    for j, s in enumerate(state):
        east = lane_roll(s, -1)
        west = lane_roll(s, 1)
        north, south = pitch_neighbours(s, lower[j], upper[j])
        diffs_a.append(east - west)
        diffs_p.append(north - south)
        laps.append((east + west) + (north + south) - 4.0 * s)
    out = []
    for i in fields_out:
        r = DIFFUSION * laps[i]
        for j in range(len(state)):
            r = r - (0.5 * ax[i][j]) * diffs_a[j] - (0.5 * pt[i][j]) * diffs_p[j]
        if i == 1 and push is not None:
            r = r + push
        out.append(masked(r, inside))
    return out


def read_jacobians(ax_ref, pt_ref, fields):
    ax = [[ax_ref[i, j] for j in range(fields)] for i in range(fields)]
    pt = [[pt_ref[i, j] for j in range(fields)] for i in range(fields)]
    return ax, pt


def lane_fold(x):
    x = jnp.sum(x, axis=0, keepdims=True)
    total = x[:, :LANES]
    for t in range(1, x.shape[1] // LANES):
        total = total + x[:, t * LANES : (t + 1) * LANES]
    return total


def pick_kernel(peers, lower_slot_ref, upper_slot_ref, upper_hist_ref, lower_hist_ref, up_ref, down_ref):
    fields, slots = upper_hist_ref.shape[0], upper_hist_ref.shape[1]
    position = lax.axis_index("blk")
    slot_next = lower_slot_ref[(position + 1) % peers]
    slot_prev = upper_slot_ref[(position + peers - 1) % peers]
    for s in range(up_ref.shape[0]):
        up_at = (slot_next + s) % slots
        down_at = (slot_prev + s) % slots
        for f in range(fields):
            up_ref[s, f : f + 1, :] = upper_hist_ref[f, pl.ds(up_at, 1), :]
            down_ref[s, f : f + 1, :] = lower_hist_ref[f, pl.ds(down_at, 1), :]


def widened(own, tile):
    return jnp.concatenate([own, lane_roll(tile, -2 * STEP_COUNT)], axis=-1)


def unfold_halo(halo_ref, columns_ref):
    block = halo_ref[...]
    spare = jnp.zeros((LANES - block.shape[0], block.shape[1]), block.dtype)
    columns_ref[...] = jnp.concatenate([block, spare], axis=0).T


def lane_masks(peers, shape, own_width):
    reach = 2 * STEP_COUNT
    me = lax.axis_index("mesh")
    lane = lax.broadcasted_iota(jnp.int32, shape, len(shape) - 1)
    width = shape[-1]
    right_ok = (lane >= own_width) & (lane < own_width + reach) & (me < peers - 1)
    left_ok = (lane >= width - reach) & (me > 0)
    owned = lane < own_width
    inside = owned | right_ok | left_ok
    return inside.astype(jnp.float32), owned.astype(jnp.float32)


def assemble(u_ref, ms_ref, glo_ref, gup_ref, halo_ref, fields, modes, pitch):
    u = []
    for j in range(fields if u_ref is not None else 0):
        rows = slice(j * pitch, (j + 1) * pitch)
        u.append(widened(u_ref[j], halo_ref[rows, :]))
    ms = []
    for m in range(modes if ms_ref is not None else 0):
        rows = slice((fields + m) * pitch, (fields + m + 1) * pitch)
        ms.append(widened(ms_ref[m], halo_ref[rows, :]))
    base = (fields + modes) * pitch
    steps = glo_ref.shape[0]
    ghosts = []
    for side, ref in enumerate((glo_ref, gup_ref)):
        per_step = []
        for s in range(steps):
            start = base + (side * steps + s) * fields
            rows = slice(start, start + fields)
            block = widened(ref[s], halo_ref[rows, :])
            per_step.append([block[j : j + 1, :] for j in range(fields)])
        ghosts.append(per_step)
    return u, ms, ghosts[0], ghosts[1]


def first_kernel(peers, ax_ref, pt_ref, vel_ref, u_ref, ms_ref, glo_ref, gup_ref, packed_ref, a_ref, part_ref, halo_ref):
    h = TIME_STEP
    unfold_halo(packed_ref, halo_ref)
    fields = u_ref.shape[0]
    modes = ms_ref.shape[0]
    pitch = u_ref.shape[1]
    jac = read_jacobians(ax_ref, pt_ref, fields)
    vel = [vel_ref[0, m] for m in range(modes)]
    u0, ms, gl, gu = assemble(u_ref, ms_ref, glo_ref, gup_ref, halo_ref, fields, modes, pitch)
    inside, _ = lane_masks(peers, u0[0].shape, u_ref.shape[-1])
    push = vel[0] * ms[0]
    for m in range(1, modes):
        push = push + vel[m] * ms[m]
    push = COUPLING * push
    gl1, gu1, gl2, gu2 = gl[0], gu[0], gl[1], gu[1]
    every = list(range(fields))
    k1 = kernel_rate(u0, gl1, gu1, jac, push, inside, every)
    mid = [u0[j] + h * k1[j] for j in every]
    k2 = kernel_rate(mid, gl1, gu1, jac, push, inside, every)
    a = [u0[j] + 0.5 * h * (k1[j] + k2[j]) for j in every]
    for j in every:
        a_ref[j] = a[j]
    (ra4,) = kernel_rate(a, gl2, gu2, jac, None, inside, [4])
    own = u_ref.shape[-1]
    weighted = [ms_ref[m] for m in range(modes)]
    k = 0
    for field in (u0[4], mid[4], a[4], ra4):
        field = field[:, :own]
        for m in range(modes):
            part_ref[k : k + 1, :] = lane_fold(weighted[m] * field)
            k += 1
    ax41, pt41 = 0.5 * jac[0][4][1], 0.5 * jac[1][4][1]
    no_ghost = jnp.zeros((1, ms[0].shape[1]), ms[0].dtype)
    for n in range(modes):
        s = ms[n]
        north, south = pitch_neighbours(s, no_ghost, no_ghost)
        t = -(ax41 * (lane_roll(s, -1) - lane_roll(s, 1)) + pt41 * (north - south))
        t = t[:, :own]
        for m in range(modes):
            part_ref[k + m * modes + n : k + m * modes + n + 1, :] = lane_fold(weighted[m] * t)


def modal_steps(force_scale, tot_ref, stiff_ref, disp_ref, vel_ref, modes):
    h = TIME_STEP
    t = [force_scale * tot_ref[k] for k in range(4 * modes + modes * modes)]
    force = [t[w * modes : (w + 1) * modes] for w in range(4)]
    couple = [t[4 * modes + m * modes : 4 * modes + (m + 1) * modes] for m in range(modes)]
    stiff = [stiff_ref[0, m] for m in range(modes)]
    disp0 = [disp_ref[0, m] for m in range(modes)]
    vel0 = [vel_ref[0, m] for m in range(modes)]

    def accel(f, q, v):
        return [f[m] - stiff[m] * q[m] - DAMPING * v[m] for m in range(modes)]

    def axpy(x, a, y):
        return [x[m] + a * y[m] for m in range(modes)]

    acc1 = accel(force[0], disp0, vel0)
    disp1m = axpy(disp0, h, vel0)
    vel1m = axpy(vel0, h, acc1)
    acc1m = accel(force[1], disp1m, vel1m)
    disp1 = [disp0[m] + 0.5 * h * (vel0[m] + vel1m[m]) for m in range(modes)]
    vel1 = [vel0[m] + 0.5 * h * (acc1[m] + acc1m[m]) for m in range(modes)]
    acc2 = accel(force[2], disp1, vel1)
    disp2m = axpy(disp1, h, vel1)
    vel2m = axpy(vel1, h, acc2)
    corr = 0.5 * h * h * COUPLING
    force2m = []
    for m in range(modes):
        coupled = couple[m][0] * acc1[0]
        for n in range(1, modes):
            coupled = coupled + couple[m][n] * acc1[n]
        force2m.append(force[2][m] + h * force[3][m] + h * corr * coupled)
    acc2m = accel(force2m, disp2m, vel2m)
    disp2 = [disp1[m] + 0.5 * h * (vel1[m] + vel2m[m]) for m in range(modes)]
    vel2 = [vel1[m] + 0.5 * h * (acc2[m] + acc2m[m]) for m in range(modes)]
    coef = [[corr * acc1[m] for m in range(modes)], vel1, vel2m]
    return coef, disp2, vel2


def step2_rate_kernel(peers, modes, ax_ref, pt_ref, a_ref, glo_ref, gup_ref, packed_ref, ra_ref, halo_ref):
    unfold_halo(packed_ref, halo_ref)
    fields = a_ref.shape[0]
    pitch = a_ref.shape[1]
    jac = read_jacobians(ax_ref, pt_ref, fields)
    _, _, gl, gu = assemble(None, None, glo_ref, gup_ref, halo_ref, fields, modes, pitch)
    inside, _ = lane_masks(peers, a_ref.shape[1:], a_ref.shape[-1] - LANES)
    every = list(range(fields))
    a = [a_ref[j] for j in every]
    ra = kernel_rate(a, gl[1], gu[1], jac, None, inside, every)
    for j in every:
        ra_ref[j] = ra[j]


def second_kernel(
    peers,
    force_scale,
    tot_ref,
    stiff_ref,
    disp_ref,
    vel_ref,
    ax_ref,
    pt_ref,
    a_ref,
    ra_ref,
    ms_ref,
    glo_ref,
    gup_ref,
    packed_ref,
    out_ref,
    disp_out_ref,
    vel_out_ref,
    halo_ref,
):
    h = TIME_STEP
    unfold_halo(packed_ref, halo_ref)
    fields = a_ref.shape[0]
    modes = ms_ref.shape[0]
    pitch = ms_ref.shape[1]
    jac = read_jacobians(ax_ref, pt_ref, fields)
    coef, disp2, vel2 = modal_steps(force_scale, tot_ref, stiff_ref, disp_ref, vel_ref, modes)
    for m in range(modes):
        disp_out_ref[0, m] = disp2[m]
        vel_out_ref[0, m] = vel2[m]
    _, ms, gl, gu = assemble(None, ms_ref, glo_ref, gup_ref, halo_ref, fields, modes, pitch)
    inside, _ = lane_masks(peers, ms[0].shape, ms_ref.shape[-1])

    def combine(weights):
        total = weights[0] * ms[0]
        for m in range(1, modes):
            total = total + weights[m] * ms[m]
        return total

    gl2, gu2 = gl[1], gu[1]
    every = list(range(fields))
    s1 = [a_ref[j] for j in every]
    correction = combine(coef[0])
    s1[1] = s1[1] + correction
    rows = correction.shape[0]
    row = lax.broadcasted_iota(jnp.int32, correction.shape, 0)
    east, west = lane_roll(correction, -1), lane_roll(correction, 1)
    north = jnp.where(row == rows - 1, 0.0, row_roll(correction, -1))
    south = jnp.where(row == 0, 0.0, row_roll(correction, 1))
    ga = 0.5 * (east - west)
    gp = 0.5 * (north - south)
    lap = east + west + north + south - 4.0 * correction
    ax, pt = jac
    push1 = COUPLING * combine(coef[1])
    k1 = []
    for i in every:
        r = -ax[i][1] * ga - pt[i][1] * gp
        if i == 1:
            r = r + DIFFUSION * lap + push1
        k1.append(ra_ref[i] + masked(r, inside))
    mid = [s1[j] + h * k1[j] for j in every]
    k2 = kernel_rate(mid, gl2, gu2, jac, COUPLING * combine(coef[2]), inside, every)
    width = out_ref.shape[-1]
    for j in every:
        s2 = s1[j] + 0.5 * h * (k1[j] + k2[j])
        out_ref[j] = s2[:, :width]


def vmem_spec():
    return pl.BlockSpec(memory_space=pltpu.VMEM)


def smem_spec():
    return pl.BlockSpec(memory_space=pltpu.SMEM)


def on_device(
    flow_field,
    lower_row_history,
    upper_row_history,
    lower_lag_slot,
    upper_lag_slot,
    axial_jacobian,
    pitch_jacobian,
    mode_shape,
    stiffness,
    displacement,
    velocity,
):
    h = TIME_STEP
    state0 = flow_field[0]
    fields, pitch_cells, axial_cells = state0.shape
    modes = mode_shape.shape[0]
    mesh_peers = lax.axis_size("mesh")
    me = lax.axis_index("mesh")
    force_scale = 1.0 / math.sqrt(pitch_cells * axial_cells * mesh_peers)
    passages = lax.axis_size("blk")
    position = lax.axis_index("blk")
    blade_stiffness = stiffness[0]
    disp0 = displacement[0]
    vel0 = velocity[0]

    row_shape = jax.ShapeDtypeStruct((STEP_COUNT,) + upper_row_history.shape[2:], state0.dtype)
    rows_up, rows_down = pl.pallas_call(
        functools.partial(pick_kernel, passages),
        out_shape=(row_shape, row_shape),
        in_specs=[smem_spec(), smem_spec(), vmem_spec(), vmem_spec()],
        out_specs=(vmem_spec(), vmem_spec()),
    )(
        lower_lag_slot,
        upper_lag_slot,
        jnp.transpose(upper_row_history[0], (1, 0, 2)),
        jnp.transpose(lower_row_history[0], (1, 0, 2)),
    )
    lower_ghosts = shifted(rows_up, "blk", 1)
    upper_ghosts = shifted(rows_down, "blk", -1)

    reach = 2 * STEP_COUNT
    own = [state0, mode_shape, lower_ghosts, upper_ghosts]
    shapes = [part.shape[:-1] + (reach,) for part in own]
    from_left = shifted(pack([part[..., -reach:] for part in own], reach).reshape(-1), "mesh", 1)
    from_right = shifted(pack([part[..., :reach] for part in own], reach).reshape(-1), "mesh", -1)
    from_left = from_left.reshape(reach, -1)
    from_right = from_right.reshape(reach, -1)
    from_left = jnp.where(me > 0, from_left, jnp.zeros_like(from_left))
    from_right = jnp.where(me < mesh_peers - 1, from_right, jnp.zeros_like(from_right))
    packed_rows = from_left.shape[1]
    padded_rows = -(-packed_rows // LANES) * LANES
    halo_tile = jnp.pad(
        jnp.concatenate([from_left, from_right], axis=0), [(0, 0), (0, padded_rows - packed_rows)]
    )
    columns = [pltpu.VMEM((padded_rows, LANES), state0.dtype)]
    lanes_wide = axial_cells + LANES
    ins = (state0, mode_shape, lower_ghosts, upper_ghosts, halo_tile)

    base1, part_lanes = pl.pallas_call(
        functools.partial(first_kernel, mesh_peers),
        out_shape=(
            jax.ShapeDtypeStruct((fields, pitch_cells, lanes_wide), state0.dtype),
            jax.ShapeDtypeStruct((4 * modes + modes * modes, LANES), state0.dtype),
        ),
        in_specs=[smem_spec()] * 3 + [vmem_spec()] * 5,
        out_specs=(vmem_spec(), vmem_spec()),
        scratch_shapes=columns,
    )(axial_jacobian, pitch_jacobian, velocity, *ins)

    totals = mesh_sum(jnp.sum(part_lanes, axis=1))

    rate_a = pl.pallas_call(
        functools.partial(step2_rate_kernel, mesh_peers, modes),
        out_shape=jax.ShapeDtypeStruct(base1.shape, base1.dtype),
        in_specs=[smem_spec()] * 2 + [vmem_spec()] * 4,
        out_specs=vmem_spec(),
        scratch_shapes=columns,
    )(axial_jacobian, pitch_jacobian, base1, *ins[2:])

    small = jax.ShapeDtypeStruct(displacement.shape, displacement.dtype)
    state2, disp2, vel2 = pl.pallas_call(
        functools.partial(second_kernel, mesh_peers, force_scale),
        out_shape=(jax.ShapeDtypeStruct(state0.shape, state0.dtype), small, small),
        in_specs=[smem_spec()] * 6 + [vmem_spec()] * 6,
        out_specs=(vmem_spec(), smem_spec(), smem_spec()),
        scratch_shapes=columns,
    )(totals, stiffness, displacement, velocity, axial_jacobian, pitch_jacobian, base1, rate_a, *ins[1:])
    return (state2[None], disp2, vel2)


def solution(mesh):
    return jax.shard_map(
        on_device,
        mesh=mesh,
        in_specs=(
            P("blk", None, None, "mesh"),
            P("blk", None, None, "mesh"),
            P("blk", None, None, "mesh"),
            P(),
            P(),
            P(),
            P(),
            P(None, None, "mesh"),
            P("blk", None),
            P("blk", None),
            P("blk", None),
        ),
        out_specs=(P("blk", None, None, "mesh"), P("blk", None), P("blk", None)),
        check_vma=False,
    )
```

```python
import functools
import math

import jax
import jax.numpy as jnp
from jax import lax
from jax.experimental import pallas as pl
from jax.experimental.pallas import tpu as pltpu
from jax.sharding import PartitionSpec as P

STEP_COUNT = 2


PRECISE = lax.Precision.HIGHEST
TIME_STEP = 0.4
DIFFUSION = 0.1
COUPLING = 0.3
DAMPING = 0.1


def shifted(value, axis, by):
    peers = lax.axis_size(axis)
    return lax.ppermute(value, axis, [(i, (i + by) % peers) for i in range(peers)])


def halo(value):
    peers = lax.axis_size("mesh")
    me = lax.axis_index("mesh")
    before = shifted(value[..., -1:], "mesh", 1)
    after = shifted(value[..., :1], "mesh", -1)
    before = jnp.where(me > 0, before, jnp.zeros_like(before))
    after = jnp.where(me < peers - 1, after, jnp.zeros_like(after))
    return before, after


def mesh_sum_pair(value):
    peers = lax.axis_size("mesh")
    if peers & (peers - 1) or peers < 2:
        return lax.psum(value, "mesh"), jnp.zeros_like(value)
    step = 1
    while 2 * step < peers:
        value = value + lax.ppermute(value, "mesh", [(i, i ^ step) for i in range(peers)])
        step *= 2
    return value, lax.ppermute(value, "mesh", [(i, i ^ step) for i in range(peers)])


def mesh_sum(value):
    peers = lax.axis_size("mesh")
    if peers & (peers - 1):
        return lax.psum(value, "mesh")
    step = 1
    while step < peers:
        value = value + lax.ppermute(value, "mesh", [(i, i ^ step) for i in range(peers)])
        step *= 2
    return value


def pick_rows(table, index, count):
    slots = table.shape[0]
    slot = jnp.arange(slots, dtype=jnp.int32).reshape((slots,) + (1,) * (table.ndim - 1))
    rows = []
    for s in range(count):
        hit = slot == (index + s) % slots
        rows.append(jnp.sum(jnp.where(hit, table, jnp.zeros_like(table)), axis=0))
    return jnp.stack(rows)


def pick_entry(values, index):
    hit = jnp.arange(values.shape[0], dtype=jnp.int32) == index
    return jnp.sum(jnp.where(hit, values, jnp.zeros_like(values)))


def axial_pad(value, before, after):
    return jnp.concatenate([before, value, after], axis=-1)


def pitch_pad(value, lower, upper):
    return jnp.concatenate([lower[:, None, :], value, upper[:, None, :]], axis=1)


def flow_rate(state, before, after, lower_ghost, upper_ghost, axial_jacobian, pitch_jacobian):
    padded_axial = axial_pad(state, before, after)
    padded_pitch = pitch_pad(state, lower_ghost, upper_ghost)
    grad_axial = 0.5 * (padded_axial[:, :, 2:] - padded_axial[:, :, :-2])
    grad_pitch = 0.5 * (padded_pitch[:, 2:, :] - padded_pitch[:, :-2, :])
    laplacian = (
        padded_axial[:, :, 2:]
        + padded_axial[:, :, :-2]
        + padded_pitch[:, 2:, :]
        + padded_pitch[:, :-2, :]
        - 4.0 * state
    )
    flux = jnp.einsum("ij,jpx->ipx", axial_jacobian, grad_axial, precision=PRECISE)
    flux = flux + jnp.einsum("ij,jpx->ipx", pitch_jacobian, grad_pitch, precision=PRECISE)
    return DIFFUSION * laplacian - flux


def single_field_grads(field, before, after):
    padded_axial = jnp.concatenate([before, field, after], axis=-1)
    zero_row = jnp.zeros_like(field[..., :1, :])
    padded_pitch = jnp.concatenate([zero_row, field, zero_row], axis=-2)
    grad_axial = 0.5 * (padded_axial[..., 2:] - padded_axial[..., :-2])
    grad_pitch = 0.5 * (padded_pitch[..., 2:, :] - padded_pitch[..., :-2, :])
    laplacian = (
        padded_axial[..., 2:]
        + padded_axial[..., :-2]
        + padded_pitch[..., 2:, :]
        + padded_pitch[..., :-2, :]
        - 4.0 * field
    )
    return grad_axial, grad_pitch, laplacian


def modal_field(weights, mode_shape):
    return jnp.einsum("m,mpx->px", weights, mode_shape, precision=PRECISE)


def projection(mode_shape, field):
    return jnp.einsum("mpx,px->m", mode_shape, field, precision=PRECISE)


def add_field_one(rate, extra):
    return rate.at[1].add(extra)


def rate_field4(state, lower_ghost, upper_ghost, axial_jacobian, pitch_jacobian):
    zero_col = jnp.zeros_like(state[..., :1])
    padded_axial = jnp.concatenate([zero_col, state, zero_col], axis=-1)
    padded_pitch = pitch_pad(state, lower_ghost, upper_ghost)
    grad_axial = 0.5 * (padded_axial[:, :, 2:] - padded_axial[:, :, :-2])
    grad_pitch = 0.5 * (padded_pitch[:, 2:, :] - padded_pitch[:, :-2, :])
    laplacian = (
        padded_axial[4, :, 2:]
        + padded_axial[4, :, :-2]
        + padded_pitch[4, 2:, :]
        + padded_pitch[4, :-2, :]
        - 4.0 * state[4]
    )
    flux = jnp.einsum("j,jpx->px", axial_jacobian[4], grad_axial, precision=PRECISE)
    flux = flux + jnp.einsum("j,jpx->px", pitch_jacobian[4], grad_pitch, precision=PRECISE)
    return DIFFUSION * laplacian - flux


def pack(parts, width):
    flat = [jnp.moveaxis(part, -1, 0).reshape(width, -1) for part in parts]
    return jnp.concatenate(flat, axis=1)


def unpack(buffer, shapes):
    out, offset = [], 0
    for shape in shapes:
        count = math.prod(shape[:-1])
        out.append(buffer[offset : offset + count].reshape(shape))
        offset += count
    return out


LANES = 128


def lane_roll(x, shift):
    return pltpu.roll(x, shift % x.shape[-1], x.ndim - 1)


def row_roll(x, shift):
    return pltpu.roll(x, shift % x.shape[0], 0)


def pitch_neighbours(s, lower, upper):
    rows = s.shape[0]
    tile = 8
    edge = lax.broadcasted_iota(jnp.int32, (tile,) + s.shape[1:], 0)
    north = row_roll(s, -1)
    south = row_roll(s, 1)
    north = jnp.concatenate(
        [north[: rows - tile], jnp.where(edge == tile - 1, upper, north[rows - tile :])], axis=0
    )
    south = jnp.concatenate([jnp.where(edge == 0, lower, south[:tile]), south[tile:]], axis=0)
    return north, south


def masked(r, inside):
    cut = r.shape[-1] - LANES
    return jnp.concatenate([r[:, :cut], r[:, cut:] * inside[:, cut:]], axis=1)


def kernel_rate(state, lower, upper, jac, push, inside, fields_out):
    ax, pt = jac
    diffs_a, diffs_p, laps = [], [], []
    for j, s in enumerate(state):
        east = lane_roll(s, -1)
        west = lane_roll(s, 1)
        north, south = pitch_neighbours(s, lower[j], upper[j])
        diffs_a.append(east - west)
        diffs_p.append(north - south)
        laps.append((east + west) + (north + south) - 4.0 * s)
    out = []
    for i in fields_out:
        r = DIFFUSION * laps[i]
        for j in range(len(state)):
            r = r - (0.5 * ax[i][j]) * diffs_a[j] - (0.5 * pt[i][j]) * diffs_p[j]
        if i == 1 and push is not None:
            r = r + push
        out.append(masked(r, inside))
    return out


def read_jacobians(ax_ref, pt_ref, fields):
    ax = [[ax_ref[i, j] for j in range(fields)] for i in range(fields)]
    pt = [[pt_ref[i, j] for j in range(fields)] for i in range(fields)]
    return ax, pt


def lane_fold(x):
    x = jnp.sum(x, axis=0, keepdims=True)
    total = x[:, :LANES]
    for t in range(1, x.shape[1] // LANES):
        total = total + x[:, t * LANES : (t + 1) * LANES]
    return total


def pick_kernel(peers, lower_slot_ref, upper_slot_ref, upper_hist_ref, lower_hist_ref, up_ref, down_ref):
    fields, slots = upper_hist_ref.shape[0], upper_hist_ref.shape[1]
    position = lax.axis_index("blk")
    slot_next = lower_slot_ref[(position + 1) % peers]
    slot_prev = upper_slot_ref[(position + peers - 1) % peers]
    for s in range(up_ref.shape[0]):
        up_at = (slot_next + s) % slots
        down_at = (slot_prev + s) % slots
        for f in range(fields):
            up_ref[s, f : f + 1, :] = upper_hist_ref[f, pl.ds(up_at, 1), :]
            down_ref[s, f : f + 1, :] = lower_hist_ref[f, pl.ds(down_at, 1), :]


def widened(own, tile):
    return jnp.concatenate([own, lane_roll(tile, -2 * STEP_COUNT)], axis=-1)


def unfold_halo(halo_ref, columns_ref):
    block = halo_ref[...]
    spare = jnp.zeros((LANES - block.shape[0], block.shape[1]), block.dtype)
    columns_ref[...] = jnp.concatenate([block, spare], axis=0).T


def lane_masks(peers, shape, own_width):
    reach = 2 * STEP_COUNT
    me = lax.axis_index("mesh")
    lane = lax.broadcasted_iota(jnp.int32, shape, len(shape) - 1)
    width = shape[-1]
    right_ok = (lane >= own_width) & (lane < own_width + reach) & (me < peers - 1)
    left_ok = (lane >= width - reach) & (me > 0)
    owned = lane < own_width
    inside = owned | right_ok | left_ok
    return inside.astype(jnp.float32), owned.astype(jnp.float32)


def assemble(u_ref, ms_ref, glo_ref, gup_ref, halo_ref, fields, modes, pitch):
    u = []
    for j in range(fields if u_ref is not None else 0):
        rows = slice(j * pitch, (j + 1) * pitch)
        u.append(widened(u_ref[j], halo_ref[rows, :]))
    ms = []
    for m in range(modes if ms_ref is not None else 0):
        rows = slice((fields + m) * pitch, (fields + m + 1) * pitch)
        ms.append(widened(ms_ref[m], halo_ref[rows, :]))
    base = (fields + modes) * pitch
    steps = glo_ref.shape[0]
    ghosts = []
    for side, ref in enumerate((glo_ref, gup_ref)):
        per_step = []
        for s in range(steps):
            start = base + (side * steps + s) * fields
            rows = slice(start, start + fields)
            block = widened(ref[s], halo_ref[rows, :])
            per_step.append([block[j : j + 1, :] for j in range(fields)])
        ghosts.append(per_step)
    return u, ms, ghosts[0], ghosts[1]


def first_kernel(peers, ax_ref, pt_ref, vel_ref, u_ref, ms_ref, glo_ref, gup_ref, packed_ref, a_ref, part_ref, halo_ref):
    h = TIME_STEP
    unfold_halo(packed_ref, halo_ref)
    fields = u_ref.shape[0]
    modes = ms_ref.shape[0]
    pitch = u_ref.shape[1]
    jac = read_jacobians(ax_ref, pt_ref, fields)
    vel = [vel_ref[0, m] for m in range(modes)]
    u0, ms, gl, gu = assemble(u_ref, ms_ref, glo_ref, gup_ref, halo_ref, fields, modes, pitch)
    inside, _ = lane_masks(peers, u0[0].shape, u_ref.shape[-1])
    push = vel[0] * ms[0]
    for m in range(1, modes):
        push = push + vel[m] * ms[m]
    push = COUPLING * push
    gl1, gu1, gl2, gu2 = gl[0], gu[0], gl[1], gu[1]
    every = list(range(fields))
    k1 = kernel_rate(u0, gl1, gu1, jac, push, inside, every)
    mid = [u0[j] + h * k1[j] for j in every]
    k2 = kernel_rate(mid, gl1, gu1, jac, push, inside, every)
    a = [u0[j] + 0.5 * h * (k1[j] + k2[j]) for j in every]
    for j in every:
        a_ref[j] = a[j]
    (ra4,) = kernel_rate(a, gl2, gu2, jac, None, inside, [4])
    own = u_ref.shape[-1]
    weighted = [ms_ref[m] for m in range(modes)]
    k = 0
    for field in (u0[4], mid[4], a[4], ra4):
        field = field[:, :own]
        for m in range(modes):
            part_ref[k : k + 1, :] = lane_fold(weighted[m] * field)
            k += 1
    ax41, pt41 = 0.5 * jac[0][4][1], 0.5 * jac[1][4][1]
    no_ghost = jnp.zeros((1, ms[0].shape[1]), ms[0].dtype)
    for n in range(modes):
        s = ms[n]
        north, south = pitch_neighbours(s, no_ghost, no_ghost)
        t = -(ax41 * (lane_roll(s, -1) - lane_roll(s, 1)) + pt41 * (north - south))
        t = t[:, :own]
        for m in range(modes):
            part_ref[k + m * modes + n : k + m * modes + n + 1, :] = lane_fold(weighted[m] * t)


def modal_steps(force_scale, sums, stiff_ref, disp_ref, vel_ref, modes):
    h = TIME_STEP
    t = [force_scale * value for value in sums]
    force = [t[w * modes : (w + 1) * modes] for w in range(4)]
    couple = [t[4 * modes + m * modes : 4 * modes + (m + 1) * modes] for m in range(modes)]
    stiff = [stiff_ref[0, m] for m in range(modes)]
    disp0 = [disp_ref[0, m] for m in range(modes)]
    vel0 = [vel_ref[0, m] for m in range(modes)]

    def accel(f, q, v):
        return [f[m] - stiff[m] * q[m] - DAMPING * v[m] for m in range(modes)]

    def axpy(x, a, y):
        return [x[m] + a * y[m] for m in range(modes)]

    acc1 = accel(force[0], disp0, vel0)
    disp1m = axpy(disp0, h, vel0)
    vel1m = axpy(vel0, h, acc1)
    acc1m = accel(force[1], disp1m, vel1m)
    disp1 = [disp0[m] + 0.5 * h * (vel0[m] + vel1m[m]) for m in range(modes)]
    vel1 = [vel0[m] + 0.5 * h * (acc1[m] + acc1m[m]) for m in range(modes)]
    acc2 = accel(force[2], disp1, vel1)
    disp2m = axpy(disp1, h, vel1)
    vel2m = axpy(vel1, h, acc2)
    corr = 0.5 * h * h * COUPLING
    force2m = []
    for m in range(modes):
        coupled = couple[m][0] * acc1[0]
        for n in range(1, modes):
            coupled = coupled + couple[m][n] * acc1[n]
        force2m.append(force[2][m] + h * force[3][m] + h * corr * coupled)
    acc2m = accel(force2m, disp2m, vel2m)
    disp2 = [disp1[m] + 0.5 * h * (vel1[m] + vel2m[m]) for m in range(modes)]
    vel2 = [vel1[m] + 0.5 * h * (acc2[m] + acc2m[m]) for m in range(modes)]
    coef = [[corr * acc1[m] for m in range(modes)], vel1, vel2m]
    return coef, disp2, vel2


def step2_rate_kernel(peers, modes, ax_ref, pt_ref, a_ref, glo_ref, gup_ref, packed_ref, ra_ref, halo_ref):
    unfold_halo(packed_ref, halo_ref)
    fields = a_ref.shape[0]
    pitch = a_ref.shape[1]
    jac = read_jacobians(ax_ref, pt_ref, fields)
    _, _, gl, gu = assemble(None, None, glo_ref, gup_ref, halo_ref, fields, modes, pitch)
    inside, _ = lane_masks(peers, a_ref.shape[1:], a_ref.shape[-1] - LANES)
    every = list(range(fields))
    a = [a_ref[j] for j in every]
    ra = kernel_rate(a, gl[1], gu[1], jac, None, inside, every)
    for j in every:
        ra_ref[j] = ra[j]


def second_kernel(
    peers,
    force_scale,
    stiff_ref,
    disp_ref,
    vel_ref,
    ax_ref,
    pt_ref,
    tot_ref,
    other_ref,
    a_ref,
    ra_ref,
    ms_ref,
    glo_ref,
    gup_ref,
    packed_ref,
    out_ref,
    disp_out_ref,
    vel_out_ref,
    halo_ref,
):
    h = TIME_STEP
    unfold_halo(packed_ref, halo_ref)
    fields = a_ref.shape[0]
    modes = ms_ref.shape[0]
    pitch = ms_ref.shape[1]
    jac = read_jacobians(ax_ref, pt_ref, fields)
    coef, disp2, vel2 = modal_steps(
        force_scale,
        [jnp.sum(tot_ref[k : k + 1, :] + other_ref[k : k + 1, :]) for k in range(tot_ref.shape[0])],
        stiff_ref,
        disp_ref,
        vel_ref,
        modes,
    )
    for m in range(modes):
        disp_out_ref[0, m] = disp2[m]
        vel_out_ref[0, m] = vel2[m]
    _, ms, gl, gu = assemble(None, ms_ref, glo_ref, gup_ref, halo_ref, fields, modes, pitch)
    inside, _ = lane_masks(peers, ms[0].shape, ms_ref.shape[-1])

    def combine(weights):
        total = weights[0] * ms[0]
        for m in range(1, modes):
            total = total + weights[m] * ms[m]
        return total

    gl2, gu2 = gl[1], gu[1]
    every = list(range(fields))
    s1 = [a_ref[j] for j in every]
    correction = combine(coef[0])
    s1[1] = s1[1] + correction
    rows = correction.shape[0]
    row = lax.broadcasted_iota(jnp.int32, correction.shape, 0)
    east, west = lane_roll(correction, -1), lane_roll(correction, 1)
    north = jnp.where(row == rows - 1, 0.0, row_roll(correction, -1))
    south = jnp.where(row == 0, 0.0, row_roll(correction, 1))
    ga = 0.5 * (east - west)
    gp = 0.5 * (north - south)
    lap = east + west + north + south - 4.0 * correction
    ax, pt = jac
    push1 = COUPLING * combine(coef[1])
    k1 = []
    for i in every:
        r = -ax[i][1] * ga - pt[i][1] * gp
        if i == 1:
            r = r + DIFFUSION * lap + push1
        k1.append(ra_ref[i] + masked(r, inside))
    mid = [s1[j] + h * k1[j] for j in every]
    k2 = kernel_rate(mid, gl2, gu2, jac, COUPLING * combine(coef[2]), inside, every)
    width = out_ref.shape[-1]
    for j in every:
        s2 = s1[j] + 0.5 * h * (k1[j] + k2[j])
        out_ref[j] = s2[:, :width]


def vmem_spec():
    return pl.BlockSpec(memory_space=pltpu.VMEM)


def smem_spec():
    return pl.BlockSpec(memory_space=pltpu.SMEM)


def on_device(
    flow_field,
    lower_row_history,
    upper_row_history,
    lower_lag_slot,
    upper_lag_slot,
    axial_jacobian,
    pitch_jacobian,
    mode_shape,
    stiffness,
    displacement,
    velocity,
):
    h = TIME_STEP
    state0 = flow_field[0]
    fields, pitch_cells, axial_cells = state0.shape
    modes = mode_shape.shape[0]
    mesh_peers = lax.axis_size("mesh")
    me = lax.axis_index("mesh")
    force_scale = 1.0 / math.sqrt(pitch_cells * axial_cells * mesh_peers)
    passages = lax.axis_size("blk")
    position = lax.axis_index("blk")
    blade_stiffness = stiffness[0]
    disp0 = displacement[0]
    vel0 = velocity[0]

    row_shape = jax.ShapeDtypeStruct((STEP_COUNT,) + upper_row_history.shape[2:], state0.dtype)
    rows_up, rows_down = pl.pallas_call(
        functools.partial(pick_kernel, passages),
        out_shape=(row_shape, row_shape),
        in_specs=[smem_spec(), smem_spec(), vmem_spec(), vmem_spec()],
        out_specs=(vmem_spec(), vmem_spec()),
    )(
        lower_lag_slot,
        upper_lag_slot,
        jnp.transpose(upper_row_history[0], (1, 0, 2)),
        jnp.transpose(lower_row_history[0], (1, 0, 2)),
    )
    lower_ghosts = shifted(rows_up, "blk", 1)
    upper_ghosts = shifted(rows_down, "blk", -1)

    reach = 2 * STEP_COUNT
    own = [state0, mode_shape, lower_ghosts, upper_ghosts]
    shapes = [part.shape[:-1] + (reach,) for part in own]
    from_left = shifted(pack([part[..., -reach:] for part in own], reach).reshape(-1), "mesh", 1)
    from_right = shifted(pack([part[..., :reach] for part in own], reach).reshape(-1), "mesh", -1)
    from_left = from_left.reshape(reach, -1)
    from_right = from_right.reshape(reach, -1)
    from_left = jnp.where(me > 0, from_left, jnp.zeros_like(from_left))
    from_right = jnp.where(me < mesh_peers - 1, from_right, jnp.zeros_like(from_right))
    packed_rows = from_left.shape[1]
    padded_rows = -(-packed_rows // LANES) * LANES
    halo_tile = jnp.pad(
        jnp.concatenate([from_left, from_right], axis=0), [(0, 0), (0, padded_rows - packed_rows)]
    )
    columns = [pltpu.VMEM((padded_rows, LANES), state0.dtype)]
    lanes_wide = axial_cells + LANES
    ins = (state0, mode_shape, lower_ghosts, upper_ghosts, halo_tile)

    base1, part_lanes = pl.pallas_call(
        functools.partial(first_kernel, mesh_peers),
        out_shape=(
            jax.ShapeDtypeStruct((fields, pitch_cells, lanes_wide), state0.dtype),
            jax.ShapeDtypeStruct((4 * modes + modes * modes, LANES), state0.dtype),
        ),
        in_specs=[smem_spec()] * 3 + [vmem_spec()] * 5,
        out_specs=(vmem_spec(), vmem_spec()),
        scratch_shapes=columns,
    )(axial_jacobian, pitch_jacobian, velocity, *ins)

    totals, totals_other = mesh_sum_pair(part_lanes)

    rate_a = pl.pallas_call(
        functools.partial(step2_rate_kernel, mesh_peers, modes),
        out_shape=jax.ShapeDtypeStruct(base1.shape, base1.dtype),
        in_specs=[smem_spec()] * 2 + [vmem_spec()] * 4,
        out_specs=vmem_spec(),
        scratch_shapes=columns,
    )(axial_jacobian, pitch_jacobian, base1, *ins[2:])

    small = jax.ShapeDtypeStruct(displacement.shape, displacement.dtype)
    state2, disp2, vel2 = pl.pallas_call(
        functools.partial(second_kernel, mesh_peers, force_scale),
        out_shape=(jax.ShapeDtypeStruct(state0.shape, state0.dtype), small, small),
        in_specs=[smem_spec()] * 5 + [vmem_spec()] * 8,
        out_specs=(vmem_spec(), smem_spec(), smem_spec()),
        scratch_shapes=columns,
    )(
        stiffness,
        displacement,
        velocity,
        axial_jacobian,
        pitch_jacobian,
        totals,
        totals_other,
        base1,
        rate_a,
        *ins[1:],
    )
    return (state2[None], disp2, vel2)


def solution(mesh):
    return jax.shard_map(
        on_device,
        mesh=mesh,
        in_specs=(
            P("blk", None, None, "mesh"),
            P("blk", None, None, "mesh"),
            P("blk", None, None, "mesh"),
            P(),
            P(),
            P(),
            P(),
            P(None, None, "mesh"),
            P("blk", None),
            P("blk", None),
            P("blk", None),
        ),
        out_specs=(P("blk", None, None, "mesh"), P("blk", None), P("blk", None)),
        check_vma=False,
    )
```
